32 devices in a mesh: req: 16 (over z, x, core), kv: 2 (over y).
Axes of the slice: x: 2, y: 2, z: 4, core: 2. Of those that a mesh axis runs over, the one named last changes fastest.
Arguments:
- hidden: bfloat16 [32, 256, 1024], P('req', 'kv'), may hold values from -6 to 6
- queries: bfloat16 [32, 256, 1024], P('req', 'kv'), may hold values from -24 to 24
- span_kv: bfloat16 [32, 256, 8, 128], P('req', 'kv'), may hold values from -48 to 48
- cache: bfloat16 [32, 2048, 8, 128], P('req', 'kv'), may hold values from -48 to 48
- req_order: int32 [32], replicated, may hold values from 0 to 31, each once
- cached_len: int32 [32], replicated, may hold values from 8 to 2048, as said below
- out_weight: bfloat16 [1024, 1024], replicated, may hold values from -0.1875 to 0.1875
- norm_gain: float32 [1024], replicated, may hold values from 0.1 to 1.9
- expert_ids: int32 [8192, 8], P(('req', 'kv')), may hold values from 0 to 15, all different within a row; in each aligned block of 256 rows (0 to 255, 256 to 511, ...) at most 256 rows name the same one
- expert_weights: float32 [8192, 8], P(('req', 'kv')), may hold values from 0.05 to 0.5
- w_experts: bfloat16 [16, 3, 1024, 512], P('req', None, None, 'kv'), may hold values from -0.25 to 0.25
- block_map: int32 [32, 128], P('req'), may hold values from 0 to 4095, as said below
Outputs:
- layer_out: bfloat16 [32, 256, 1024], P('req', 'kv')
- decode_pool: bfloat16 [4096, 8, 16, 128], P('req', 'kv')
The draws below stay inside these ranges and needn't reach their ends.
Inputs may be any that keep to these rules, and one draw needn't show every extreme that they name: `cached_len`: some request fills its cache. `block_map`: a permutation of the 4096 pool pages; pool page s belongs to req index s // 256; the pages that one kv index holds of the slots of one req index (positions of its cache share) go to every req index equally often. `expert_ids`: in the rows of one device no expert is named more than 256 times.
All inputs are finite; a program needn't handle non-finite values.
Results may differ from the reference program's by a relative error of at most 0.023.
Values may be sent and summed in bfloat16 or wider, within the bound.
No kernel may reach another device: no remote copies, remote signals or barrier semaphores. Data moves between devices by JAX's collectives and lax.ppermute only.
A program may use at most 128 MiB of HBM per device.

```python
import math
import jax
import jax.numpy as jnp
import numpy as np
from jax import lax

D = 1024
HEADS = 16
KV_HEADS = 8
HEAD_DIM = 64
FF = 512
TOPK = 8
REQ_DEV = 2
SPAN = 256
CACHE_DEV = 1024
BLOCK = 16
EXPERTS = 16
REQS = 32
SPAN_DEV = 128
MAXLEN = 2048
ROWS_DEV = 256
TOKENS = 8192
CAP = 256
BLOCKS_REQ = 128
SLOTS = 4096
N_REQ = 16
N_KV = 2


def split_parts(key, full_shape, value_scale):
    head_dim = full_shape[-1] // 2
    half_shape = tuple(full_shape[:-1]) + (head_dim,)
    key_first, key_second = jax.random.split(key)
    key_part = jnp.clip(jax.random.normal(key_first, half_shape, jnp.float32), -6.0, 6.0)
    value_part = jnp.clip(jax.random.normal(key_second, half_shape, jnp.float32), -6.0, 6.0) * value_scale
    return (key_part, value_part)


def draw_cache(key, part):
    key_part, value_part = split_parts(jax.random.fold_in(key, 11), (REQS, MAXLEN, KV_HEADS, 2 * HEAD_DIM), 8.0)
    return jnp.concatenate([key_part, value_part], axis=-1).astype(jnp.bfloat16)


def draw_span_kv(key, part):
    key_part, value_part = split_parts(jax.random.fold_in(key, 13), (REQS, SPAN, KV_HEADS, 2 * HEAD_DIM), 8.0)
    return jnp.concatenate([key_part, value_part], axis=-1).astype(jnp.bfloat16)


def draw_queries(key, part):
    per_group = HEADS // KV_HEADS
    full_shape = (REQS, SPAN, KV_HEADS, per_group, HEAD_DIM)
    entries = jnp.clip(jax.random.normal(jax.random.fold_in(key, 15), full_shape, jnp.float32), -6.0, 6.0)
    return entries.reshape(REQS, SPAN, HEADS * HEAD_DIM).astype(jnp.bfloat16)


def draw_cached_len(key, part):
    lengths = jax.random.randint(jax.random.fold_in(key, 17), (REQS,), 8, MAXLEN + 1)
    longest = jax.random.randint(jax.random.fold_in(key, 19), (), 0, REQS)
    return jnp.where(jnp.arange(REQS) == longest, MAXLEN, lengths).astype(jnp.int32)


def draw_block_map(key, part):
    req_count = REQS // REQ_DEV
    kv_count = MAXLEN // CACHE_DEV
    page_count = CACHE_DEV // BLOCK
    per_source = REQ_DEV * page_count
    sources = req_count * kv_count
    repeats = per_source // req_count
    slots_dev = REQ_DEV * (MAXLEN // BLOCK)
    base_owner = jnp.tile(jnp.arange(req_count, dtype=jnp.int32), repeats)
    owner_key = jax.random.fold_in(key, 23)
    shuffle_key = jax.random.fold_in(key, 29)

    def owners_of(source_index):
        return jax.random.permutation(jax.random.fold_in(owner_key, source_index), base_owner)
    owners = jax.vmap(owners_of)(jnp.arange(sources, dtype=jnp.int32))
    arrangement = jnp.argsort(owners, axis=1, stable=True)
    sorted_rank = jnp.broadcast_to(jnp.arange(per_source, dtype=jnp.int32) % repeats, (sources, per_source))
    slot_rank = jnp.zeros((sources, per_source), jnp.int32).at[jnp.arange(sources)[:, None], arrangement].set(sorted_rank)
    incoming = jnp.arange(sources, dtype=jnp.int32)[:, None] * repeats + slot_rank

    def shuffle_of(owner_index):
        return jax.random.permutation(jax.random.fold_in(shuffle_key, owner_index), slots_dev).astype(jnp.int32)
    shuffles = jax.vmap(shuffle_of)(jnp.arange(req_count, dtype=jnp.int32))
    local_slot = shuffles[owners, incoming]
    pool_slot = owners * slots_dev + local_slot
    return pool_slot.reshape(req_count, kv_count, REQ_DEV, page_count).transpose(0, 2, 1, 3).reshape(REQS, MAXLEN // BLOCK).astype(jnp.int32)


def levels(own_key, extent, pieces, smallest, largest):
    factor_of, own = 1.0, jax.random.fold_in(own_key, 6)
    for axis_at, shards_of in pieces:
        heights = jnp.exp(jax.random.uniform(jax.random.fold_in(own, axis_at), (shards_of,), jnp.float32, smallest / len(pieces), largest / len(pieces)))
        factor_of = factor_of * jnp.repeat(heights, extent[axis_at] // shards_of).reshape([-1 if axis == axis_at else 1 for axis in range(len(extent))])
    return factor_of


def routed_block(own_key, own, number, rows, number_of, top, reach, slope):
    sequence = jax.random.permutation(own_key, number_of)
    heavy_load, ordinary = shares(number_of, rows * top, reach, slope, True), shares(number_of, rows * top, reach, slope, False)
    places = jnp.arange(number_of)

    def named(sizes, rotation):
        used = int((sizes > 0).sum())
        fixed = max(1, used // 4)
        passed = fixed + (places - fixed + rotation * (used - fixed)) % max(1, number_of - fixed)
        return jnp.zeros((number_of,), jnp.int32).at[sequence[jnp.where(places < fixed, places, passed)]].set(jnp.asarray(sizes, jnp.int32))

    sizes = jnp.where(number % 4 == 0, named(heavy_load, number // 4), named(ordinary, number - number // 4 - 1))
    mixed = jax.random.permutation(jax.random.fold_in(own, 3), number_of)
    source_of, sink = mixed[0:number_of // 2 * 2:2], mixed[1:number_of // 2 * 2:2]
    margin = jnp.minimum(sizes[source_of] - 1, reach - sizes[sink]) // 2
    margin = jnp.where((source_of == sequence[0]) | (sink == sequence[0]) | (sizes[sink] == 0), 0, jnp.maximum(margin, 0))
    passed = jax.random.randint(jax.random.fold_in(own, 4), (number_of // 2,), 0, 1 << 20) % (margin + 1)
    sizes = sizes.at[source_of].add(-passed).at[sink].add(passed)
    items = jnp.searchsorted(jnp.cumsum(sizes), jnp.arange(rows * top), side="right").astype(jnp.int32)
    listing = items.reshape(top, rows).T
    listing = listing[jax.random.permutation(jax.random.fold_in(own, 1), rows)]
    rotation = jax.random.randint(jax.random.fold_in(own, 2), (rows, 1), 0, top)
    return jnp.take_along_axis(listing, (jnp.arange(top)[None, :] + rotation) % top, axis=1)


def shares(amount, total, reach, lean, full):
    loads = [(1 << 20) // math.isqrt(standing ** lean) + 1 for standing in range(1, amount + 1)]
    largest = reach if full else min(reach, max(-(-total // amount), total * loads[0] // sum(loads)))
    least = 1 if total - largest >= amount - 1 else 0
    given, surplus = [largest] + [least] * (amount - 1), total - largest - least * (amount - 1)
    while surplus > 0:
        candidates = [i for i in range(1, amount) if given[i] < largest] or [i for i in range(1, amount) if given[i] < reach]
        mass, budget = sum([loads[i] for i in candidates]), surplus
        for i in candidates:
            more = min(reach - given[i], max(1, budget * loads[i] // mass), surplus)
            given[i] = given[i] + more
            surplus = surplus - more
    return np.array(given)


def scatter_about(rng, extent, width, limit, pieces=(), kind=jnp.bfloat16):
    values = width * jax.random.normal(rng, extent, jnp.float32)
    if pieces:
        values = values * levels(rng, extent, pieces, -0.22, 0.18)
    return jnp.clip(values, -limit, limit).astype(kind)


def setup_inputs(seed: int = 0) -> dict:
    key_of = jax.random.split(jax.random.key(seed), 13)
    hidden = scatter_about(key_of[0], (REQS, SPAN, D), 1.0, 6.0, ((0, 16), (1, 2)))
    queries = draw_queries(jax.random.fold_in(key_of[12], 71), 0)
    span_kv = draw_span_kv(jax.random.fold_in(key_of[12], 71), 0)
    cache = draw_cache(jax.random.fold_in(key_of[12], 71), 0)
    req_order = jax.random.permutation(key_of[4], REQS).astype(jnp.int32)
    cached_len = draw_cached_len(jax.random.fold_in(key_of[12], 71), 0)
    out_weight = scatter_about(key_of[6], (HEADS * HEAD_DIM, D), (HEADS * HEAD_DIM) ** -0.5, 0.1875)
    norm_gain = jnp.clip(1.0 + 0.18 * jax.random.normal(key_of[7], (D,), jnp.float32), 0.1, 1.9)
    expert_ids_keys = jax.random.split(jax.random.fold_in(key_of[8], 1), TOKENS // ROWS_DEV)
    expert_ids_turns = jax.random.permutation(jax.random.fold_in(key_of[8], 3), TOKENS // ROWS_DEV)
    expert_ids = jax.vmap(lambda own, number: routed_block(jax.random.fold_in(key_of[8], 2), own, number, ROWS_DEV, EXPERTS, TOPK, CAP, 1))(expert_ids_keys, expert_ids_turns).reshape((TOKENS, TOPK))
    expert_weights = jnp.clip(jnp.exp(math.log(0.5) - 2.3025851 * jax.random.uniform(key_of[9], (TOKENS, TOPK), jnp.float32) ** levels(key_of[9], (TOKENS, TOPK), ((0, 32),), -0.2, 0.2)), 0.05, 0.5)
    w_experts = scatter_about(key_of[10], (EXPERTS, 3, D, FF), FF ** -0.5, 0.25, ((0, 16), (3, 2)))
    block_map = draw_block_map(jax.random.fold_in(key_of[12], 71), 0)
    return {"hidden": hidden, "queries": queries, "span_kv": span_kv, "cache": cache, "req_order": req_order, "cached_len": cached_len, "out_weight": out_weight, "norm_gain": norm_gain, "expert_ids": expert_ids, "expert_weights": expert_weights, "w_experts": w_experts, "block_map": block_map}


def attend_request(operands):
    query_rows, cache_rows, span_rows, length = operands
    per_group = HEADS // KV_HEADS
    query_split = query_rows.reshape(SPAN, KV_HEADS, per_group, HEAD_DIM).astype(jnp.float32)
    key_rows = jnp.concatenate([cache_rows[..., :HEAD_DIM], span_rows[..., :HEAD_DIM]], axis=0).astype(jnp.float32)
    value_rows = jnp.concatenate([cache_rows[..., HEAD_DIM:], span_rows[..., HEAD_DIM:]], axis=0).astype(jnp.float32)
    scores = jnp.einsum('igsd,pgd->gsip', query_split, key_rows) * (1.0 / math.sqrt(HEAD_DIM))
    position = jnp.arange(MAXLEN + SPAN)[None, :]
    query_pos = jnp.arange(SPAN)[:, None]
    allowed = jnp.where(position < MAXLEN, position < length, position - MAXLEN <= query_pos)
    masked = jnp.where(allowed, scores, -1e+30)
    row_max = lax.optimization_barrier(jnp.max(masked, axis=-1, keepdims=True))
    probability = jnp.where(allowed, jnp.exp(masked - row_max), 0.0)
    prob_sum = lax.optimization_barrier(jnp.sum(probability, axis=-1))
    rounded = lax.optimization_barrier(probability.astype(jnp.bfloat16)).astype(jnp.float32)
    weighted = jnp.einsum('gsip,pgd->igsd', rounded, value_rows)
    result = weighted / jnp.transpose(prob_sum, (2, 0, 1))[..., None]
    return result.reshape(SPAN, HEADS * HEAD_DIM).astype(jnp.bfloat16)

def to_device_major(array):
    return array.reshape(N_REQ, REQ_DEV, N_KV, SPAN_DEV, -1).transpose(0, 2, 1, 3, 4).reshape(TOKENS, -1)

def reference(hidden, queries, span_kv, cache, req_order, cached_len, out_weight, norm_gain, expert_ids, expert_weights, w_experts, block_map):
    lengths = cached_len[req_order]
    attn = lax.map(attend_request, (queries, cache, span_kv, lengths))
    residual = hidden.astype(jnp.float32) + jnp.dot(attn.reshape(TOKENS, HEADS * HEAD_DIM), out_weight, preferred_element_type=jnp.float32).reshape(REQS, SPAN, D)
    inverse_rms = lax.rsqrt(lax.optimization_barrier(jnp.mean(residual * residual, axis=-1, keepdims=True)) + 1e-05)
    normed = (residual * inverse_rms * norm_gain).astype(jnp.bfloat16)
    normed_rows = to_device_major(normed)
    residual_rows = to_device_major(residual)
    chosen = expert_ids.reshape(-1)
    assignments = chosen.shape[0]
    arrangement = jnp.argsort(chosen, stable=True).astype(jnp.int32)
    counts = lax.optimization_barrier(jnp.sum((chosen[:, None] == jnp.arange(EXPERTS, dtype=jnp.int32)[None, :]).astype(jnp.int32), axis=0))
    starts = (jnp.cumsum(counts) - counts).astype(jnp.int32)
    seg_rows = 512
    gathered = normed_rows[arrangement // TOPK]
    padded = jnp.concatenate([gathered, jnp.zeros((seg_rows, D), jnp.bfloat16)], axis=0)
    initial = jnp.zeros((assignments + seg_rows, D), jnp.bfloat16)

    def expert_step(expert_index, outputs):
        weights_here = lax.dynamic_index_in_dim(w_experts, expert_index, 0, keepdims=False)
        start = starts[expert_index]
        count = counts[expert_index]

        def segment_step(step_index, inner_out):
            offset = (start + step_index * seg_rows).astype(jnp.int32)
            rows_in = lax.dynamic_slice_in_dim(padded, offset, seg_rows, 0)
            gate_act = jnp.dot(rows_in, weights_here[0], preferred_element_type=jnp.float32)
            up_act = jnp.dot(rows_in, weights_here[1], preferred_element_type=jnp.float32)
            activated = (jax.nn.silu(gate_act) * up_act).astype(jnp.bfloat16)
            produced = jnp.dot(activated, weights_here[2].T, preferred_element_type=jnp.float32).astype(jnp.bfloat16)
            previous = lax.dynamic_slice_in_dim(inner_out, offset, seg_rows, 0)
            keep_rows = jnp.arange(seg_rows) + step_index * seg_rows < count
            merged = jnp.where(keep_rows[:, None], produced, previous)
            return lax.dynamic_update_slice_in_dim(inner_out, merged, offset, 0)
        steps_needed = ((count + seg_rows - 1) // seg_rows).astype(jnp.int32)
        return lax.fori_loop(jnp.int32(0), steps_needed, segment_step, outputs)
    produced_all = lax.fori_loop(jnp.int32(0), jnp.int32(EXPERTS), expert_step, initial)
    unsorted = jnp.zeros((assignments, D), jnp.bfloat16).at[arrangement].set(produced_all[:assignments])
    expert_sum = lax.optimization_barrier(jnp.sum(expert_weights[..., None] * unsorted.reshape(TOKENS, TOPK, D).astype(jnp.float32), axis=1))
    combined = (residual_rows + expert_sum).astype(jnp.bfloat16)
    layer_out = combined.reshape(N_REQ, N_KV, REQ_DEV, SPAN_DEV, D).transpose(0, 2, 1, 3, 4).reshape(REQS, SPAN, D)
    visible = jnp.arange(MAXLEN)[None, :] < lengths[:, None]
    visible_cache = jnp.where(visible[:, :, None, None], cache, jnp.zeros((), jnp.bfloat16))
    page_rows = visible_cache.reshape(REQS, BLOCKS_REQ, BLOCK, KV_HEADS, 2 * HEAD_DIM).transpose(0, 1, 3, 2, 4).reshape(SLOTS, KV_HEADS, BLOCK, 2 * HEAD_DIM)
    decode_pool = jnp.zeros_like(page_rows).at[block_map.reshape(-1)].set(page_rows)
    return (layer_out, decode_pool)
```

```python
import functools
import math

import jax
import jax.numpy as jnp
from jax import lax
from jax.experimental import pallas as pl
from jax.experimental.pallas import tpu as pltpu
from jax.sharding import PartitionSpec as P

BLOCK = 16


def lookup_lengths(req_order, cached_len, count):
    start = lax.axis_index("req") * count
    mine = lax.dynamic_slice_in_dim(req_order, start, count)
    match = mine[:, None] == jnp.arange(cached_len.shape[0], dtype=jnp.int32)[None, :]
    return jnp.sum(jnp.where(match, cached_len[None, :], 0), axis=1)


def attend_kernel(len_ref, q_ref, c_ref, s_ref, o_ref, *, tk, head_dim):
    b = pl.program_id(0)
    length = len_ref[b]
    span = q_ref.shape[1]
    lanes = q_ref.shape[2]
    per_group = lanes // head_dim
    scale = 1.0 / math.sqrt(head_dim)
    lane = lax.broadcasted_iota(jnp.int32, (span, lanes), 1)
    q_all = q_ref[0].astype(jnp.float32)
    nblk = (length + tk - 1) // tk
    row = lax.broadcasted_iota(jnp.int32, (span, span), 0)
    col = lax.broadcasted_iota(jnp.int32, (span, span), 1)
    causal = col <= row
    span_keys = s_ref[0]
    dims = (((1,), (1,)), ((), ()))
    outs = []
    for j in range(per_group):
        shifted = q_all if j == 0 else pltpu.roll(q_all, lanes - j * head_dim, 1)
        qj = jnp.where(lane < head_dim, shifted, 0.0).astype(jnp.bfloat16)

        def block_scores(kb):
            start = pl.multiple_of(kb * tk, tk)
            keys = c_ref[0, pl.ds(start, tk), :]
            s = lax.dot_general(qj, keys, dims, preferred_element_type=jnp.float32) * scale
            pos = start + lax.broadcasted_iota(jnp.int32, (span, tk), 1)
            return keys, pos < length, s

        def max_body(kb, m):
            _, ok, s = block_scores(kb)
            return jnp.maximum(m, jnp.max(jnp.where(ok, s, -1e30), axis=1, keepdims=True))

        s_span = lax.dot_general(qj, span_keys, dims, preferred_element_type=jnp.float32) * scale
        m0 = jnp.max(jnp.where(causal, s_span, -1e30), axis=1, keepdims=True)
        m = lax.fori_loop(0, nblk, max_body, m0)

        def sum_body(kb, carry):
            l, acc = carry
            keys, ok, s = block_scores(kb)
            p = jnp.where(ok, jnp.exp(s - m), 0.0)
            l = l + jnp.sum(p, axis=1, keepdims=True)
            acc = acc + jnp.dot(p.astype(jnp.bfloat16), keys, preferred_element_type=jnp.float32)
            return l, acc

        p_span = jnp.where(causal, jnp.exp(s_span - m), 0.0)
        l0 = jnp.sum(p_span, axis=1, keepdims=True)
        acc0 = jnp.dot(p_span.astype(jnp.bfloat16), span_keys, preferred_element_type=jnp.float32)
        l, acc = lax.fori_loop(0, nblk, sum_body, (l0, acc0))
        res = acc / l
        shift = (j * head_dim - head_dim) % lanes
        outs.append(res if shift == 0 else pltpu.roll(res, shift, 1))
    out = outs[0]
    for j in range(1, per_group):
        out = jnp.where(lane >= j * head_dim, outs[j], out)
    o_ref[0] = out.astype(o_ref.dtype)


def attend(query_heads, cache_heads, span_heads, lengths):
    local_reqs, span, groups, lanes = query_heads.shape
    cached = cache_heads.shape[1]
    head_dim = cache_heads.shape[-1] // 2
    tk = 256 if cached % 256 == 0 else cached
    q2 = query_heads.reshape(local_reqs, span, groups * lanes)
    c2 = cache_heads.reshape(local_reqs, cached, groups * lanes)
    s2 = span_heads.reshape(local_reqs, span, groups * lanes)
    flops = 2 * local_reqs * groups * (lanes // head_dim) * span * (cached + span) * lanes * 3
    out = pl.pallas_call(
        functools.partial(attend_kernel, tk=tk, head_dim=head_dim),
        out_shape=jax.ShapeDtypeStruct(q2.shape, jnp.bfloat16),
        grid_spec=pltpu.PrefetchScalarGridSpec(
            num_scalar_prefetch=1,
            grid=(local_reqs, groups),
            in_specs=[
                pl.BlockSpec((1, span, lanes), lambda b, g, n: (b, 0, g)),
                pl.BlockSpec((1, cached, lanes), lambda b, g, n: (b, 0, g)),
                pl.BlockSpec((1, span, lanes), lambda b, g, n: (b, 0, g)),
            ],
            out_specs=pl.BlockSpec((1, span, lanes), lambda b, g, n: (b, 0, g)),
        ),
        cost_estimate=pl.CostEstimate(
            flops=flops,
            transcendentals=local_reqs * groups * 2 * span * (cached + span),
            bytes_accessed=2 * (2 * q2.size + c2.size + s2.size),
        ),
    )(lengths.astype(jnp.int32), q2, c2, s2)
    return out.reshape(local_reqs, span, groups, lanes)


def place_pages(page_rows, slot_numbers, slots_dev):
    owner_index = slot_numbers // slots_dev
    arrangement = jnp.argsort(owner_index, stable=True)
    return (page_rows[arrangement], (slot_numbers % slots_dev)[arrangement])


def body(
    hidden,
    queries,
    span_kv,
    cache,
    req_order,
    cached_len,
    out_weight,
    norm_gain,
    expert_ids,
    expert_weights,
    w_experts,
    block_map,
):
    local_reqs, local_tokens, width_model = hidden.shape
    row_count = local_reqs * local_tokens
    req_count = lax.axis_size("req")
    kv_count = lax.axis_size("kv")
    kv_heads = span_kv.shape[2]
    head_pair = span_kv.shape[3]
    group_width = queries.shape[2] // kv_heads
    group_count = kv_heads // kv_count
    slots_dev = local_reqs * block_map.shape[1]
    lengths = lookup_lengths(req_order, cached_len, local_reqs)
    queries_grouped = queries.reshape(local_reqs, local_tokens, kv_heads, group_width)
    cache_heads, span_heads, query_heads = (
        lax.all_to_all(cache, "kv", split_axis=2, concat_axis=1, tiled=True),
        lax.all_to_all(span_kv, "kv", split_axis=2, concat_axis=1, tiled=True),
        lax.all_to_all(queries_grouped, "kv", split_axis=2, concat_axis=1, tiled=True),
    )
    attn_heads = attend(query_heads, cache_heads, span_heads, lengths)
    attn = lax.all_to_all(attn_heads, "kv", split_axis=1, concat_axis=2, tiled=True).reshape(
        row_count, kv_heads * group_width
    )
    page_total = block_map.shape[1]
    visible = jnp.arange(cache_heads.shape[1])[None, :] < lengths[:, None]
    visible_cache = jnp.where(visible[:, :, None, None], cache_heads, jnp.zeros((), jnp.bfloat16))
    page_rows = (
        visible_cache.reshape(local_reqs, page_total, BLOCK, group_count, head_pair)
        .transpose(0, 1, 3, 2, 4)
        .reshape(local_reqs * page_total, group_count, BLOCK, head_pair)
    )
    sorted_pages, local_slot = place_pages(page_rows, block_map.reshape(-1), slots_dev)
    per_owner = sorted_pages.shape[0] // req_count
    outgoing = sorted_pages.reshape(req_count, per_owner, group_count, BLOCK, head_pair)
    arrived, where_to = (
        lax.all_to_all(outgoing, "req", split_axis=0, concat_axis=0, tiled=True),
        lax.all_to_all(
            local_slot.reshape(req_count, per_owner), "req", split_axis=0, concat_axis=0, tiled=True
        ),
    )
    placement = (
        where_to.reshape(1, -1) == jnp.arange(slots_dev, dtype=jnp.int32)[:, None]
    ).astype(jnp.bfloat16)
    decode_pool = jnp.dot(
        placement,
        arrived.reshape(slots_dev, group_count * BLOCK * head_pair),
        preferred_element_type=jnp.float32,
    ).astype(jnp.bfloat16).reshape(slots_dev, group_count, BLOCK, head_pair)
    residual = hidden.reshape(row_count, width_model).astype(jnp.float32) + jnp.dot(
        attn, out_weight, preferred_element_type=jnp.float32
    )
    inverse_rms = lax.rsqrt(jnp.mean(residual * residual, axis=-1, keepdims=True) + 1e-05)
    normed = (residual * inverse_rms * norm_gain).astype(jnp.bfloat16)
    top_count = expert_ids.shape[1]
    exp_dev = w_experts.shape[0]
    experts = exp_dev * req_count
    capacity = min(row_count, 2 * row_count * top_count // experts)
    match = expert_ids[:, :, None] == jnp.arange(experts, dtype=jnp.int32)[None, None, :]
    picks = jnp.sum(match.astype(jnp.int32), axis=1)
    pick_weight = jnp.sum(jnp.where(match, expert_weights[:, :, None], 0.0), axis=1)
    rank = jnp.cumsum(picks, axis=0) - 1
    slot_of = jnp.where(picks > 0, rank, -1).T
    selector = slot_of[:, None, :] == jnp.arange(capacity, dtype=jnp.int32)[None, :, None]
    buffer = jnp.einsum(
        "ect,td->ecd", selector.astype(jnp.bfloat16), normed, preferred_element_type=jnp.float32
    ).astype(jnp.bfloat16)
    full_weights = lax.all_gather(w_experts, "kv", axis=3, tiled=True)
    slot_block = lax.all_to_all(buffer, "req", split_axis=0, concat_axis=0, tiled=True)
    source_count = slot_block.shape[0] // exp_dev
    grouped = slot_block.reshape(source_count, exp_dev, slot_block.shape[1], width_model)
    gate_act = jnp.einsum(
        "sejd,edf->sejf", grouped, full_weights[:, 0], preferred_element_type=jnp.float32
    )
    up_act = jnp.einsum(
        "sejd,edf->sejf", grouped, full_weights[:, 1], preferred_element_type=jnp.float32
    )
    activated = (jax.nn.silu(gate_act) * up_act).astype(jnp.bfloat16)
    expert_out = jnp.einsum(
        "sejf,edf->sejd", activated, full_weights[:, 2], preferred_element_type=jnp.float32
    ).astype(jnp.bfloat16)
    returned = lax.all_to_all(
        expert_out.reshape(slot_block.shape), "req", split_axis=0, concat_axis=0, tiled=True
    )
    combine = jnp.where(selector, pick_weight.T[:, None, :], 0.0)
    combine_hi = combine.astype(jnp.bfloat16)
    combine_lo = (combine - combine_hi.astype(jnp.float32)).astype(jnp.bfloat16)
    returned = returned.reshape(experts, capacity, width_model)
    expert_sum = jnp.einsum(
        "ect,ecd->td", combine_hi, returned, preferred_element_type=jnp.float32
    ) + jnp.einsum("ect,ecd->td", combine_lo, returned, preferred_element_type=jnp.float32)
    layer_out = (
        (residual + expert_sum).astype(jnp.bfloat16).reshape(local_reqs, local_tokens, width_model)
    )
    return (layer_out, decode_pool)


def solution(mesh):
    return jax.shard_map(
        body,
        mesh=mesh,
        in_specs=(
            P("req", "kv", None),
            P("req", "kv", None),
            P("req", "kv", None, None),
            P("req", "kv", None, None),
            P(),
            P(),
            P(),
            P(),
            P(("req", "kv"), None),
            P(("req", "kv"), None),
            P("req", None, None, "kv"),
            P("req", None),
        ),
        out_specs=(P("req", "kv", None), P("req", "kv", None, None)),
        check_vma=False,
    )
```

```python
import functools
import math

import jax
import jax.numpy as jnp
from jax import lax
from jax.experimental import pallas as pl
from jax.experimental.pallas import tpu as pltpu
from jax.sharding import PartitionSpec as P

BLOCK = 16


REQ = ("zhi", "rlow")


def lookup_lengths(req_order, cached_len, count):
    start = lax.axis_index(REQ) * count
    mine = lax.dynamic_slice_in_dim(req_order, start, count)
    match = mine[:, None] == jnp.arange(cached_len.shape[0], dtype=jnp.int32)[None, :]
    return jnp.sum(jnp.where(match, cached_len[None, :], 0), axis=1)


def attend_kernel(len_ref, q_ref, c_ref, s_ref, o_ref, *, tk, head_dim):
    b = pl.program_id(0)
    length = len_ref[b]
    span = q_ref.shape[1]
    lanes = q_ref.shape[2]
    per_group = lanes // head_dim
    scale = 1.0 / math.sqrt(head_dim)
    lane = lax.broadcasted_iota(jnp.int32, (span, lanes), 1)
    q_all = q_ref[0].astype(jnp.float32)
    nblk = (length + tk - 1) // tk
    row = lax.broadcasted_iota(jnp.int32, (span, span), 0)
    col = lax.broadcasted_iota(jnp.int32, (span, span), 1)
    causal = col <= row
    span_keys = s_ref[0]
    dims = (((1,), (1,)), ((), ()))
    outs = []
    for j in range(per_group):
        shifted = q_all if j == 0 else pltpu.roll(q_all, lanes - j * head_dim, 1)
        qj = jnp.where(lane < head_dim, shifted, 0.0).astype(jnp.bfloat16)

        def block_scores(kb):
            start = pl.multiple_of(kb * tk, tk)
            keys = c_ref[0, pl.ds(start, tk), :]
            s = lax.dot_general(qj, keys, dims, preferred_element_type=jnp.float32) * scale
            pos = start + lax.broadcasted_iota(jnp.int32, (span, tk), 1)
            return keys, pos < length, s

        def max_body(kb, m):
            _, ok, s = block_scores(kb)
            return jnp.maximum(m, jnp.max(jnp.where(ok, s, -1e30), axis=1, keepdims=True))

        s_span = lax.dot_general(qj, span_keys, dims, preferred_element_type=jnp.float32) * scale
        m0 = jnp.max(jnp.where(causal, s_span, -1e30), axis=1, keepdims=True)
        m = lax.fori_loop(0, nblk, max_body, m0)

        def sum_body(kb, carry):
            l, acc = carry
            keys, ok, s = block_scores(kb)
            p = jnp.where(ok, jnp.exp(s - m), 0.0)
            l = l + jnp.sum(p, axis=1, keepdims=True)
            acc = acc + jnp.dot(p.astype(jnp.bfloat16), keys, preferred_element_type=jnp.float32)
            return l, acc

        p_span = jnp.where(causal, jnp.exp(s_span - m), 0.0)
        l0 = jnp.sum(p_span, axis=1, keepdims=True)
        acc0 = jnp.dot(p_span.astype(jnp.bfloat16), span_keys, preferred_element_type=jnp.float32)
        l, acc = lax.fori_loop(0, nblk, sum_body, (l0, acc0))
        res = acc / l
        shift = (j * head_dim - head_dim) % lanes
        outs.append(res if shift == 0 else pltpu.roll(res, shift, 1))
    out = outs[0]
    for j in range(1, per_group):
        out = jnp.where(lane >= j * head_dim, outs[j], out)
    o_ref[0] = out.astype(o_ref.dtype)


def attend(query_heads, cache_heads, span_heads, lengths):
    local_reqs, span, groups, lanes = query_heads.shape
    cached = cache_heads.shape[1]
    head_dim = cache_heads.shape[-1] // 2
    tk = 256 if cached % 256 == 0 else cached
    q2 = query_heads.reshape(local_reqs, span, groups * lanes)
    c2 = cache_heads.reshape(local_reqs, cached, groups * lanes)
    s2 = span_heads.reshape(local_reqs, span, groups * lanes)
    flops = 2 * local_reqs * groups * (lanes // head_dim) * span * (cached + span) * lanes * 3
    out = pl.pallas_call(
        functools.partial(attend_kernel, tk=tk, head_dim=head_dim),
        out_shape=jax.ShapeDtypeStruct(q2.shape, jnp.bfloat16),
        grid_spec=pltpu.PrefetchScalarGridSpec(
            num_scalar_prefetch=1,
            grid=(local_reqs, groups),
            in_specs=[
                pl.BlockSpec((1, span, lanes), lambda b, g, n: (b, 0, g)),
                pl.BlockSpec((1, cached, lanes), lambda b, g, n: (b, 0, g)),
                pl.BlockSpec((1, span, lanes), lambda b, g, n: (b, 0, g)),
            ],
            out_specs=pl.BlockSpec((1, span, lanes), lambda b, g, n: (b, 0, g)),
        ),
        cost_estimate=pl.CostEstimate(
            flops=flops,
            transcendentals=local_reqs * groups * 2 * span * (cached + span),
            bytes_accessed=2 * (2 * q2.size + c2.size + s2.size),
        ),
    )(lengths.astype(jnp.int32), q2, c2, s2)
    return out.reshape(local_reqs, span, groups, lanes)


def place_pages(page_rows, slot_numbers, slots_dev):
    owner_index = slot_numbers // slots_dev
    arrangement = jnp.argsort(owner_index, stable=True)
    return (page_rows[arrangement], (slot_numbers % slots_dev)[arrangement])


def body(
    hidden,
    queries,
    span_kv,
    cache,
    req_order,
    cached_len,
    out_weight,
    norm_gain,
    expert_ids,
    expert_weights,
    w_experts,
    block_map,
):
    local_reqs, local_tokens, width_model = hidden.shape
    row_count = local_reqs * local_tokens
    req_count = lax.axis_size(REQ)
    kv_count = lax.axis_size("kv")
    kv_heads = span_kv.shape[2]
    head_pair = span_kv.shape[3]
    group_width = queries.shape[2] // kv_heads
    group_count = kv_heads // kv_count
    slots_dev = local_reqs * block_map.shape[1]
    lengths = lookup_lengths(req_order, cached_len, local_reqs)
    queries_grouped = queries.reshape(local_reqs, local_tokens, kv_heads, group_width)
    cache_heads, span_heads, query_heads = (
        lax.all_to_all(cache, "kv", split_axis=2, concat_axis=1, tiled=True),
        lax.all_to_all(span_kv, "kv", split_axis=2, concat_axis=1, tiled=True),
        lax.all_to_all(queries_grouped, "kv", split_axis=2, concat_axis=1, tiled=True),
    )
    attn_heads = attend(query_heads, cache_heads, span_heads, lengths)
    attn = lax.all_to_all(attn_heads, "kv", split_axis=1, concat_axis=2, tiled=True).reshape(
        row_count, kv_heads * group_width
    )
    page_total = block_map.shape[1]
    visible = jnp.arange(cache_heads.shape[1])[None, :] < lengths[:, None]
    visible_cache = jnp.where(visible[:, :, None, None], cache_heads, jnp.zeros((), jnp.bfloat16))
    page_rows = (
        visible_cache.reshape(local_reqs, page_total, BLOCK, group_count, head_pair)
        .transpose(0, 1, 3, 2, 4)
        .reshape(local_reqs * page_total, group_count, BLOCK, head_pair)
    )
    sorted_pages, local_slot = place_pages(page_rows, block_map.reshape(-1), slots_dev)
    per_owner = sorted_pages.shape[0] // req_count
    outgoing = sorted_pages.reshape(req_count, per_owner, group_count, BLOCK, head_pair)
    arrived, where_to = (
        lax.all_to_all(outgoing, REQ, split_axis=0, concat_axis=0, tiled=True),
        lax.all_to_all(
            local_slot.reshape(req_count, per_owner), REQ, split_axis=0, concat_axis=0, tiled=True
        ),
    )
    placement = (
        where_to.reshape(1, -1) == jnp.arange(slots_dev, dtype=jnp.int32)[:, None]
    ).astype(jnp.bfloat16)
    decode_pool = jnp.dot(
        placement,
        arrived.reshape(slots_dev, group_count * BLOCK * head_pair),
        preferred_element_type=jnp.float32,
    ).astype(jnp.bfloat16).reshape(slots_dev, group_count, BLOCK, head_pair)
    residual = hidden.reshape(row_count, width_model).astype(jnp.float32) + jnp.dot(
        attn, out_weight, preferred_element_type=jnp.float32
    )
    inverse_rms = lax.rsqrt(jnp.mean(residual * residual, axis=-1, keepdims=True) + 1e-05)
    normed = (residual * inverse_rms * norm_gain).astype(jnp.bfloat16)
    top_count = expert_ids.shape[1]
    exp_dev = w_experts.shape[0]
    experts = exp_dev * req_count
    capacity = min(row_count, 2 * row_count * top_count // experts)
    halves = lax.axis_size("zhi")
    side = lax.axis_size("rlow")
    match = expert_ids[:, :, None] == jnp.arange(experts, dtype=jnp.int32)[None, None, :]
    picks = jnp.sum(match.astype(jnp.int32), axis=1)
    pick_weight = jnp.sum(jnp.where(match, expert_weights[:, :, None], 0.0), axis=1)
    rank = jnp.cumsum(picks, axis=0) - 1

    def side_major(table):
        return (
            table.reshape(halves, side, exp_dev, row_count)
            .transpose(1, 0, 2, 3)
            .reshape(experts, row_count)
        )

    slot_of = side_major(jnp.where(picks > 0, rank, -1).T)
    weight_of = side_major(pick_weight.T)
    selector = slot_of[:, None, :] == jnp.arange(capacity, dtype=jnp.int32)[None, :, None]
    buffer = jnp.einsum(
        "ect,td->ecd", selector.astype(jnp.bfloat16), normed, preferred_element_type=jnp.float32
    ).astype(jnp.bfloat16)
    pair_weights = lax.all_gather(w_experts, "zhi", axis=0, tiled=True)
    full_weights = lax.all_gather(pair_weights, "kv", axis=3, tiled=True)
    per_dev = halves * exp_dev
    slot_block = lax.all_to_all(
        buffer.reshape(side, per_dev * capacity, width_model), "rlow", split_axis=0, concat_axis=0, tiled=True
    )
    grouped = slot_block.reshape(side, per_dev, capacity, width_model)
    gate_act = jnp.einsum(
        "sejd,edf->sejf", grouped, full_weights[:, 0], preferred_element_type=jnp.float32
    )
    up_act = jnp.einsum(
        "sejd,edf->sejf", grouped, full_weights[:, 1], preferred_element_type=jnp.float32
    )
    activated = (jax.nn.silu(gate_act) * up_act).astype(jnp.bfloat16)
    expert_out = jnp.einsum(
        "sejf,edf->sejd", activated, full_weights[:, 2], preferred_element_type=jnp.float32
    ).astype(jnp.bfloat16)
    returned = lax.all_to_all(
        expert_out.reshape(side, per_dev * capacity, width_model), "rlow", split_axis=0, concat_axis=0, tiled=True
    )
    combine = jnp.where(selector, weight_of[:, None, :], 0.0)
    combine_hi = combine.astype(jnp.bfloat16)
    combine_lo = (combine - combine_hi.astype(jnp.float32)).astype(jnp.bfloat16)
    returned = returned.reshape(experts, capacity, width_model)
    expert_sum = jnp.einsum(
        "ect,ecd->td", combine_hi, returned, preferred_element_type=jnp.float32
    ) + jnp.einsum("ect,ecd->td", combine_lo, returned, preferred_element_type=jnp.float32)
    layer_out = (
        (residual + expert_sum).astype(jnp.bfloat16).reshape(local_reqs, local_tokens, width_model)
    )
    return (layer_out, decode_pool)


def solution(mesh):
    devices = mesh.devices
    req_total, kv_total = devices.shape
    split_mesh = jax.sharding.Mesh(
        devices.reshape(2, req_total // 2, kv_total), ("zhi", "rlow", "kv")
    )
    return jax.shard_map(
        body,
        mesh=split_mesh,
        in_specs=(
            P(REQ, "kv", None),
            P(REQ, "kv", None),
            P(REQ, "kv", None, None),
            P(REQ, "kv", None, None),
            P(),
            P(),
            P(),
            P(),
            P((*REQ, "kv"), None),
            P((*REQ, "kv"), None),
            P(REQ, None, None, "kv"),
            P(REQ, None),
        ),
        out_specs=(P(REQ, "kv", None), P(REQ, "kv", None, None)),
        check_vma=False,
    )
```

```python
import functools
import math

import jax
import jax.numpy as jnp
from jax import lax
from jax.experimental import pallas as pl
from jax.experimental.pallas import tpu as pltpu
from jax.sharding import PartitionSpec as P

BLOCK = 16


REQ = ("zhi", "rlow")


def lookup_lengths(req_order, cached_len, count):
    start = lax.axis_index(REQ) * count
    mine = lax.dynamic_slice_in_dim(req_order, start, count)
    match = mine[:, None] == jnp.arange(cached_len.shape[0], dtype=jnp.int32)[None, :]
    return jnp.sum(jnp.where(match, cached_len[None, :], 0), axis=1)


def attend_kernel(len_ref, q_ref, c_ref, s_ref, o_ref, *, tk, head_dim):
    b = pl.program_id(0)
    length = len_ref[b]
    span = q_ref.shape[1]
    lanes = q_ref.shape[2]
    per_group = lanes // head_dim
    scale = 1.0 / math.sqrt(head_dim)
    lane = lax.broadcasted_iota(jnp.int32, (span, lanes), 1)
    q_all = q_ref[0].astype(jnp.float32)
    nblk = (length + tk - 1) // tk
    row = lax.broadcasted_iota(jnp.int32, (span, span), 0)
    col = lax.broadcasted_iota(jnp.int32, (span, span), 1)
    causal = col <= row
    span_keys = s_ref[0]
    dims = (((1,), (1,)), ((), ()))
    outs = []
    for j in range(per_group):
        shifted = q_all if j == 0 else pltpu.roll(q_all, lanes - j * head_dim, 1)
        qj = jnp.where(lane < head_dim, shifted, 0.0).astype(jnp.bfloat16)

        def block_scores(kb):
            start = pl.multiple_of(kb * tk, tk)
            keys = c_ref[0, pl.ds(start, tk), :]
            s = lax.dot_general(qj, keys, dims, preferred_element_type=jnp.float32) * scale
            pos = start + lax.broadcasted_iota(jnp.int32, (span, tk), 1)
            return keys, pos < length, s

        def max_body(kb, m):
            _, ok, s = block_scores(kb)
            return jnp.maximum(m, jnp.max(jnp.where(ok, s, -1e30), axis=1, keepdims=True))

        s_span = lax.dot_general(qj, span_keys, dims, preferred_element_type=jnp.float32) * scale
        m0 = jnp.max(jnp.where(causal, s_span, -1e30), axis=1, keepdims=True)
        m = lax.fori_loop(0, nblk, max_body, m0)

        def sum_body(kb, carry):
            l, acc = carry
            keys, ok, s = block_scores(kb)
            p = jnp.where(ok, jnp.exp(s - m), 0.0)
            l = l + jnp.sum(p, axis=1, keepdims=True)
            acc = acc + jnp.dot(p.astype(jnp.bfloat16), keys, preferred_element_type=jnp.float32)
            return l, acc

        p_span = jnp.where(causal, jnp.exp(s_span - m), 0.0)
        l0 = jnp.sum(p_span, axis=1, keepdims=True)
        acc0 = jnp.dot(p_span.astype(jnp.bfloat16), span_keys, preferred_element_type=jnp.float32)
        l, acc = lax.fori_loop(0, nblk, sum_body, (l0, acc0))
        res = acc / l
        shift = (j * head_dim - head_dim) % lanes
        outs.append(res if shift == 0 else pltpu.roll(res, shift, 1))
    out = outs[0]
    for j in range(1, per_group):
        out = jnp.where(lane >= j * head_dim, outs[j], out)
    o_ref[0] = out.astype(o_ref.dtype)


def attend(query_heads, cache_heads, span_heads, lengths):
    local_reqs, span, groups, lanes = query_heads.shape
    cached = cache_heads.shape[1]
    head_dim = cache_heads.shape[-1] // 2
    tk = 256 if cached % 256 == 0 else cached
    q2 = query_heads.reshape(local_reqs, span, groups * lanes)
    c2 = cache_heads.reshape(local_reqs, cached, groups * lanes)
    s2 = span_heads.reshape(local_reqs, span, groups * lanes)
    flops = 2 * local_reqs * groups * (lanes // head_dim) * span * (cached + span) * lanes * 3
    out = pl.pallas_call(
        functools.partial(attend_kernel, tk=tk, head_dim=head_dim),
        out_shape=jax.ShapeDtypeStruct(q2.shape, jnp.bfloat16),
        grid_spec=pltpu.PrefetchScalarGridSpec(
            num_scalar_prefetch=1,
            grid=(local_reqs, groups),
            in_specs=[
                pl.BlockSpec((1, span, lanes), lambda b, g, n: (b, 0, g)),
                pl.BlockSpec((1, cached, lanes), lambda b, g, n: (b, 0, g)),
                pl.BlockSpec((1, span, lanes), lambda b, g, n: (b, 0, g)),
            ],
            out_specs=pl.BlockSpec((1, span, lanes), lambda b, g, n: (b, 0, g)),
        ),
        cost_estimate=pl.CostEstimate(
            flops=flops,
            transcendentals=local_reqs * groups * 2 * span * (cached + span),
            bytes_accessed=2 * (2 * q2.size + c2.size + s2.size),
        ),
    )(lengths.astype(jnp.int32), q2, c2, s2)
    return out.reshape(local_reqs, span, groups, lanes)


def place_pages(page_rows, slot_numbers, slots_dev):
    owner_index = slot_numbers // slots_dev
    arrangement = jnp.argsort(owner_index, stable=True)
    return (page_rows[arrangement], (slot_numbers % slots_dev)[arrangement])


def body(
    hidden,
    queries,
    span_kv,
    cache,
    req_order,
    cached_len,
    out_weight,
    norm_gain,
    expert_ids,
    expert_weights,
    w_experts,
    block_map,
):
    local_reqs, local_tokens, width_model = hidden.shape
    row_count = local_reqs * local_tokens
    req_count = lax.axis_size(REQ)
    kv_count = lax.axis_size("kv")
    kv_heads = span_kv.shape[2]
    head_pair = span_kv.shape[3]
    group_width = queries.shape[2] // kv_heads
    group_count = kv_heads // kv_count
    slots_dev = local_reqs * block_map.shape[1]
    lengths = lookup_lengths(req_order, cached_len, local_reqs)
    queries_grouped = queries.reshape(local_reqs, local_tokens, kv_heads, group_width)
    cache_heads, span_heads, query_heads = (
        lax.all_to_all(cache, "kv", split_axis=2, concat_axis=1, tiled=True),
        lax.all_to_all(span_kv, "kv", split_axis=2, concat_axis=1, tiled=True),
        lax.all_to_all(queries_grouped, "kv", split_axis=2, concat_axis=1, tiled=True),
    )
    full_weights = lax.all_gather(w_experts, ("zhi", "kv"), axis=0, tiled=False)
    page_total = block_map.shape[1]
    visible = jnp.arange(cache_heads.shape[1])[None, :] < lengths[:, None]
    visible_cache = jnp.where(visible[:, :, None, None], cache_heads, jnp.zeros((), jnp.bfloat16))
    page_rows = (
        visible_cache.reshape(local_reqs, page_total, BLOCK, group_count, head_pair)
        .transpose(0, 1, 3, 2, 4)
        .reshape(local_reqs * page_total, group_count, BLOCK, head_pair)
    )
    sorted_pages, local_slot = place_pages(page_rows, block_map.reshape(-1), slots_dev)
    per_owner = sorted_pages.shape[0] // req_count
    outgoing = sorted_pages.reshape(req_count, per_owner, group_count, BLOCK, head_pair)
    arrived, where_to = (
        lax.all_to_all(outgoing, REQ, split_axis=0, concat_axis=0, tiled=True),
        lax.all_to_all(
            local_slot.reshape(req_count, per_owner), REQ, split_axis=0, concat_axis=0, tiled=True
        ),
    )
    attn_heads = attend(query_heads, cache_heads, span_heads, lengths)
    attn_heads, full_weights, arrived, where_to = lax.optimization_barrier(
        (attn_heads, full_weights, arrived, where_to)
    )
    attn = lax.all_to_all(attn_heads, "kv", split_axis=1, concat_axis=2, tiled=True).reshape(
        row_count, kv_heads * group_width
    )
    placement = (
        where_to.reshape(1, -1) == jnp.arange(slots_dev, dtype=jnp.int32)[:, None]
    ).astype(jnp.bfloat16)
    decode_pool = jnp.dot(
        placement,
        arrived.reshape(slots_dev, group_count * BLOCK * head_pair),
        preferred_element_type=jnp.float32,
    ).astype(jnp.bfloat16).reshape(slots_dev, group_count, BLOCK, head_pair)
    residual = hidden.reshape(row_count, width_model).astype(jnp.float32) + jnp.dot(
        attn, out_weight, preferred_element_type=jnp.float32
    )
    inverse_rms = lax.rsqrt(jnp.mean(residual * residual, axis=-1, keepdims=True) + 1e-05)
    normed = (residual * inverse_rms * norm_gain).astype(jnp.bfloat16)
    top_count = expert_ids.shape[1]
    exp_dev = w_experts.shape[0]
    experts = exp_dev * req_count
    capacity = min(row_count, 2 * row_count * top_count // experts)
    halves = lax.axis_size("zhi")
    side = lax.axis_size("rlow")
    match = expert_ids[:, :, None] == jnp.arange(experts, dtype=jnp.int32)[None, None, :]
    picks = jnp.sum(match.astype(jnp.int32), axis=1)
    pick_weight = jnp.sum(jnp.where(match, expert_weights[:, :, None], 0.0), axis=1)
    rank = jnp.cumsum(picks, axis=0) - 1

    def side_major(table):
        return (
            table.reshape(halves, side, exp_dev, row_count)
            .transpose(1, 0, 2, 3)
            .reshape(experts, row_count)
        )

    slot_of = side_major(jnp.where(picks > 0, rank, -1).T)
    weight_of = side_major(pick_weight.T)
    selector = slot_of[:, None, :] == jnp.arange(capacity, dtype=jnp.int32)[None, :, None]
    buffer = jnp.einsum(
        "ect,td->ecd", selector.astype(jnp.bfloat16), normed, preferred_element_type=jnp.float32
    ).astype(jnp.bfloat16)
    per_dev = halves * exp_dev
    slot_block = lax.all_to_all(
        buffer.reshape(side, per_dev * capacity, width_model), "rlow", split_axis=0, concat_axis=0, tiled=True
    )
    grouped = slot_block.reshape(side, halves, exp_dev, capacity, width_model)
    weights = full_weights.reshape(halves, kv_count, *w_experts.shape)
    gate_act = jnp.einsum(
        "szjcd,zkjdf->szjckf", grouped, weights[:, :, :, 0], preferred_element_type=jnp.float32
    )
    up_act = jnp.einsum(
        "szjcd,zkjdf->szjckf", grouped, weights[:, :, :, 1], preferred_element_type=jnp.float32
    )
    activated = (jax.nn.silu(gate_act) * up_act).astype(jnp.bfloat16)
    expert_out = jnp.einsum(
        "szjckf,zkjdf->szjcd", activated, weights[:, :, :, 2], preferred_element_type=jnp.float32
    ).astype(jnp.bfloat16)
    returned = lax.all_to_all(
        expert_out.reshape(side, per_dev * capacity, width_model), "rlow", split_axis=0, concat_axis=0, tiled=True
    )
    combine = jnp.where(selector, weight_of[:, None, :], 0.0)
    combine_hi = combine.astype(jnp.bfloat16)
    combine_lo = (combine - combine_hi.astype(jnp.float32)).astype(jnp.bfloat16)
    returned = returned.reshape(experts, capacity, width_model)
    expert_sum = jnp.einsum(
        "ect,ecd->td", combine_hi, returned, preferred_element_type=jnp.float32
    ) + jnp.einsum("ect,ecd->td", combine_lo, returned, preferred_element_type=jnp.float32)
    layer_out = (
        (residual + expert_sum).astype(jnp.bfloat16).reshape(local_reqs, local_tokens, width_model)
    )
    return (layer_out, decode_pool)


def solution(mesh):
    devices = mesh.devices
    req_total, kv_total = devices.shape
    split_mesh = jax.sharding.Mesh(
        devices.reshape(2, req_total // 2, kv_total), ("zhi", "rlow", "kv")
    )
    return jax.shard_map(
        body,
        mesh=split_mesh,
        in_specs=(
            P(REQ, "kv", None),
            P(REQ, "kv", None),
            P(REQ, "kv", None, None),
            P(REQ, "kv", None, None),
            P(),
            P(),
            P(),
            P(),
            P((*REQ, "kv"), None),
            P((*REQ, "kv"), None),
            P(REQ, None, None, "kv"),
            P(REQ, None),
        ),
        out_specs=(P(REQ, "kv", None), P(REQ, "kv", None, None)),
        check_vma=False,
    )
```

```python
import functools
import math

import jax
import jax.numpy as jnp
from jax import lax
from jax.experimental import pallas as pl
from jax.experimental.pallas import tpu as pltpu
from jax.sharding import PartitionSpec as P

BLOCK = 16


REQ = ("zhi", "rlow")


def lookup_lengths(req_order, cached_len, count):
    start = lax.axis_index(REQ) * count
    mine = lax.dynamic_slice_in_dim(req_order, start, count)
    match = mine[:, None] == jnp.arange(cached_len.shape[0], dtype=jnp.int32)[None, :]
    return jnp.sum(jnp.where(match, cached_len[None, :], 0), axis=1)


def attend_kernel(len_ref, q_ref, c_ref, s_ref, o_ref, *, tk, head_dim):
    b = pl.program_id(0)
    length = len_ref[b]
    span = q_ref.shape[1]
    lanes = q_ref.shape[2]
    per_group = lanes // head_dim
    scale = 1.0 / math.sqrt(head_dim)
    lane = lax.broadcasted_iota(jnp.int32, (span, lanes), 1)
    q_all = q_ref[0].astype(jnp.float32) * scale
    blocks = c_ref.shape[1] // tk
    full = length // tk
    tail = jnp.minimum(full, blocks - 1)
    row = lax.broadcasted_iota(jnp.int32, (span, span), 0)
    col = lax.broadcasted_iota(jnp.int32, (span, span), 1)
    causal = col <= row
    key_lane = lax.broadcasted_iota(jnp.int32, (tk, lanes), 1) < head_dim
    span_lane = lax.broadcasted_iota(jnp.int32, (span, lanes), 1) < head_dim
    span_keys = s_ref[0]
    span_vals = jnp.where(span_lane, jnp.ones_like(span_keys), span_keys)
    dims = (((1,), (1,)), ((), ()))
    tail_pos = tail * tk + lax.broadcasted_iota(jnp.int32, (span, tk), 1)
    tail_ok = (tail_pos >= full * tk) & (tail_pos < length)
    outs = []
    for j in range(per_group):
        shifted = q_all if j == 0 else pltpu.roll(q_all, lanes - j * head_dim, 1)
        qj = jnp.where(lane < head_dim, shifted, 0.0).astype(jnp.bfloat16)

        def block(kb):
            start = pl.multiple_of(kb * tk, tk)
            keys = c_ref[0, pl.ds(start, tk), :]
            s = lax.dot_general(qj, keys, dims, preferred_element_type=jnp.float32)
            return keys, s

        def max_body(kb, m):
            _, s = block(kb)
            return jnp.maximum(m, jnp.max(s, axis=1, keepdims=True))

        s_span = lax.dot_general(qj, span_keys, dims, preferred_element_type=jnp.float32)
        m = jnp.max(jnp.where(causal, s_span, -1e30), axis=1, keepdims=True)
        m = lax.fori_loop(0, full, max_body, m)
        _, s_tail = block(tail)
        m = jnp.maximum(m, jnp.max(jnp.where(tail_ok, s_tail, -1e30), axis=1, keepdims=True))

        def accumulate(acc, p, keys):
            vals = jnp.where(key_lane, jnp.ones_like(keys), keys)
            return acc + jnp.dot(p.astype(jnp.bfloat16), vals, preferred_element_type=jnp.float32)

        def sum_body(kb, acc):
            keys, s = block(kb)
            return accumulate(acc, jnp.exp(s - m), keys)

        p_span = jnp.where(causal, jnp.exp(s_span - m), 0.0)
        acc = jnp.dot(p_span.astype(jnp.bfloat16), span_vals, preferred_element_type=jnp.float32)
        acc = lax.fori_loop(0, full, sum_body, acc)
        keys_tail, s_tail = block(tail)
        acc = accumulate(acc, jnp.where(tail_ok, jnp.exp(s_tail - m), 0.0), keys_tail)
        total = acc[:, 0:1]
        res = acc / total
        shift = (j * head_dim - head_dim) % lanes
        outs.append(res if shift == 0 else pltpu.roll(res, shift, 1))
    out = outs[0]
    for j in range(1, per_group):
        out = jnp.where(lane >= j * head_dim, outs[j], out)
    o_ref[0] = out.astype(o_ref.dtype)


def attend(query_heads, cache_heads, span_heads, lengths):
    local_reqs, span, groups, lanes = query_heads.shape
    cached = cache_heads.shape[1]
    head_dim = cache_heads.shape[-1] // 2
    tk = 256 if cached % 256 == 0 else cached
    q2 = query_heads.reshape(local_reqs, span, groups * lanes)
    c2 = cache_heads.reshape(local_reqs, cached, groups * lanes)
    s2 = span_heads.reshape(local_reqs, span, groups * lanes)
    flops = 2 * local_reqs * groups * (lanes // head_dim) * span * (cached + span) * lanes * 3
    out = pl.pallas_call(
        functools.partial(attend_kernel, tk=tk, head_dim=head_dim),
        out_shape=jax.ShapeDtypeStruct(q2.shape, jnp.bfloat16),
        grid_spec=pltpu.PrefetchScalarGridSpec(
            num_scalar_prefetch=1,
            grid=(local_reqs, groups),
            in_specs=[
                pl.BlockSpec((1, span, lanes), lambda b, g, n: (b, 0, g)),
                pl.BlockSpec((1, cached, lanes), lambda b, g, n: (b, 0, g)),
                pl.BlockSpec((1, span, lanes), lambda b, g, n: (b, 0, g)),
            ],
            out_specs=pl.BlockSpec((1, span, lanes), lambda b, g, n: (b, 0, g)),
        ),
        cost_estimate=pl.CostEstimate(
            flops=flops,
            transcendentals=local_reqs * groups * 2 * span * (cached + span),
            bytes_accessed=2 * (2 * q2.size + c2.size + s2.size),
        ),
    )(lengths.astype(jnp.int32), q2, c2, s2)
    return out.reshape(local_reqs, span, groups, lanes)


def place_pages(page_rows, slot_numbers, slots_dev):
    owner_index = slot_numbers // slots_dev
    arrangement = jnp.argsort(owner_index, stable=True)
    return (page_rows[arrangement], (slot_numbers % slots_dev)[arrangement])


def body(
    hidden,
    queries,
    span_kv,
    cache,
    req_order,
    cached_len,
    out_weight,
    norm_gain,
    expert_ids,
    expert_weights,
    w_experts,
    block_map,
):
    local_reqs, local_tokens, width_model = hidden.shape
    row_count = local_reqs * local_tokens
    req_count = lax.axis_size(REQ)
    kv_count = lax.axis_size("kv")
    kv_heads = span_kv.shape[2]
    head_pair = span_kv.shape[3]
    group_width = queries.shape[2] // kv_heads
    group_count = kv_heads // kv_count
    slots_dev = local_reqs * block_map.shape[1]
    lengths = lookup_lengths(req_order, cached_len, local_reqs)
    queries_grouped = queries.reshape(local_reqs, local_tokens, kv_heads, group_width)
    cache_heads, span_heads, query_heads = (
        lax.all_to_all(cache, "kv", split_axis=2, concat_axis=1, tiled=True),
        lax.all_to_all(span_kv, "kv", split_axis=2, concat_axis=1, tiled=True),
        lax.all_to_all(queries_grouped, "kv", split_axis=2, concat_axis=1, tiled=True),
    )
    expert_part, cache_heads = lax.optimization_barrier((w_experts, cache_heads))
    full_weights = lax.all_gather(expert_part, ("zhi", "kv"), axis=0, tiled=False)
    page_total = block_map.shape[1]
    visible = jnp.arange(cache_heads.shape[1])[None, :] < lengths[:, None]
    visible_cache = jnp.where(visible[:, :, None, None], cache_heads, jnp.zeros((), jnp.bfloat16))
    page_rows = (
        visible_cache.reshape(local_reqs, page_total, BLOCK, group_count, head_pair)
        .transpose(0, 1, 3, 2, 4)
        .reshape(local_reqs * page_total, group_count, BLOCK, head_pair)
    )
    sorted_pages, local_slot = place_pages(page_rows, block_map.reshape(-1), slots_dev)
    per_owner = sorted_pages.shape[0] // req_count
    outgoing = sorted_pages.reshape(req_count, per_owner, group_count, BLOCK, head_pair)
    arrived, where_to = (
        lax.all_to_all(outgoing, REQ, split_axis=0, concat_axis=0, tiled=True),
        lax.all_to_all(
            local_slot.reshape(req_count, per_owner), REQ, split_axis=0, concat_axis=0, tiled=True
        ),
    )
    attn_heads = attend(query_heads, cache_heads, span_heads, lengths)
    attn_heads, full_weights, arrived, where_to = lax.optimization_barrier(
        (attn_heads, full_weights, arrived, where_to)
    )
    attn = lax.all_to_all(attn_heads, "kv", split_axis=1, concat_axis=2, tiled=True).reshape(
        row_count, kv_heads * group_width
    )
    placement = (
        where_to.reshape(1, -1) == jnp.arange(slots_dev, dtype=jnp.int32)[:, None]
    ).astype(jnp.bfloat16)
    decode_pool = jnp.dot(
        placement,
        arrived.reshape(slots_dev, group_count * BLOCK * head_pair),
        preferred_element_type=jnp.float32,
    ).astype(jnp.bfloat16).reshape(slots_dev, group_count, BLOCK, head_pair)
    residual = hidden.reshape(row_count, width_model).astype(jnp.float32) + jnp.dot(
        attn, out_weight, preferred_element_type=jnp.float32
    )
    inverse_rms = lax.rsqrt(jnp.mean(residual * residual, axis=-1, keepdims=True) + 1e-05)
    normed = (residual * inverse_rms * norm_gain).astype(jnp.bfloat16)
    top_count = expert_ids.shape[1]
    exp_dev = w_experts.shape[0]
    experts = exp_dev * req_count
    capacity = min(row_count, 2 * row_count * top_count // experts)
    halves = lax.axis_size("zhi")
    side = lax.axis_size("rlow")
    match = expert_ids[:, :, None] == jnp.arange(experts, dtype=jnp.int32)[None, None, :]
    picks = jnp.sum(match.astype(jnp.int32), axis=1)
    pick_weight = jnp.sum(jnp.where(match, expert_weights[:, :, None], 0.0), axis=1)
    rank = jnp.cumsum(picks, axis=0) - 1

    def side_major(table):
        return (
            table.reshape(halves, side, exp_dev, row_count)
            .transpose(1, 0, 2, 3)
            .reshape(experts, row_count)
        )

    slot_of = side_major(jnp.where(picks > 0, rank, -1).T)
    weight_of = side_major(pick_weight.T)
    selector = slot_of[:, None, :] == jnp.arange(capacity, dtype=jnp.int32)[None, :, None]
    buffer = jnp.einsum(
        "ect,td->ecd", selector.astype(jnp.bfloat16), normed, preferred_element_type=jnp.float32
    ).astype(jnp.bfloat16)
    per_dev = halves * exp_dev
    slot_block = lax.all_to_all(
        buffer.reshape(side, per_dev * capacity, width_model), "rlow", split_axis=0, concat_axis=0, tiled=True
    )
    grouped = slot_block.reshape(side, halves, exp_dev, capacity, width_model)
    weights = full_weights.reshape(halves, kv_count, *w_experts.shape)
    gate_act = jnp.einsum(
        "szjcd,zkjdf->szjckf", grouped, weights[:, :, :, 0], preferred_element_type=jnp.float32
    )
    up_act = jnp.einsum(
        "szjcd,zkjdf->szjckf", grouped, weights[:, :, :, 1], preferred_element_type=jnp.float32
    )
    activated = (jax.nn.silu(gate_act) * up_act).astype(jnp.bfloat16)
    expert_out = jnp.einsum(
        "szjckf,zkjdf->szjcd", activated, weights[:, :, :, 2], preferred_element_type=jnp.float32
    ).astype(jnp.bfloat16)
    returned = lax.all_to_all(
        expert_out.reshape(side, per_dev * capacity, width_model), "rlow", split_axis=0, concat_axis=0, tiled=True
    )
    combine = jnp.where(selector, weight_of[:, None, :], 0.0)
    combine_hi = combine.astype(jnp.bfloat16)
    combine_lo = (combine - combine_hi.astype(jnp.float32)).astype(jnp.bfloat16)
    returned = returned.reshape(experts, capacity, width_model)
    expert_sum = jnp.einsum(
        "ect,ecd->td", combine_hi, returned, preferred_element_type=jnp.float32
    ) + jnp.einsum("ect,ecd->td", combine_lo, returned, preferred_element_type=jnp.float32)
    layer_out = (
        (residual + expert_sum).astype(jnp.bfloat16).reshape(local_reqs, local_tokens, width_model)
    )
    return (layer_out, decode_pool)


def solution(mesh):
    devices = mesh.devices
    req_total, kv_total = devices.shape
    split_mesh = jax.sharding.Mesh(
        devices.reshape(2, req_total // 2, kv_total), ("zhi", "rlow", "kv")
    )
    return jax.shard_map(
        body,
        mesh=split_mesh,
        in_specs=(
            P(REQ, "kv", None),
            P(REQ, "kv", None),
            P(REQ, "kv", None, None),
            P(REQ, "kv", None, None),
            P(),
            P(),
            P(),
            P(),
            P((*REQ, "kv"), None),
            P((*REQ, "kv"), None),
            P(REQ, None, None, "kv"),
            P(REQ, None),
        ),
        out_specs=(P(REQ, "kv", None), P(REQ, "kv", None, None)),
        check_vma=False,
    )
```

```python
import functools
import math

import jax
import jax.numpy as jnp
from jax import lax
from jax.experimental import pallas as pl
from jax.experimental.pallas import tpu as pltpu
from jax.sharding import PartitionSpec as P

BLOCK = 16


REQ = ("zhi", "rlow")


def lookup_lengths(req_order, cached_len, count):
    start = lax.axis_index(REQ) * count
    mine = lax.dynamic_slice_in_dim(req_order, start, count)
    match = mine[:, None] == jnp.arange(cached_len.shape[0], dtype=jnp.int32)[None, :]
    return jnp.sum(jnp.where(match, cached_len[None, :], 0), axis=1)


def attend_kernel(len_ref, q_ref, c_ref, s_ref, o_ref, *, tk, head_dim):
    b = pl.program_id(0)
    length = len_ref[b]
    span = q_ref.shape[1]
    lanes = q_ref.shape[2]
    per_group = lanes // head_dim
    scale = 1.0 / math.sqrt(head_dim)
    lane = lax.broadcasted_iota(jnp.int32, (span, lanes), 1)
    q_all = q_ref[0].astype(jnp.float32) * scale
    blocks = c_ref.shape[1] // tk
    full = length // tk
    tail = jnp.minimum(full, blocks - 1)
    row = lax.broadcasted_iota(jnp.int32, (span, span), 0)
    col = lax.broadcasted_iota(jnp.int32, (span, span), 1)
    causal = col <= row
    key_lane = lax.broadcasted_iota(jnp.int32, (tk, lanes), 1) < head_dim
    span_lane = lax.broadcasted_iota(jnp.int32, (span, lanes), 1) < head_dim
    span_keys = s_ref[0]
    span_vals = jnp.where(span_lane, jnp.ones_like(span_keys), span_keys)
    dims = (((1,), (1,)), ((), ()))
    tail_pos = tail * tk + lax.broadcasted_iota(jnp.int32, (span, tk), 1)
    tail_ok = (tail_pos >= full * tk) & (tail_pos < length)
    outs = []
    for j in range(per_group):
        shifted = q_all if j == 0 else pltpu.roll(q_all, lanes - j * head_dim, 1)
        qj = jnp.where(lane < head_dim, shifted, 0.0).astype(jnp.bfloat16)

        def block(kb):
            start = pl.multiple_of(kb * tk, tk)
            keys = c_ref[0, pl.ds(start, tk), :]
            s = lax.dot_general(qj, keys, dims, preferred_element_type=jnp.float32)
            return keys, s

        def max_body(kb, m):
            _, s = block(kb)
            return jnp.maximum(m, jnp.max(s, axis=1, keepdims=True))

        s_span = lax.dot_general(qj, span_keys, dims, preferred_element_type=jnp.float32)
        m = jnp.max(jnp.where(causal, s_span, -1e30), axis=1, keepdims=True)
        m = lax.fori_loop(0, full, max_body, m)
        _, s_tail = block(tail)
        m = jnp.maximum(m, jnp.max(jnp.where(tail_ok, s_tail, -1e30), axis=1, keepdims=True))

        def accumulate(acc, p, keys):
            vals = jnp.where(key_lane, jnp.ones_like(keys), keys)
            return acc + jnp.dot(p.astype(jnp.bfloat16), vals, preferred_element_type=jnp.float32)

        def sum_body(kb, acc):
            keys, s = block(kb)
            return accumulate(acc, jnp.exp(s - m), keys)

        p_span = jnp.where(causal, jnp.exp(s_span - m), 0.0)
        acc = jnp.dot(p_span.astype(jnp.bfloat16), span_vals, preferred_element_type=jnp.float32)
        acc = lax.fori_loop(0, full, sum_body, acc)
        keys_tail, s_tail = block(tail)
        acc = accumulate(acc, jnp.where(tail_ok, jnp.exp(s_tail - m), 0.0), keys_tail)
        total = acc[:, 0:1]
        res = acc / total
        shift = (j * head_dim - head_dim) % lanes
        outs.append(res if shift == 0 else pltpu.roll(res, shift, 1))
    out = outs[0]
    for j in range(1, per_group):
        out = jnp.where(lane >= j * head_dim, outs[j], out)
    o_ref[0] = out.astype(o_ref.dtype)


def attend(query_heads, cache_heads, span_heads, lengths):
    local_reqs, span, groups, lanes = query_heads.shape
    cached = cache_heads.shape[1]
    head_dim = cache_heads.shape[-1] // 2
    tk = 256 if cached % 256 == 0 else cached
    q2 = query_heads.reshape(local_reqs, span, groups * lanes)
    c2 = cache_heads.reshape(local_reqs, cached, groups * lanes)
    s2 = span_heads.reshape(local_reqs, span, groups * lanes)
    flops = 2 * local_reqs * groups * (lanes // head_dim) * span * (cached + span) * lanes * 3
    out = pl.pallas_call(
        functools.partial(attend_kernel, tk=tk, head_dim=head_dim),
        out_shape=jax.ShapeDtypeStruct(q2.shape, jnp.bfloat16),
        grid_spec=pltpu.PrefetchScalarGridSpec(
            num_scalar_prefetch=1,
            grid=(local_reqs, groups),
            in_specs=[
                pl.BlockSpec((1, span, lanes), lambda b, g, n: (b, 0, g)),
                pl.BlockSpec((1, cached, lanes), lambda b, g, n: (b, 0, g)),
                pl.BlockSpec((1, span, lanes), lambda b, g, n: (b, 0, g)),
            ],
            out_specs=pl.BlockSpec((1, span, lanes), lambda b, g, n: (b, 0, g)),
        ),
        cost_estimate=pl.CostEstimate(
            flops=flops,
            transcendentals=local_reqs * groups * 2 * span * (cached + span),
            bytes_accessed=2 * (2 * q2.size + c2.size + s2.size),
        ),
    )(lengths.astype(jnp.int32), q2, c2, s2)
    return out.reshape(local_reqs, span, groups, lanes)


def place_pages(page_rows, slot_numbers, slots_dev):
    owner_index = slot_numbers // slots_dev
    arrangement = jnp.argsort(owner_index, stable=True)
    return (page_rows[arrangement], (slot_numbers % slots_dev)[arrangement])


def body(
    hidden,
    queries,
    span_kv,
    cache,
    req_order,
    cached_len,
    out_weight,
    norm_gain,
    expert_ids,
    expert_weights,
    w_experts,
    block_map,
):
    local_reqs, local_tokens, width_model = hidden.shape
    row_count = local_reqs * local_tokens
    req_count = lax.axis_size(REQ)
    kv_count = lax.axis_size("kv")
    kv_heads = span_kv.shape[2]
    head_pair = span_kv.shape[3]
    group_width = queries.shape[2] // kv_heads
    group_count = kv_heads // kv_count
    slots_dev = local_reqs * block_map.shape[1]
    lengths = lookup_lengths(req_order, cached_len, local_reqs)
    queries_grouped = queries.reshape(local_reqs, local_tokens, kv_heads, group_width)
    cache_heads, span_heads, query_heads = (
        lax.all_to_all(cache, "kv", split_axis=2, concat_axis=1, tiled=True),
        lax.all_to_all(span_kv, "kv", split_axis=2, concat_axis=1, tiled=True),
        lax.all_to_all(queries_grouped, "kv", split_axis=2, concat_axis=1, tiled=True),
    )
    pair_weights = lax.all_gather(w_experts, "zhi", axis=0, tiled=False)
    pair_weights, cache_heads = lax.optimization_barrier((pair_weights, cache_heads))
    full_weights = lax.all_gather(pair_weights, "kv", axis=1, tiled=False)
    page_total = block_map.shape[1]
    visible = jnp.arange(cache_heads.shape[1])[None, :] < lengths[:, None]
    visible_cache = jnp.where(visible[:, :, None, None], cache_heads, jnp.zeros((), jnp.bfloat16))
    page_rows = (
        visible_cache.reshape(local_reqs, page_total, BLOCK, group_count, head_pair)
        .transpose(0, 1, 3, 2, 4)
        .reshape(local_reqs * page_total, group_count, BLOCK, head_pair)
    )
    sorted_pages, local_slot = place_pages(page_rows, block_map.reshape(-1), slots_dev)
    per_owner = sorted_pages.shape[0] // req_count
    outgoing = sorted_pages.reshape(req_count, per_owner, group_count, BLOCK, head_pair)
    arrived, where_to = (
        lax.all_to_all(outgoing, REQ, split_axis=0, concat_axis=0, tiled=True),
        lax.all_to_all(
            local_slot.reshape(req_count, per_owner), REQ, split_axis=0, concat_axis=0, tiled=True
        ),
    )
    attn_heads = attend(query_heads, cache_heads, span_heads, lengths)
    attn_heads, full_weights, arrived, where_to = lax.optimization_barrier(
        (attn_heads, full_weights, arrived, where_to)
    )
    attn = lax.all_to_all(attn_heads, "kv", split_axis=1, concat_axis=2, tiled=True).reshape(
        row_count, kv_heads * group_width
    )
    placement = (
        where_to.reshape(1, -1) == jnp.arange(slots_dev, dtype=jnp.int32)[:, None]
    ).astype(jnp.bfloat16)
    decode_pool = jnp.dot(
        placement,
        arrived.reshape(slots_dev, group_count * BLOCK * head_pair),
        preferred_element_type=jnp.float32,
    ).astype(jnp.bfloat16).reshape(slots_dev, group_count, BLOCK, head_pair)
    residual = hidden.reshape(row_count, width_model).astype(jnp.float32) + jnp.dot(
        attn, out_weight, preferred_element_type=jnp.float32
    )
    inverse_rms = lax.rsqrt(jnp.mean(residual * residual, axis=-1, keepdims=True) + 1e-05)
    normed = (residual * inverse_rms * norm_gain).astype(jnp.bfloat16)
    top_count = expert_ids.shape[1]
    exp_dev = w_experts.shape[0]
    experts = exp_dev * req_count
    capacity = min(row_count, 2 * row_count * top_count // experts)
    halves = lax.axis_size("zhi")
    side = lax.axis_size("rlow")
    match = expert_ids[:, :, None] == jnp.arange(experts, dtype=jnp.int32)[None, None, :]
    picks = jnp.sum(match.astype(jnp.int32), axis=1)
    pick_weight = jnp.sum(jnp.where(match, expert_weights[:, :, None], 0.0), axis=1)
    rank = jnp.cumsum(picks, axis=0) - 1

    def side_major(table):
        return (
            table.reshape(halves, side, exp_dev, row_count)
            .transpose(1, 0, 2, 3)
            .reshape(experts, row_count)
        )

    slot_of = side_major(jnp.where(picks > 0, rank, -1).T)
    weight_of = side_major(pick_weight.T)
    selector = slot_of[:, None, :] == jnp.arange(capacity, dtype=jnp.int32)[None, :, None]
    buffer = jnp.einsum(
        "ect,td->ecd", selector.astype(jnp.bfloat16), normed, preferred_element_type=jnp.float32
    ).astype(jnp.bfloat16)
    per_dev = halves * exp_dev
    slot_block = lax.all_to_all(
        buffer.reshape(side, per_dev * capacity, width_model), "rlow", split_axis=0, concat_axis=0, tiled=True
    )
    grouped = slot_block.reshape(side, halves, exp_dev, capacity, width_model)
    weights = full_weights.reshape(halves, kv_count, *w_experts.shape)
    gate_act = jnp.einsum(
        "szjcd,zkjdf->szjckf", grouped, weights[:, :, :, 0], preferred_element_type=jnp.float32
    )
    up_act = jnp.einsum(
        "szjcd,zkjdf->szjckf", grouped, weights[:, :, :, 1], preferred_element_type=jnp.float32
    )
    activated = (jax.nn.silu(gate_act) * up_act).astype(jnp.bfloat16)
    expert_out = jnp.einsum(
        "szjckf,zkjdf->szjcd", activated, weights[:, :, :, 2], preferred_element_type=jnp.float32
    ).astype(jnp.bfloat16)
    returned = lax.all_to_all(
        expert_out.reshape(side, per_dev * capacity, width_model), "rlow", split_axis=0, concat_axis=0, tiled=True
    )
    combine = jnp.where(selector, weight_of[:, None, :], 0.0)
    combine_hi = combine.astype(jnp.bfloat16)
    combine_lo = (combine - combine_hi.astype(jnp.float32)).astype(jnp.bfloat16)
    returned = returned.reshape(experts, capacity, width_model)
    expert_sum = jnp.einsum(
        "ect,ecd->td", combine_hi, returned, preferred_element_type=jnp.float32
    ) + jnp.einsum("ect,ecd->td", combine_lo, returned, preferred_element_type=jnp.float32)
    layer_out = (
        (residual + expert_sum).astype(jnp.bfloat16).reshape(local_reqs, local_tokens, width_model)
    )
    return (layer_out, decode_pool)


def solution(mesh):
    devices = mesh.devices
    req_total, kv_total = devices.shape
    split_mesh = jax.sharding.Mesh(
        devices.reshape(2, req_total // 2, kv_total), ("zhi", "rlow", "kv")
    )
    return jax.shard_map(
        body,
        mesh=split_mesh,
        in_specs=(
            P(REQ, "kv", None),
            P(REQ, "kv", None),
            P(REQ, "kv", None, None),
            P(REQ, "kv", None, None),
            P(),
            P(),
            P(),
            P(),
            P((*REQ, "kv"), None),
            P((*REQ, "kv"), None),
            P(REQ, None, None, "kv"),
            P(REQ, None),
        ),
        out_specs=(P(REQ, "kv", None), P(REQ, "kv", None, None)),
        check_vma=False,
    )
```

```python
import functools
import math

import jax
import jax.numpy as jnp
from jax import lax
from jax.experimental import pallas as pl
from jax.experimental.pallas import tpu as pltpu
from jax.sharding import PartitionSpec as P

BLOCK = 16


REQ = ("zhi", "rlow")


def lookup_lengths(req_order, cached_len, count):
    start = lax.axis_index(REQ) * count
    mine = lax.dynamic_slice_in_dim(req_order, start, count)
    match = mine[:, None] == jnp.arange(cached_len.shape[0], dtype=jnp.int32)[None, :]
    return jnp.sum(jnp.where(match, cached_len[None, :], 0), axis=1)


def attend_kernel(meta_ref, q_ref, c_ref, s_ref, o_ref, st_ref, *, tk, head_dim):
    b = pl.program_id(0)
    reqs = pl.num_programs(0)
    cached = c_ref.shape[1]
    length = jnp.clip(meta_ref[b], 0, cached)
    offset = meta_ref[reqs]
    span = q_ref.shape[1]
    span_here = s_ref.shape[1]
    lanes = q_ref.shape[2]
    per_group = lanes // head_dim
    scale = 1.0 / math.sqrt(head_dim)
    lane = lax.broadcasted_iota(jnp.int32, (span, lanes), 1)
    q_all = q_ref[0].astype(jnp.float32) * scale
    blocks = cached // tk
    full = length // tk
    tail = jnp.minimum(full, blocks - 1)
    row = lax.broadcasted_iota(jnp.int32, (span, span_here), 0)
    col = lax.broadcasted_iota(jnp.int32, (span, span_here), 1)
    causal = col + offset <= row
    key_lane = lax.broadcasted_iota(jnp.int32, (tk, lanes), 1) < head_dim
    span_lane = lax.broadcasted_iota(jnp.int32, (span_here, lanes), 1) < head_dim
    span_keys = s_ref[0]
    span_vals = jnp.where(span_lane, jnp.ones_like(span_keys), span_keys)
    dims = (((1,), (1,)), ((), ()))
    tail_pos = tail * tk + lax.broadcasted_iota(jnp.int32, (span, tk), 1)
    tail_ok = (tail_pos >= full * tk) & (tail_pos < length)
    outs, stats = [], []
    for j in range(per_group):
        shifted = q_all if j == 0 else pltpu.roll(q_all, lanes - j * head_dim, 1)
        qj = jnp.where(lane < head_dim, shifted, 0.0).astype(jnp.bfloat16)

        def block(kb):
            start = pl.multiple_of(kb * tk, tk)
            keys = c_ref[0, pl.ds(start, tk), :]
            s = lax.dot_general(qj, keys, dims, preferred_element_type=jnp.float32)
            return keys, s

        def max_body(kb, m):
            _, s = block(kb)
            return jnp.maximum(m, jnp.max(s, axis=1, keepdims=True))

        s_span = lax.dot_general(qj, span_keys, dims, preferred_element_type=jnp.float32)
        m = jnp.max(jnp.where(causal, s_span, -1e30), axis=1, keepdims=True)
        m = lax.fori_loop(0, full, max_body, m)
        _, s_tail = block(tail)
        m = jnp.maximum(m, jnp.max(jnp.where(tail_ok, s_tail, -1e30), axis=1, keepdims=True))

        def accumulate(acc, p, keys):
            vals = jnp.where(key_lane, jnp.ones_like(keys), keys)
            return acc + jnp.dot(p.astype(jnp.bfloat16), vals, preferred_element_type=jnp.float32)

        def sum_body(kb, acc):
            keys, s = block(kb)
            return accumulate(acc, jnp.exp(s - m), keys)

        p_span = jnp.where(causal, jnp.exp(s_span - m), 0.0)
        acc = jnp.dot(p_span.astype(jnp.bfloat16), span_vals, preferred_element_type=jnp.float32)
        acc = lax.fori_loop(0, full, sum_body, acc)
        keys_tail, s_tail = block(tail)
        acc = accumulate(acc, jnp.where(tail_ok, jnp.exp(s_tail - m), 0.0), keys_tail)
        total = acc[:, 0:1]
        res = acc / jnp.where(total > 0.0, total, 1.0)
        shift = (j * head_dim - head_dim) % lanes
        outs.append(res if shift == 0 else pltpu.roll(res, shift, 1))
        stats.append((m, total))
    out = outs[0]
    stat = jnp.zeros((span, lanes), jnp.float32)
    for j in range(per_group):
        if j > 0:
            out = jnp.where(lane >= j * head_dim, outs[j], out)
        m, total = stats[j]
        here = (lane >= j * head_dim) & (lane < (j + 1) * head_dim)
        first = lane < j * head_dim + head_dim // 2
        stat = jnp.where(here, jnp.where(first, m, total), stat)
    o_ref[0] = out.astype(o_ref.dtype)
    st_ref[0] = stat


def attend(q_all, cache, span_kv, meta):
    local_reqs, span, width = q_all.shape
    cached, kv_heads, lanes = cache.shape[1:]
    span_here = span_kv.shape[1]
    head_dim = lanes // 2
    tk = 256 if cached % 256 == 0 else cached
    c2 = cache.reshape(local_reqs, cached, kv_heads * lanes)
    s2 = span_kv.reshape(local_reqs, span_here, kv_heads * lanes)
    flops = 2 * local_reqs * kv_heads * (lanes // head_dim) * span * (cached + span_here) * lanes * 3
    out, stat = pl.pallas_call(
        functools.partial(attend_kernel, tk=tk, head_dim=head_dim),
        out_shape=(
            jax.ShapeDtypeStruct(q_all.shape, jnp.bfloat16),
            jax.ShapeDtypeStruct(q_all.shape, jnp.float32),
        ),
        grid_spec=pltpu.PrefetchScalarGridSpec(
            num_scalar_prefetch=1,
            grid=(local_reqs, kv_heads),
            in_specs=[
                pl.BlockSpec((1, span, lanes), lambda b, g, n: (b, 0, g)),
                pl.BlockSpec((1, cached, lanes), lambda b, g, n: (b, 0, g)),
                pl.BlockSpec((1, span_here, lanes), lambda b, g, n: (b, 0, g)),
            ],
            out_specs=(
                pl.BlockSpec((1, span, lanes), lambda b, g, n: (b, 0, g)),
                pl.BlockSpec((1, span, lanes), lambda b, g, n: (b, 0, g)),
            ),
        ),
        cost_estimate=pl.CostEstimate(
            flops=flops,
            transcendentals=local_reqs * kv_heads * 2 * span * (cached + span_here),
            bytes_accessed=2 * (3 * q_all.size + c2.size + s2.size) + 4 * q_all.size,
        ),
    )(meta, q_all, c2, s2)
    return out, stat


def place_pages(page_rows, slot_numbers, slots_dev):
    owner_index = slot_numbers // slots_dev
    arrangement = jnp.argsort(owner_index, stable=True)
    return (page_rows[arrangement], (slot_numbers % slots_dev)[arrangement])


def body(
    hidden,
    queries,
    span_kv,
    cache,
    req_order,
    cached_len,
    out_weight,
    norm_gain,
    expert_ids,
    expert_weights,
    w_experts,
    block_map,
):
    local_reqs, local_tokens, width_model = hidden.shape
    row_count = local_reqs * local_tokens
    req_count = lax.axis_size(REQ)
    kv_count = lax.axis_size("kv")
    kv_heads = span_kv.shape[2]
    head_pair = span_kv.shape[3]
    group_width = queries.shape[2] // kv_heads
    group_count = kv_heads // kv_count
    slots_dev = local_reqs * block_map.shape[1]
    lengths = lookup_lengths(req_order, cached_len, local_reqs)
    kv_index = lax.axis_index("kv")
    cached_local = cache.shape[1]
    head_dim = head_pair // 2
    heads = kv_heads * (group_width // head_dim)
    full_weights = lax.all_gather(w_experts, ("zhi", "kv"), axis=0, tiled=False)
    pages_local = cached_local // BLOCK
    position = kv_index * cached_local + jnp.arange(cached_local)
    visible = position[None, :] < lengths[:, None]
    visible_cache = jnp.where(visible[:, :, None, None], cache, jnp.zeros((), jnp.bfloat16))
    page_rows = (
        visible_cache.reshape(local_reqs, pages_local, BLOCK, kv_heads, head_pair)
        .transpose(0, 1, 3, 2, 4)
        .reshape(local_reqs * pages_local, kv_heads, BLOCK, head_pair)
    )
    my_map = lax.dynamic_slice_in_dim(block_map, kv_index * pages_local, pages_local, axis=1)
    sorted_pages, local_slot = place_pages(page_rows, my_map.reshape(-1), slots_dev)
    per_owner = sorted_pages.shape[0] // req_count
    outgoing = (
        sorted_pages.reshape(req_count, per_owner, kv_count, group_count, BLOCK, head_pair)
        .transpose(0, 2, 1, 3, 4, 5)
        .reshape(req_count * kv_count, per_owner, group_count, BLOCK, head_pair)
    )
    slots_out = jnp.broadcast_to(
        local_slot.reshape(req_count, 1, per_owner), (req_count, kv_count, per_owner)
    ).reshape(req_count * kv_count, per_owner)
    everyone = (*REQ, "kv")
    arrived, where_to = (
        lax.all_to_all(outgoing, everyone, split_axis=0, concat_axis=0, tiled=True),
        lax.all_to_all(slots_out, everyone, split_axis=0, concat_axis=0, tiled=True),
    )
    q_all = lax.all_gather(queries, "kv", axis=1, tiled=True)
    meta = jnp.concatenate(
        [lengths - kv_index * cached_local, (kv_index * local_tokens)[None]]
    ).astype(jnp.int32)
    part_out, part_stat = attend(q_all, cache, span_kv, meta)
    part_out, part_stat, full_weights, arrived, where_to = lax.optimization_barrier(
        (part_out, part_stat, full_weights, arrived, where_to)
    )
    span_total = q_all.shape[1]
    stat = part_stat.reshape(local_reqs, span_total, heads, 2, head_dim // 2)[..., 0]
    got_out = lax.all_to_all(
        part_out.reshape(local_reqs, kv_count, local_tokens, width_model),
        "kv", split_axis=1, concat_axis=1, tiled=True,
    )
    got_stat = lax.all_to_all(
        stat.reshape(local_reqs, kv_count, local_tokens, heads, 2),
        "kv", split_axis=1, concat_axis=1, tiled=True,
    )
    part_max = got_stat[..., 0]
    top = jnp.max(part_max, axis=1, keepdims=True)
    part_weight = got_stat[..., 1] * jnp.exp(part_max - top)
    merged = jnp.sum(
        got_out.reshape(local_reqs, kv_count, local_tokens, heads, head_dim).astype(jnp.float32)
        * part_weight[..., None],
        axis=1,
    ) / jnp.sum(part_weight, axis=1)[..., None]
    attn = merged.astype(jnp.bfloat16).reshape(row_count, width_model)
    placement = (
        where_to.reshape(1, -1) == jnp.arange(slots_dev, dtype=jnp.int32)[:, None]
    ).astype(jnp.bfloat16)
    decode_pool = jnp.dot(
        placement,
        arrived.reshape(slots_dev, group_count * BLOCK * head_pair),
        preferred_element_type=jnp.float32,
    ).astype(jnp.bfloat16).reshape(slots_dev, group_count, BLOCK, head_pair)
    residual = hidden.reshape(row_count, width_model).astype(jnp.float32) + jnp.dot(
        attn, out_weight, preferred_element_type=jnp.float32
    )
    inverse_rms = lax.rsqrt(jnp.mean(residual * residual, axis=-1, keepdims=True) + 1e-05)
    normed = (residual * inverse_rms * norm_gain).astype(jnp.bfloat16)
    top_count = expert_ids.shape[1]
    exp_dev = w_experts.shape[0]
    experts = exp_dev * req_count
    capacity = min(row_count, 2 * row_count * top_count // experts)
    halves = lax.axis_size("zhi")
    side = lax.axis_size("rlow")
    match = expert_ids[:, :, None] == jnp.arange(experts, dtype=jnp.int32)[None, None, :]
    picks = jnp.sum(match.astype(jnp.int32), axis=1)
    pick_weight = jnp.sum(jnp.where(match, expert_weights[:, :, None], 0.0), axis=1)
    rank = jnp.cumsum(picks, axis=0) - 1

    def side_major(table):
        return (
            table.reshape(halves, side, exp_dev, row_count)
            .transpose(1, 0, 2, 3)
            .reshape(experts, row_count)
        )

    slot_of = side_major(jnp.where(picks > 0, rank, -1).T)
    weight_of = side_major(pick_weight.T)
    selector = slot_of[:, None, :] == jnp.arange(capacity, dtype=jnp.int32)[None, :, None]
    buffer = jnp.einsum(
        "ect,td->ecd", selector.astype(jnp.bfloat16), normed, preferred_element_type=jnp.float32
    ).astype(jnp.bfloat16)
    per_dev = halves * exp_dev
    slot_block = lax.all_to_all(
        buffer.reshape(side, per_dev * capacity, width_model), "rlow", split_axis=0, concat_axis=0, tiled=True
    )
    grouped = slot_block.reshape(side, halves, exp_dev, capacity, width_model)
    weights = full_weights.reshape(halves, kv_count, *w_experts.shape)
    gate_act = jnp.einsum(
        "szjcd,zkjdf->szjckf", grouped, weights[:, :, :, 0], preferred_element_type=jnp.float32
    )
    up_act = jnp.einsum(
        "szjcd,zkjdf->szjckf", grouped, weights[:, :, :, 1], preferred_element_type=jnp.float32
    )
    activated = (jax.nn.silu(gate_act) * up_act).astype(jnp.bfloat16)
    expert_out = jnp.einsum(
        "szjckf,zkjdf->szjcd", activated, weights[:, :, :, 2], preferred_element_type=jnp.float32
    ).astype(jnp.bfloat16)
    returned = lax.all_to_all(
        expert_out.reshape(side, per_dev * capacity, width_model), "rlow", split_axis=0, concat_axis=0, tiled=True
    )
    combine = jnp.where(selector, weight_of[:, None, :], 0.0)
    combine_hi = combine.astype(jnp.bfloat16)
    combine_lo = (combine - combine_hi.astype(jnp.float32)).astype(jnp.bfloat16)
    returned = returned.reshape(experts, capacity, width_model)
    expert_sum = jnp.einsum(
        "ect,ecd->td", combine_hi, returned, preferred_element_type=jnp.float32
    ) + jnp.einsum("ect,ecd->td", combine_lo, returned, preferred_element_type=jnp.float32)
    layer_out = (
        (residual + expert_sum).astype(jnp.bfloat16).reshape(local_reqs, local_tokens, width_model)
    )
    return (layer_out, decode_pool)


def solution(mesh):
    devices = mesh.devices
    req_total, kv_total = devices.shape
    split_mesh = jax.sharding.Mesh(
        devices.reshape(2, req_total // 2, kv_total), ("zhi", "rlow", "kv")
    )
    return jax.shard_map(
        body,
        mesh=split_mesh,
        in_specs=(
            P(REQ, "kv", None),
            P(REQ, "kv", None),
            P(REQ, "kv", None, None),
            P(REQ, "kv", None, None),
            P(),
            P(),
            P(),
            P(),
            P((*REQ, "kv"), None),
            P((*REQ, "kv"), None),
            P(REQ, None, None, "kv"),
            P(REQ, None),
        ),
        out_specs=(P(REQ, "kv", None), P(REQ, "kv", None, None)),
        check_vma=False,
    )
```

```python
import functools
import math

import jax
import jax.numpy as jnp
from jax import lax
from jax.experimental import pallas as pl
from jax.experimental.pallas import tpu as pltpu
from jax.sharding import PartitionSpec as P

BLOCK = 16


REQ = ("zhi", "rlow")


def lookup_lengths(req_order, cached_len, count):
    start = lax.axis_index(REQ) * count
    mine = lax.dynamic_slice_in_dim(req_order, start, count)
    match = mine[:, None] == jnp.arange(cached_len.shape[0], dtype=jnp.int32)[None, :]
    return jnp.sum(jnp.where(match, cached_len[None, :], 0), axis=1)


def attend_kernel(meta_ref, q_ref, c_ref, *rest, piece, kv_count, head_dim, received):
    if received:
        o_ref, st_ref = rest
    else:
        s_ref, o_ref, st_ref = rest
    b = pl.program_id(0)
    reqs = pl.num_programs(0)
    length = meta_ref[b]
    me = meta_ref[reqs]
    cached = meta_ref[reqs + 1]
    span = q_ref.shape[1]
    lanes = q_ref.shape[2]
    per_group = lanes // head_dim
    step = kv_count * piece
    rounds = (c_ref.shape[1] if received else c_ref.shape[1] // step)
    scale = 1.0 / math.sqrt(head_dim)
    lane = lax.broadcasted_iota(jnp.int32, (span, lanes), 1)
    q_all = q_ref[0].astype(jnp.float32) * scale
    key_lane = lax.broadcasted_iota(jnp.int32, (piece, lanes), 1) < head_dim
    key_col = lax.broadcasted_iota(jnp.int32, (span, piece), 1)
    dims = (((1,), (1,)), ((), ()))

    def count(base):
        return jnp.minimum((jnp.maximum(length - base, 0) + step - 1) // step, rounds)

    runs = []
    if received:
        for t in range(1, kv_count):
            src = lax.rem(me + t, kv_count)
            base = src * cached + me * piece
            runs.append((count(base), functools.partial(
                lambda i, src, base: (c_ref[0, i, src], base + i * step), src=src, base=base)))
    else:
        base = me * cached + me * piece

        def local_piece(i):
            start = pl.multiple_of((i * kv_count + me) * piece, piece)
            return c_ref[0, pl.ds(start, piece), :], base + i * step

        runs.append((count(base), local_piece))
    if not received:
        span_keys = s_ref[0]
        span_here = span_keys.shape[0]
        row = lax.broadcasted_iota(jnp.int32, (span, span_here), 0)
        col = lax.broadcasted_iota(jnp.int32, (span, span_here), 1)
        causal = col + me * span_here <= row
        span_lane = lax.broadcasted_iota(jnp.int32, (span_here, lanes), 1) < head_dim
        span_vals = jnp.where(span_lane, jnp.ones_like(span_keys), span_keys)
    outs, stats = [], []
    for j in range(per_group):
        shifted = q_all if j == 0 else pltpu.roll(q_all, lanes - j * head_dim, 1)
        qj = jnp.where(lane < head_dim, shifted, 0.0).astype(jnp.bfloat16)

        def scores(get, i):
            keys, first = get(i)
            s = lax.dot_general(qj, keys, dims, preferred_element_type=jnp.float32)
            return keys, first + key_col < length, s

        m = jnp.full((span, 1), -1e30, jnp.float32)
        if not received:
            s_span = lax.dot_general(qj, span_keys, dims, preferred_element_type=jnp.float32)
            m = jnp.maximum(m, jnp.max(jnp.where(causal, s_span, -1e30), axis=1, keepdims=True))
        for n, get in runs:
            def max_body(i, m, get=get):
                _, ok, s = scores(get, i)
                return jnp.maximum(m, jnp.max(jnp.where(ok, s, -1e30), axis=1, keepdims=True))
            m = lax.fori_loop(0, n, max_body, m)
        acc = jnp.zeros((span, lanes), jnp.float32)
        if not received:
            p_span = jnp.where(causal, jnp.exp(s_span - m), 0.0)
            acc = acc + jnp.dot(p_span.astype(jnp.bfloat16), span_vals, preferred_element_type=jnp.float32)
        for n, get in runs:
            def sum_body(i, acc, get=get):
                keys, ok, s = scores(get, i)
                p = jnp.where(ok, jnp.exp(s - m), 0.0)
                vals = jnp.where(key_lane, jnp.ones_like(keys), keys)
                return acc + jnp.dot(p.astype(jnp.bfloat16), vals, preferred_element_type=jnp.float32)
            acc = lax.fori_loop(0, n, sum_body, acc)
        total = acc[:, 0:1]
        res = acc / jnp.where(total > 0.0, total, 1.0)
        shift = (j * head_dim - head_dim) % lanes
        outs.append(res if shift == 0 else pltpu.roll(res, shift, 1))
        stats.append((m, total))
    out = outs[0]
    stat = jnp.zeros((span, lanes), jnp.float32)
    for j in range(per_group):
        if j > 0:
            out = jnp.where(lane >= j * head_dim, outs[j], out)
        m, total = stats[j]
        here = (lane >= j * head_dim) & (lane < (j + 1) * head_dim)
        first = lane < j * head_dim + head_dim // 2
        stat = jnp.where(here, jnp.where(first, m, total), stat)
    o_ref[0] = out
    st_ref[0] = stat


def attend(q_all, keys, span_kv, meta, piece, kv_count):
    local_reqs, span, width = q_all.shape
    received = span_kv is None
    if received:
        _, rounds, _, _, kv_heads, lanes = keys.shape
        k2 = keys.reshape(local_reqs, rounds, kv_count, piece, kv_heads * lanes)
        key_spec = pl.BlockSpec((1, rounds, kv_count, piece, lanes), lambda b, g, n: (b, 0, 0, 0, g))
        key_count = rounds * (kv_count - 1) * piece
        operands = (k2,)
        specs = [key_spec]
    else:
        cached, kv_heads, lanes = keys.shape[1:]
        k2 = keys.reshape(local_reqs, cached, kv_heads * lanes)
        s2 = span_kv.reshape(local_reqs, span_kv.shape[1], kv_heads * lanes)
        key_count = cached // kv_count + s2.shape[1]
        operands = (k2, s2)
        specs = [
            pl.BlockSpec((1, cached, lanes), lambda b, g, n: (b, 0, g)),
            pl.BlockSpec((1, s2.shape[1], lanes), lambda b, g, n: (b, 0, g)),
        ]
    head_dim = lanes // 2
    flops = 2 * local_reqs * kv_heads * (lanes // head_dim) * span * key_count * lanes * 3
    return pl.pallas_call(
        functools.partial(
            attend_kernel, piece=piece, kv_count=kv_count, head_dim=head_dim, received=received
        ),
        out_shape=(
            jax.ShapeDtypeStruct(q_all.shape, jnp.float32),
            jax.ShapeDtypeStruct(q_all.shape, jnp.float32),
        ),
        grid_spec=pltpu.PrefetchScalarGridSpec(
            num_scalar_prefetch=1,
            grid=(local_reqs, kv_heads),
            in_specs=[pl.BlockSpec((1, span, lanes), lambda b, g, n: (b, 0, g))] + specs,
            out_specs=(
                pl.BlockSpec((1, span, lanes), lambda b, g, n: (b, 0, g)),
                pl.BlockSpec((1, span, lanes), lambda b, g, n: (b, 0, g)),
            ),
        ),
        cost_estimate=pl.CostEstimate(
            flops=flops,
            transcendentals=local_reqs * kv_heads * 2 * span * key_count,
            bytes_accessed=2 * (q_all.size + sum(x.size for x in operands)) + 8 * q_all.size,
        ),
    )(meta, q_all, *operands)


def place_pages(page_rows, slot_numbers, slots_dev):
    owner_index = slot_numbers // slots_dev
    arrangement = jnp.argsort(owner_index, stable=True)
    return (page_rows[arrangement], (slot_numbers % slots_dev)[arrangement])


def body(
    hidden,
    queries,
    span_kv,
    cache,
    req_order,
    cached_len,
    out_weight,
    norm_gain,
    expert_ids,
    expert_weights,
    w_experts,
    block_map,
):
    local_reqs, local_tokens, width_model = hidden.shape
    row_count = local_reqs * local_tokens
    req_count = lax.axis_size(REQ)
    kv_count = lax.axis_size("kv")
    kv_heads = span_kv.shape[2]
    head_pair = span_kv.shape[3]
    group_width = queries.shape[2] // kv_heads
    group_count = kv_heads // kv_count
    slots_dev = local_reqs * block_map.shape[1]
    lengths = lookup_lengths(req_order, cached_len, local_reqs)
    kv_index = lax.axis_index("kv")
    cached_local = cache.shape[1]
    head_dim = head_pair // 2
    heads = kv_heads * (group_width // head_dim)
    full_weights = lax.all_gather(w_experts, ("zhi", "kv"), axis=0, tiled=False)
    pages_local = cached_local // BLOCK
    position = kv_index * cached_local + jnp.arange(cached_local)
    visible = position[None, :] < lengths[:, None]
    visible_cache = jnp.where(visible[:, :, None, None], cache, jnp.zeros((), jnp.bfloat16))
    page_rows = (
        visible_cache.reshape(local_reqs, pages_local, BLOCK, kv_heads, head_pair)
        .transpose(0, 1, 3, 2, 4)
        .reshape(local_reqs * pages_local, kv_heads, BLOCK, head_pair)
    )
    my_map = lax.dynamic_slice_in_dim(block_map, kv_index * pages_local, pages_local, axis=1)
    sorted_pages, local_slot = place_pages(page_rows, my_map.reshape(-1), slots_dev)
    per_owner = sorted_pages.shape[0] // req_count
    outgoing = (
        sorted_pages.reshape(req_count, per_owner, kv_count, group_count, BLOCK, head_pair)
        .transpose(0, 2, 1, 3, 4, 5)
        .reshape(req_count * kv_count, per_owner, group_count, BLOCK, head_pair)
    )
    slots_out = jnp.broadcast_to(
        local_slot.reshape(req_count, 1, per_owner), (req_count, kv_count, per_owner)
    ).reshape(req_count * kv_count, per_owner)
    everyone = (*REQ, "kv")
    arrived, where_to = (
        lax.all_to_all(outgoing, everyone, split_axis=0, concat_axis=0, tiled=True),
        lax.all_to_all(slots_out, everyone, split_axis=0, concat_axis=0, tiled=True),
    )
    piece = min(256, cached_local // kv_count)
    rounds = cached_local // (kv_count * piece)
    dealt = lax.all_to_all(
        cache.reshape(local_reqs, rounds, kv_count, piece, kv_heads, head_pair),
        "kv", split_axis=2, concat_axis=2, tiled=True,
    )
    q_all = lax.all_gather(queries, "kv", axis=1, tiled=True)
    meta = jnp.concatenate(
        [lengths, kv_index[None], jnp.full((1,), cached_local)]
    ).astype(jnp.int32)
    own_out, own_stat = attend(q_all, cache, span_kv, meta, piece, kv_count)
    got_out, got_stat = attend(q_all, dealt, None, meta, piece, kv_count)
    span_total = q_all.shape[1]

    def split_stat(table):
        table = table.reshape(local_reqs, span_total, heads, 2, head_dim // 2)[..., 0]
        return table[..., 0], table[..., 1]

    own_max, own_sum = split_stat(own_stat)
    got_max, got_sum = split_stat(got_stat)
    top = jnp.maximum(own_max, got_max)
    own_w = own_sum * jnp.exp(own_max - top)
    got_w = got_sum * jnp.exp(got_max - top)
    both_w = own_w + got_w
    part_out = (
        (own_out.reshape(local_reqs, span_total, heads, head_dim) * own_w[..., None]
         + got_out.reshape(local_reqs, span_total, heads, head_dim) * got_w[..., None])
        / jnp.where(both_w > 0.0, both_w, 1.0)[..., None]
    ).astype(jnp.bfloat16).reshape(local_reqs, span_total, width_model)
    stat = jnp.stack([top, both_w], axis=-1)
    part_out, stat, full_weights = lax.optimization_barrier((part_out, stat, full_weights))
    got_out = lax.all_to_all(
        part_out.reshape(local_reqs, kv_count, local_tokens, width_model),
        "kv", split_axis=1, concat_axis=1, tiled=True,
    )
    got_stat = lax.all_to_all(
        stat.reshape(local_reqs, kv_count, local_tokens, heads, 2),
        "kv", split_axis=1, concat_axis=1, tiled=True,
    )
    part_max = got_stat[..., 0]
    top = jnp.max(part_max, axis=1, keepdims=True)
    part_weight = got_stat[..., 1] * jnp.exp(part_max - top)
    merged = jnp.sum(
        got_out.reshape(local_reqs, kv_count, local_tokens, heads, head_dim).astype(jnp.float32)
        * part_weight[..., None],
        axis=1,
    ) / jnp.sum(part_weight, axis=1)[..., None]
    attn = merged.astype(jnp.bfloat16).reshape(row_count, width_model)
    placement = (
        where_to.reshape(1, -1) == jnp.arange(slots_dev, dtype=jnp.int32)[:, None]
    ).astype(jnp.bfloat16)
    decode_pool = jnp.dot(
        placement,
        arrived.reshape(slots_dev, group_count * BLOCK * head_pair),
        preferred_element_type=jnp.float32,
    ).astype(jnp.bfloat16).reshape(slots_dev, group_count, BLOCK, head_pair)
    residual = hidden.reshape(row_count, width_model).astype(jnp.float32) + jnp.dot(
        attn, out_weight, preferred_element_type=jnp.float32
    )
    inverse_rms = lax.rsqrt(jnp.mean(residual * residual, axis=-1, keepdims=True) + 1e-05)
    normed = (residual * inverse_rms * norm_gain).astype(jnp.bfloat16)
    top_count = expert_ids.shape[1]
    exp_dev = w_experts.shape[0]
    experts = exp_dev * req_count
    capacity = min(row_count, 2 * row_count * top_count // experts)
    halves = lax.axis_size("zhi")
    side = lax.axis_size("rlow")
    match = expert_ids[:, :, None] == jnp.arange(experts, dtype=jnp.int32)[None, None, :]
    picks = jnp.sum(match.astype(jnp.int32), axis=1)
    pick_weight = jnp.sum(jnp.where(match, expert_weights[:, :, None], 0.0), axis=1)
    rank = jnp.cumsum(picks, axis=0) - 1

    def side_major(table):
        return (
            table.reshape(halves, side, exp_dev, row_count)
            .transpose(1, 0, 2, 3)
            .reshape(experts, row_count)
        )

    slot_of = side_major(jnp.where(picks > 0, rank, -1).T)
    weight_of = side_major(pick_weight.T)
    selector = slot_of[:, None, :] == jnp.arange(capacity, dtype=jnp.int32)[None, :, None]
    buffer = jnp.einsum(
        "ect,td->ecd", selector.astype(jnp.bfloat16), normed, preferred_element_type=jnp.float32
    ).astype(jnp.bfloat16)
    per_dev = halves * exp_dev
    slot_block = lax.all_to_all(
        buffer.reshape(side, per_dev * capacity, width_model), "rlow", split_axis=0, concat_axis=0, tiled=True
    )
    grouped = slot_block.reshape(side, halves, exp_dev, capacity, width_model)
    weights = full_weights.reshape(halves, kv_count, *w_experts.shape)
    gate_act = jnp.einsum(
        "szjcd,zkjdf->szjckf", grouped, weights[:, :, :, 0], preferred_element_type=jnp.float32
    )
    up_act = jnp.einsum(
        "szjcd,zkjdf->szjckf", grouped, weights[:, :, :, 1], preferred_element_type=jnp.float32
    )
    activated = (jax.nn.silu(gate_act) * up_act).astype(jnp.bfloat16)
    expert_out = jnp.einsum(
        "szjckf,zkjdf->szjcd", activated, weights[:, :, :, 2], preferred_element_type=jnp.float32
    ).astype(jnp.bfloat16)
    returned = lax.all_to_all(
        expert_out.reshape(side, per_dev * capacity, width_model), "rlow", split_axis=0, concat_axis=0, tiled=True
    )
    combine = jnp.where(selector, weight_of[:, None, :], 0.0)
    combine_hi = combine.astype(jnp.bfloat16)
    combine_lo = (combine - combine_hi.astype(jnp.float32)).astype(jnp.bfloat16)
    returned = returned.reshape(experts, capacity, width_model)
    expert_sum = jnp.einsum(
        "ect,ecd->td", combine_hi, returned, preferred_element_type=jnp.float32
    ) + jnp.einsum("ect,ecd->td", combine_lo, returned, preferred_element_type=jnp.float32)
    layer_out = (
        (residual + expert_sum).astype(jnp.bfloat16).reshape(local_reqs, local_tokens, width_model)
    )
    return (layer_out, decode_pool)


def solution(mesh):
    devices = mesh.devices
    req_total, kv_total = devices.shape
    split_mesh = jax.sharding.Mesh(
        devices.reshape(2, req_total // 2, kv_total), ("zhi", "rlow", "kv")
    )
    return jax.shard_map(
        body,
        mesh=split_mesh,
        in_specs=(
            P(REQ, "kv", None),
            P(REQ, "kv", None),
            P(REQ, "kv", None, None),
            P(REQ, "kv", None, None),
            P(),
            P(),
            P(),
            P(),
            P((*REQ, "kv"), None),
            P((*REQ, "kv"), None),
            P(REQ, None, None, "kv"),
            P(REQ, None),
        ),
        out_specs=(P(REQ, "kv", None), P(REQ, "kv", None, None)),
        check_vma=False,
    )
```

```python
import functools
import math

import jax
import jax.numpy as jnp
from jax import lax
from jax.experimental import pallas as pl
from jax.experimental.pallas import tpu as pltpu
from jax.sharding import PartitionSpec as P

BLOCK = 16


REQ = ("zhi", "rlow")


def lookup_lengths(req_order, cached_len, count):
    start = lax.axis_index(REQ) * count
    mine = lax.dynamic_slice_in_dim(req_order, start, count)
    match = mine[:, None] == jnp.arange(cached_len.shape[0], dtype=jnp.int32)[None, :]
    return jnp.sum(jnp.where(match, cached_len[None, :], 0), axis=1)


def attend_kernel(meta_ref, q_ref, c_ref, *rest, piece, kv_count, head_dim, received):
    if received:
        o_ref, st_ref = rest
    else:
        s_ref, o_ref, st_ref = rest
    b = pl.program_id(0)
    reqs = pl.num_programs(0)
    length = meta_ref[b]
    me = meta_ref[reqs]
    cached = meta_ref[reqs + 1]
    span = q_ref.shape[1]
    lanes = q_ref.shape[2]
    per_group = lanes // head_dim
    step = kv_count * piece
    rounds = (c_ref.shape[1] if received else c_ref.shape[1] // step)
    scale = 1.0 / math.sqrt(head_dim)
    lane = lax.broadcasted_iota(jnp.int32, (span, lanes), 1)
    q_all = q_ref[0].astype(jnp.float32) * scale
    key_lane = lax.broadcasted_iota(jnp.int32, (piece, lanes), 1) < head_dim
    key_col = lax.broadcasted_iota(jnp.int32, (span, piece), 1)
    dims = (((1,), (1,)), ((), ()))

    def count(base):
        return jnp.minimum((jnp.maximum(length - base, 0) + step - 1) // step, rounds)

    runs = []
    if received:
        for t in range(1, kv_count):
            src = lax.rem(me + t, kv_count)
            base = src * cached + me * piece
            runs.append((count(base), functools.partial(
                lambda i, src, base: (c_ref[0, i, src], base + i * step), src=src, base=base)))
    else:
        base = me * cached + me * piece

        def local_piece(i):
            start = pl.multiple_of((i * kv_count + me) * piece, piece)
            return c_ref[0, pl.ds(start, piece), :], base + i * step

        runs.append((count(base), local_piece))
    if not received:
        span_keys = s_ref[0]
        span_here = span_keys.shape[0]
        row = lax.broadcasted_iota(jnp.int32, (span, span_here), 0)
        col = lax.broadcasted_iota(jnp.int32, (span, span_here), 1)
        causal = col + me * span_here <= row
        span_lane = lax.broadcasted_iota(jnp.int32, (span_here, lanes), 1) < head_dim
        span_vals = jnp.where(span_lane, jnp.ones_like(span_keys), span_keys)
    outs, stats = [], []
    for j in range(per_group):
        shifted = q_all if j == 0 else pltpu.roll(q_all, lanes - j * head_dim, 1)
        qj = jnp.where(lane < head_dim, shifted, 0.0).astype(jnp.bfloat16)

        def scores(get, i):
            keys, first = get(i)
            s = lax.dot_general(qj, keys, dims, preferred_element_type=jnp.float32)
            return keys, first + key_col < length, s

        m = jnp.full((span, 1), -1e30, jnp.float32)
        acc = jnp.zeros((span, lanes), jnp.float32)

        def update(m, acc, ok, s, vals):
            m_new = jnp.maximum(m, jnp.max(jnp.where(ok, s, -1e30), axis=1, keepdims=True))
            p = jnp.where(ok, jnp.exp(s - m_new), 0.0)
            acc = acc * jnp.exp(m - m_new) + jnp.dot(
                p.astype(jnp.bfloat16), vals, preferred_element_type=jnp.float32
            )
            return m_new, acc

        if not received:
            s_span = lax.dot_general(qj, span_keys, dims, preferred_element_type=jnp.float32)
            m, acc = update(m, acc, causal, s_span, span_vals)
        for n, get in runs:
            def body_fn(i, carry, get=get):
                keys, ok, s = scores(get, i)
                vals = jnp.where(key_lane, jnp.ones_like(keys), keys)
                return update(*carry, ok, s, vals)
            m, acc = lax.fori_loop(0, n, body_fn, (m, acc))
        total = acc[:, 0:1]
        res = acc / jnp.where(total > 0.0, total, 1.0)
        shift = (j * head_dim - head_dim) % lanes
        outs.append(res if shift == 0 else pltpu.roll(res, shift, 1))
        stats.append((m, total))
    out = outs[0]
    stat = jnp.zeros((span, lanes), jnp.float32)
    for j in range(per_group):
        if j > 0:
            out = jnp.where(lane >= j * head_dim, outs[j], out)
        m, total = stats[j]
        here = (lane >= j * head_dim) & (lane < (j + 1) * head_dim)
        first = lane < j * head_dim + head_dim // 2
        stat = jnp.where(here, jnp.where(first, m, total), stat)
    o_ref[0] = out
    st_ref[0] = stat


def attend(q_all, keys, span_kv, meta, piece, kv_count):
    local_reqs, span, width = q_all.shape
    received = span_kv is None
    if received:
        _, rounds, _, _, kv_heads, lanes = keys.shape
        k2 = keys.reshape(local_reqs, rounds, kv_count, piece, kv_heads * lanes)
        key_spec = pl.BlockSpec((1, rounds, kv_count, piece, lanes), lambda b, g, n: (b, 0, 0, 0, g))
        key_count = rounds * (kv_count - 1) * piece
        operands = (k2,)
        specs = [key_spec]
    else:
        cached, kv_heads, lanes = keys.shape[1:]
        k2 = keys.reshape(local_reqs, cached, kv_heads * lanes)
        s2 = span_kv.reshape(local_reqs, span_kv.shape[1], kv_heads * lanes)
        key_count = cached // kv_count + s2.shape[1]
        operands = (k2, s2)
        specs = [
            pl.BlockSpec((1, cached, lanes), lambda b, g, n: (b, 0, g)),
            pl.BlockSpec((1, s2.shape[1], lanes), lambda b, g, n: (b, 0, g)),
        ]
    head_dim = lanes // 2
    flops = 2 * local_reqs * kv_heads * (lanes // head_dim) * span * key_count * lanes * 3
    return pl.pallas_call(
        functools.partial(
            attend_kernel, piece=piece, kv_count=kv_count, head_dim=head_dim, received=received
        ),
        out_shape=(
            jax.ShapeDtypeStruct(q_all.shape, jnp.float32),
            jax.ShapeDtypeStruct(q_all.shape, jnp.float32),
        ),
        grid_spec=pltpu.PrefetchScalarGridSpec(
            num_scalar_prefetch=1,
            grid=(local_reqs, kv_heads),
            in_specs=[pl.BlockSpec((1, span, lanes), lambda b, g, n: (b, 0, g))] + specs,
            out_specs=(
                pl.BlockSpec((1, span, lanes), lambda b, g, n: (b, 0, g)),
                pl.BlockSpec((1, span, lanes), lambda b, g, n: (b, 0, g)),
            ),
        ),
        cost_estimate=pl.CostEstimate(
            flops=flops,
            transcendentals=local_reqs * kv_heads * 2 * span * key_count,
            bytes_accessed=2 * (q_all.size + sum(x.size for x in operands)) + 8 * q_all.size,
        ),
    )(meta, q_all, *operands)


def place_pages(page_rows, slot_numbers, slots_dev):
    owner_index = slot_numbers // slots_dev
    arrangement = jnp.argsort(owner_index, stable=True)
    return (page_rows[arrangement], (slot_numbers % slots_dev)[arrangement])


def body(
    hidden,
    queries,
    span_kv,
    cache,
    req_order,
    cached_len,
    out_weight,
    norm_gain,
    expert_ids,
    expert_weights,
    w_experts,
    block_map,
):
    local_reqs, local_tokens, width_model = hidden.shape
    row_count = local_reqs * local_tokens
    req_count = lax.axis_size(REQ)
    kv_count = lax.axis_size("kv")
    kv_heads = span_kv.shape[2]
    head_pair = span_kv.shape[3]
    group_width = queries.shape[2] // kv_heads
    group_count = kv_heads // kv_count
    slots_dev = local_reqs * block_map.shape[1]
    lengths = lookup_lengths(req_order, cached_len, local_reqs)
    kv_index = lax.axis_index("kv")
    cached_local = cache.shape[1]
    head_dim = head_pair // 2
    heads = kv_heads * (group_width // head_dim)
    full_weights = lax.all_gather(w_experts, ("zhi", "kv"), axis=0, tiled=False)
    pages_local = cached_local // BLOCK
    position = kv_index * cached_local + jnp.arange(cached_local)
    visible = position[None, :] < lengths[:, None]
    visible_cache = jnp.where(visible[:, :, None, None], cache, jnp.zeros((), jnp.bfloat16))
    page_rows = (
        visible_cache.reshape(local_reqs, pages_local, BLOCK, kv_heads, head_pair)
        .transpose(0, 1, 3, 2, 4)
        .reshape(local_reqs * pages_local, kv_heads, BLOCK, head_pair)
    )
    my_map = lax.dynamic_slice_in_dim(block_map, kv_index * pages_local, pages_local, axis=1)
    sorted_pages, local_slot = place_pages(page_rows, my_map.reshape(-1), slots_dev)
    per_owner = sorted_pages.shape[0] // req_count
    outgoing = (
        sorted_pages.reshape(req_count, per_owner, kv_count, group_count, BLOCK, head_pair)
        .transpose(0, 2, 1, 3, 4, 5)
        .reshape(req_count * kv_count, per_owner, group_count, BLOCK, head_pair)
    )
    slots_out = jnp.broadcast_to(
        local_slot.reshape(req_count, 1, per_owner), (req_count, kv_count, per_owner)
    ).reshape(req_count * kv_count, per_owner)
    everyone = (*REQ, "kv")
    arrived, where_to = (
        lax.all_to_all(outgoing, everyone, split_axis=0, concat_axis=0, tiled=True),
        lax.all_to_all(slots_out, everyone, split_axis=0, concat_axis=0, tiled=True),
    )
    piece = min(256, cached_local // kv_count)
    rounds = cached_local // (kv_count * piece)
    dealt = lax.all_to_all(
        cache.reshape(local_reqs, rounds, kv_count, piece, kv_heads, head_pair),
        "kv", split_axis=2, concat_axis=2, tiled=True,
    )
    q_all = lax.all_gather(queries, "kv", axis=1, tiled=True)
    meta = jnp.concatenate(
        [lengths, kv_index[None], jnp.full((1,), cached_local)]
    ).astype(jnp.int32)
    own_out, own_stat = attend(q_all, cache, span_kv, meta, piece, kv_count)
    got_out, got_stat = attend(q_all, dealt, None, meta, piece, kv_count)
    got_out, got_stat, arrived, where_to = lax.optimization_barrier(
        (got_out, got_stat, arrived, where_to)
    )
    span_total = q_all.shape[1]

    def split_stat(table):
        table = table.reshape(local_reqs, span_total, heads, 2, head_dim // 2)[..., 0]
        return table[..., 0], table[..., 1]

    own_max, own_sum = split_stat(own_stat)
    got_max, got_sum = split_stat(got_stat)
    top = jnp.maximum(own_max, got_max)
    own_w = own_sum * jnp.exp(own_max - top)
    got_w = got_sum * jnp.exp(got_max - top)
    both_w = own_w + got_w
    part_out = (
        (own_out.reshape(local_reqs, span_total, heads, head_dim) * own_w[..., None]
         + got_out.reshape(local_reqs, span_total, heads, head_dim) * got_w[..., None])
        / jnp.where(both_w > 0.0, both_w, 1.0)[..., None]
    ).astype(jnp.bfloat16).reshape(local_reqs, span_total, width_model)
    stat = jnp.stack([top, both_w], axis=-1)
    part_out, stat, full_weights = lax.optimization_barrier((part_out, stat, full_weights))
    got_out = lax.all_to_all(
        part_out.reshape(local_reqs, kv_count, local_tokens, width_model),
        "kv", split_axis=1, concat_axis=1, tiled=True,
    )
    got_stat = lax.all_to_all(
        stat.reshape(local_reqs, kv_count, local_tokens, heads, 2),
        "kv", split_axis=1, concat_axis=1, tiled=True,
    )
    part_max = got_stat[..., 0]
    top = jnp.max(part_max, axis=1, keepdims=True)
    part_weight = got_stat[..., 1] * jnp.exp(part_max - top)
    merged = jnp.sum(
        got_out.reshape(local_reqs, kv_count, local_tokens, heads, head_dim).astype(jnp.float32)
        * part_weight[..., None],
        axis=1,
    ) / jnp.sum(part_weight, axis=1)[..., None]
    attn = merged.astype(jnp.bfloat16).reshape(row_count, width_model)
    residual = hidden.reshape(row_count, width_model).astype(jnp.float32) + jnp.dot(
        attn, out_weight, preferred_element_type=jnp.float32
    )
    inverse_rms = lax.rsqrt(jnp.mean(residual * residual, axis=-1, keepdims=True) + 1e-05)
    normed = (residual * inverse_rms * norm_gain).astype(jnp.bfloat16)
    top_count = expert_ids.shape[1]
    exp_dev = w_experts.shape[0]
    experts = exp_dev * req_count
    capacity = min(row_count, 2 * row_count * top_count // experts)
    halves = lax.axis_size("zhi")
    side = lax.axis_size("rlow")
    match = expert_ids[:, :, None] == jnp.arange(experts, dtype=jnp.int32)[None, None, :]
    picks = jnp.sum(match.astype(jnp.int32), axis=1)
    pick_weight = jnp.sum(jnp.where(match, expert_weights[:, :, None], 0.0), axis=1)
    rank = jnp.cumsum(picks, axis=0) - 1

    def side_major(table):
        return (
            table.reshape(halves, side, exp_dev, row_count)
            .transpose(1, 0, 2, 3)
            .reshape(experts, row_count)
        )

    slot_of = side_major(jnp.where(picks > 0, rank, -1).T)
    weight_of = side_major(pick_weight.T)
    selector = slot_of[:, None, :] == jnp.arange(capacity, dtype=jnp.int32)[None, :, None]
    buffer = jnp.einsum(
        "ect,td->ecd", selector.astype(jnp.bfloat16), normed, preferred_element_type=jnp.float32
    ).astype(jnp.bfloat16)
    per_dev = halves * exp_dev
    slot_block = lax.all_to_all(
        buffer.reshape(side, per_dev * capacity, width_model), "rlow", split_axis=0, concat_axis=0, tiled=True
    )
    grouped = slot_block.reshape(side, halves, exp_dev, capacity, width_model)
    weights = full_weights.reshape(halves, kv_count, *w_experts.shape)
    gate_act = jnp.einsum(
        "szjcd,zkjdf->szjckf", grouped, weights[:, :, :, 0], preferred_element_type=jnp.float32
    )
    up_act = jnp.einsum(
        "szjcd,zkjdf->szjckf", grouped, weights[:, :, :, 1], preferred_element_type=jnp.float32
    )
    activated = (jax.nn.silu(gate_act) * up_act).astype(jnp.bfloat16)
    expert_out = jnp.einsum(
        "szjckf,zkjdf->szjcd", activated, weights[:, :, :, 2], preferred_element_type=jnp.float32
    ).astype(jnp.bfloat16)
    returned = lax.all_to_all(
        expert_out.reshape(side, per_dev * capacity, width_model), "rlow", split_axis=0, concat_axis=0, tiled=True
    )
    combine = jnp.where(selector, weight_of[:, None, :], 0.0)
    combine_hi = combine.astype(jnp.bfloat16)
    combine_lo = (combine - combine_hi.astype(jnp.float32)).astype(jnp.bfloat16)
    returned = returned.reshape(experts, capacity, width_model)
    expert_sum = jnp.einsum(
        "ect,ecd->td", combine_hi, returned, preferred_element_type=jnp.float32
    ) + jnp.einsum("ect,ecd->td", combine_lo, returned, preferred_element_type=jnp.float32)
    placement = (
        where_to.reshape(1, -1) == jnp.arange(slots_dev, dtype=jnp.int32)[:, None]
    ).astype(jnp.bfloat16)
    decode_pool = jnp.dot(
        placement,
        arrived.reshape(slots_dev, group_count * BLOCK * head_pair),
        preferred_element_type=jnp.float32,
    ).astype(jnp.bfloat16).reshape(slots_dev, group_count, BLOCK, head_pair)
    layer_out = (
        (residual + expert_sum).astype(jnp.bfloat16).reshape(local_reqs, local_tokens, width_model)
    )
    return (layer_out, decode_pool)


def solution(mesh):
    devices = mesh.devices
    req_total, kv_total = devices.shape
    split_mesh = jax.sharding.Mesh(
        devices.reshape(2, req_total // 2, kv_total), ("zhi", "rlow", "kv")
    )
    return jax.shard_map(
        body,
        mesh=split_mesh,
        in_specs=(
            P(REQ, "kv", None),
            P(REQ, "kv", None),
            P(REQ, "kv", None, None),
            P(REQ, "kv", None, None),
            P(),
            P(),
            P(),
            P(),
            P((*REQ, "kv"), None),
            P((*REQ, "kv"), None),
            P(REQ, None, None, "kv"),
            P(REQ, None),
        ),
        out_specs=(P(REQ, "kv", None), P(REQ, "kv", None, None)),
        check_vma=False,
    )
```

```python
import functools
import math

import jax
import jax.numpy as jnp
from jax import lax
from jax.experimental import pallas as pl
from jax.experimental.pallas import tpu as pltpu
from jax.sharding import PartitionSpec as P

BLOCK = 16


REQ = ("zhi", "rlow")


def lookup_lengths(req_order, cached_len, count):
    start = lax.axis_index(REQ) * count
    mine = lax.dynamic_slice_in_dim(req_order, start, count)
    match = mine[:, None] == jnp.arange(cached_len.shape[0], dtype=jnp.int32)[None, :]
    return jnp.sum(jnp.where(match, cached_len[None, :], 0), axis=1)


def attend_kernel(len_ref, q_ref, c_ref, s_ref, o_ref, *, tk, head_dim):
    b = pl.program_id(0)
    length = len_ref[b]
    span = q_ref.shape[1]
    lanes = q_ref.shape[2]
    per_group = lanes // head_dim
    scale = 1.0 / math.sqrt(head_dim)
    lane = lax.broadcasted_iota(jnp.int32, (span, lanes), 1)
    q_all = q_ref[0].astype(jnp.float32) * scale
    blocks = c_ref.shape[1] // tk
    full = length // tk
    tail = jnp.minimum(full, blocks - 1)
    row = lax.broadcasted_iota(jnp.int32, (span, span), 0)
    col = lax.broadcasted_iota(jnp.int32, (span, span), 1)
    causal = col <= row
    key_lane = lax.broadcasted_iota(jnp.int32, (tk, lanes), 1) < head_dim
    span_lane = lax.broadcasted_iota(jnp.int32, (span, lanes), 1) < head_dim
    span_keys = s_ref[0]
    span_vals = jnp.where(span_lane, jnp.ones_like(span_keys), span_keys)
    dims = (((1,), (1,)), ((), ()))
    tail_pos = tail * tk + lax.broadcasted_iota(jnp.int32, (span, tk), 1)
    tail_ok = (tail_pos >= full * tk) & (tail_pos < length)
    outs = []
    for j in range(per_group):
        shifted = q_all if j == 0 else pltpu.roll(q_all, lanes - j * head_dim, 1)
        qj = jnp.where(lane < head_dim, shifted, 0.0).astype(jnp.bfloat16)

        def block(kb):
            start = pl.multiple_of(kb * tk, tk)
            keys = c_ref[0, pl.ds(start, tk), :]
            s = lax.dot_general(qj, keys, dims, preferred_element_type=jnp.float32)
            return keys, s

        def update(m, acc, ok, s, vals):
            if ok is None:
                m_new = jnp.maximum(m, jnp.max(s, axis=1, keepdims=True))
                p = jnp.exp(s - m_new)
            else:
                m_new = jnp.maximum(m, jnp.max(jnp.where(ok, s, -1e30), axis=1, keepdims=True))
                p = jnp.where(ok, jnp.exp(s - m_new), 0.0)
            acc = acc * jnp.exp(m - m_new) + jnp.dot(
                p.astype(jnp.bfloat16), vals, preferred_element_type=jnp.float32
            )
            return m_new, acc

        def values(keys):
            return jnp.where(key_lane, jnp.ones_like(keys), keys)

        s_span = lax.dot_general(qj, span_keys, dims, preferred_element_type=jnp.float32)
        m = jnp.full((span, 1), -1e30, jnp.float32)
        acc = jnp.zeros((span, lanes), jnp.float32)
        m, acc = update(m, acc, causal, s_span, span_vals)

        def full_body(kb, carry):
            keys, s = block(kb)
            return update(*carry, None, s, values(keys))

        m, acc = lax.fori_loop(0, full, full_body, (m, acc))
        keys_tail, s_tail = block(tail)
        m, acc = update(m, acc, tail_ok, s_tail, values(keys_tail))
        total = acc[:, 0:1]
        res = acc / total
        shift = (j * head_dim - head_dim) % lanes
        outs.append(res if shift == 0 else pltpu.roll(res, shift, 1))
    out = outs[0]
    for j in range(1, per_group):
        out = jnp.where(lane >= j * head_dim, outs[j], out)
    o_ref[0] = out.astype(o_ref.dtype)


def attend(query_heads, cache_heads, span_heads, lengths):
    local_reqs, span, groups, lanes = query_heads.shape
    cached = cache_heads.shape[1]
    head_dim = cache_heads.shape[-1] // 2
    tk = 256 if cached % 256 == 0 else cached
    q2 = query_heads.reshape(local_reqs, span, groups * lanes)
    c2 = cache_heads.reshape(local_reqs, cached, groups * lanes)
    s2 = span_heads.reshape(local_reqs, span, groups * lanes)
    flops = 2 * local_reqs * groups * (lanes // head_dim) * span * (cached + span) * lanes * 3
    out = pl.pallas_call(
        functools.partial(attend_kernel, tk=tk, head_dim=head_dim),
        out_shape=jax.ShapeDtypeStruct(q2.shape, jnp.bfloat16),
        grid_spec=pltpu.PrefetchScalarGridSpec(
            num_scalar_prefetch=1,
            grid=(local_reqs, groups),
            in_specs=[
                pl.BlockSpec((1, span, lanes), lambda b, g, n: (b, 0, g)),
                pl.BlockSpec((1, cached, lanes), lambda b, g, n: (b, 0, g)),
                pl.BlockSpec((1, span, lanes), lambda b, g, n: (b, 0, g)),
            ],
            out_specs=pl.BlockSpec((1, span, lanes), lambda b, g, n: (b, 0, g)),
        ),
        cost_estimate=pl.CostEstimate(
            flops=flops,
            transcendentals=local_reqs * groups * 2 * span * (cached + span),
            bytes_accessed=2 * (2 * q2.size + c2.size + s2.size),
        ),
    )(lengths.astype(jnp.int32), q2, c2, s2)
    return out.reshape(local_reqs, span, groups, lanes)


def place_pages(page_rows, slot_numbers, slots_dev):
    owner_index = slot_numbers // slots_dev
    arrangement = jnp.argsort(owner_index, stable=True)
    return (page_rows[arrangement], (slot_numbers % slots_dev)[arrangement])


def body(
    hidden,
    queries,
    span_kv,
    cache,
    req_order,
    cached_len,
    out_weight,
    norm_gain,
    expert_ids,
    expert_weights,
    w_experts,
    block_map,
):
    local_reqs, local_tokens, width_model = hidden.shape
    row_count = local_reqs * local_tokens
    req_count = lax.axis_size(REQ)
    kv_count = lax.axis_size("kv")
    kv_heads = span_kv.shape[2]
    head_pair = span_kv.shape[3]
    group_width = queries.shape[2] // kv_heads
    group_count = kv_heads // kv_count
    slots_dev = local_reqs * block_map.shape[1]
    lengths = lookup_lengths(req_order, cached_len, local_reqs)
    queries_grouped = queries.reshape(local_reqs, local_tokens, kv_heads, group_width)
    cache_heads, span_heads, query_heads = (
        lax.all_to_all(cache, "kv", split_axis=2, concat_axis=1, tiled=True),
        lax.all_to_all(span_kv, "kv", split_axis=2, concat_axis=1, tiled=True),
        lax.all_to_all(queries_grouped, "kv", split_axis=2, concat_axis=1, tiled=True),
    )
    pair_weights = lax.all_gather(w_experts, "zhi", axis=0, tiled=False)
    pair_weights, cache_heads, block_map = lax.optimization_barrier(
        (pair_weights, cache_heads, block_map)
    )
    full_weights = lax.all_gather(pair_weights, "kv", axis=1, tiled=False)
    page_total = block_map.shape[1]
    visible = jnp.arange(cache_heads.shape[1])[None, :] < lengths[:, None]
    visible_cache = jnp.where(visible[:, :, None, None], cache_heads, jnp.zeros((), jnp.bfloat16))
    page_rows = (
        visible_cache.reshape(local_reqs, page_total, BLOCK, group_count, head_pair)
        .transpose(0, 1, 3, 2, 4)
        .reshape(local_reqs * page_total, group_count, BLOCK, head_pair)
    )
    sorted_pages, local_slot = place_pages(page_rows, block_map.reshape(-1), slots_dev)
    per_owner = sorted_pages.shape[0] // req_count
    outgoing = sorted_pages.reshape(req_count, per_owner, group_count, BLOCK, head_pair)
    arrived, where_to = (
        lax.all_to_all(outgoing, REQ, split_axis=0, concat_axis=0, tiled=True),
        lax.all_to_all(
            local_slot.reshape(req_count, per_owner), REQ, split_axis=0, concat_axis=0, tiled=True
        ),
    )
    attn_heads = attend(query_heads, cache_heads, span_heads, lengths)
    attn_heads, full_weights, arrived, where_to = lax.optimization_barrier(
        (attn_heads, full_weights, arrived, where_to)
    )
    attn = lax.all_to_all(attn_heads, "kv", split_axis=1, concat_axis=2, tiled=True).reshape(
        row_count, kv_heads * group_width
    )
    placement = (
        where_to.reshape(1, -1) == jnp.arange(slots_dev, dtype=jnp.int32)[:, None]
    ).astype(jnp.bfloat16)
    decode_pool = jnp.dot(
        placement,
        arrived.reshape(slots_dev, group_count * BLOCK * head_pair),
        preferred_element_type=jnp.float32,
    ).astype(jnp.bfloat16).reshape(slots_dev, group_count, BLOCK, head_pair)
    residual = hidden.reshape(row_count, width_model).astype(jnp.float32) + jnp.dot(
        attn, out_weight, preferred_element_type=jnp.float32
    )
    inverse_rms = lax.rsqrt(jnp.mean(residual * residual, axis=-1, keepdims=True) + 1e-05)
    normed = (residual * inverse_rms * norm_gain).astype(jnp.bfloat16)
    top_count = expert_ids.shape[1]
    exp_dev = w_experts.shape[0]
    experts = exp_dev * req_count
    capacity = min(row_count, 2 * row_count * top_count // experts)
    halves = lax.axis_size("zhi")
    side = lax.axis_size("rlow")
    match = expert_ids[:, :, None] == jnp.arange(experts, dtype=jnp.int32)[None, None, :]
    picks = jnp.sum(match.astype(jnp.int32), axis=1)
    pick_weight = jnp.sum(jnp.where(match, expert_weights[:, :, None], 0.0), axis=1)
    rank = jnp.cumsum(picks, axis=0) - 1

    def side_major(table):
        return (
            table.reshape(halves, side, exp_dev, row_count)
            .transpose(1, 0, 2, 3)
            .reshape(experts, row_count)
        )

    slot_of = side_major(jnp.where(picks > 0, rank, -1).T)
    weight_of = side_major(pick_weight.T)
    selector = slot_of[:, None, :] == jnp.arange(capacity, dtype=jnp.int32)[None, :, None]
    buffer = jnp.einsum(
        "ect,td->ecd", selector.astype(jnp.bfloat16), normed, preferred_element_type=jnp.float32
    ).astype(jnp.bfloat16)
    per_dev = halves * exp_dev
    slot_block = lax.all_to_all(
        buffer.reshape(side, per_dev * capacity, width_model), "rlow", split_axis=0, concat_axis=0, tiled=True
    )
    grouped = slot_block.reshape(side, halves, exp_dev, capacity, width_model)
    weights = full_weights.reshape(halves, kv_count, *w_experts.shape)
    gate_act = jnp.einsum(
        "szjcd,zkjdf->szjckf", grouped, weights[:, :, :, 0], preferred_element_type=jnp.float32
    )
    up_act = jnp.einsum(
        "szjcd,zkjdf->szjckf", grouped, weights[:, :, :, 1], preferred_element_type=jnp.float32
    )
    activated = (jax.nn.silu(gate_act) * up_act).astype(jnp.bfloat16)
    expert_out = jnp.einsum(
        "szjckf,zkjdf->szjcd", activated, weights[:, :, :, 2], preferred_element_type=jnp.float32
    ).astype(jnp.bfloat16)
    returned = lax.all_to_all(
        expert_out.reshape(side, per_dev * capacity, width_model), "rlow", split_axis=0, concat_axis=0, tiled=True
    )
    combine = jnp.where(selector, weight_of[:, None, :], 0.0)
    combine_hi = combine.astype(jnp.bfloat16)
    combine_lo = (combine - combine_hi.astype(jnp.float32)).astype(jnp.bfloat16)
    returned = returned.reshape(experts, capacity, width_model)
    expert_sum = jnp.einsum(
        "ect,ecd->td", combine_hi, returned, preferred_element_type=jnp.float32
    ) + jnp.einsum("ect,ecd->td", combine_lo, returned, preferred_element_type=jnp.float32)
    layer_out = (
        (residual + expert_sum).astype(jnp.bfloat16).reshape(local_reqs, local_tokens, width_model)
    )
    return (layer_out, decode_pool)


def solution(mesh):
    devices = mesh.devices
    req_total, kv_total = devices.shape
    split_mesh = jax.sharding.Mesh(
        devices.reshape(2, req_total // 2, kv_total), ("zhi", "rlow", "kv")
    )
    return jax.shard_map(
        body,
        mesh=split_mesh,
        in_specs=(
            P(REQ, "kv", None),
            P(REQ, "kv", None),
            P(REQ, "kv", None, None),
            P(REQ, "kv", None, None),
            P(),
            P(),
            P(),
            P(),
            P((*REQ, "kv"), None),
            P((*REQ, "kv"), None),
            P(REQ, None, None, "kv"),
            P(REQ, None),
        ),
        out_specs=(P(REQ, "kv", None), P(REQ, "kv", None, None)),
        check_vma=False,
    )
```

```python
import functools
import math

import jax
import jax.numpy as jnp
from jax import lax
from jax.experimental import pallas as pl
from jax.experimental.pallas import tpu as pltpu
from jax.sharding import PartitionSpec as P

BLOCK = 16


REQ = ("zhi", "rlow")


def lookup_lengths(req_order, cached_len, count):
    start = lax.axis_index(REQ) * count
    mine = lax.dynamic_slice_in_dim(req_order, start, count)
    match = mine[:, None] == jnp.arange(cached_len.shape[0], dtype=jnp.int32)[None, :]
    return jnp.sum(jnp.where(match, cached_len[None, :], 0), axis=1)


def attend_kernel(len_ref, q_ref, c_ref, s_ref, o_ref, *, tk, head_dim):
    b = pl.program_id(0)
    length = len_ref[b]
    span = q_ref.shape[1]
    lanes = q_ref.shape[2]
    per_group = lanes // head_dim
    scale = 1.0 / math.sqrt(head_dim)
    lane = lax.broadcasted_iota(jnp.int32, (span, lanes), 1)
    q_all = q_ref[0].astype(jnp.float32) * scale
    blocks = c_ref.shape[1] // tk
    full = length // tk
    tail = jnp.minimum(full, blocks - 1)
    row = lax.broadcasted_iota(jnp.int32, (span, span), 0)
    col = lax.broadcasted_iota(jnp.int32, (span, span), 1)
    causal = col <= row
    key_lane = lax.broadcasted_iota(jnp.int32, (tk, lanes), 1) < head_dim
    span_lane = lax.broadcasted_iota(jnp.int32, (span, lanes), 1) < head_dim
    span_keys = s_ref[0]
    span_vals = jnp.where(span_lane, jnp.ones_like(span_keys), span_keys)
    dims = (((1,), (1,)), ((), ()))
    tail_pos = tail * tk + lax.broadcasted_iota(jnp.int32, (span, tk), 1)
    tail_ok = (tail_pos >= full * tk) & (tail_pos < length)
    outs = []
    for j in range(per_group):
        shifted = q_all if j == 0 else pltpu.roll(q_all, lanes - j * head_dim, 1)
        qj = jnp.where(lane < head_dim, shifted, 0.0).astype(jnp.bfloat16)

        def block(kb):
            start = pl.multiple_of(kb * tk, tk)
            keys = c_ref[0, pl.ds(start, tk), :]
            s = lax.dot_general(qj, keys, dims, preferred_element_type=jnp.float32)
            return keys, s

        def update(m, acc, ok, s, vals):
            if ok is None:
                m_new = jnp.maximum(m, jnp.max(s, axis=1, keepdims=True))
                p = jnp.exp(s - m_new)
            else:
                m_new = jnp.maximum(m, jnp.max(jnp.where(ok, s, -1e30), axis=1, keepdims=True))
                p = jnp.where(ok, jnp.exp(s - m_new), 0.0)
            acc = acc * jnp.exp(m - m_new) + jnp.dot(
                p.astype(jnp.bfloat16), vals, preferred_element_type=jnp.float32
            )
            return m_new, acc

        def values(keys):
            return jnp.where(key_lane, jnp.ones_like(keys), keys)

        s_span = lax.dot_general(qj, span_keys, dims, preferred_element_type=jnp.float32)
        m = jnp.full((span, 1), -1e30, jnp.float32)
        acc = jnp.zeros((span, lanes), jnp.float32)
        m, acc = update(m, acc, causal, s_span, span_vals)

        def full_body(kb, carry):
            keys, s = block(kb)
            return update(*carry, None, s, values(keys))

        m, acc = lax.fori_loop(0, full, full_body, (m, acc))
        keys_tail, s_tail = block(tail)
        m, acc = update(m, acc, tail_ok, s_tail, values(keys_tail))
        total = acc[:, 0:1]
        res = acc / total
        shift = (j * head_dim - head_dim) % lanes
        outs.append(res if shift == 0 else pltpu.roll(res, shift, 1))
    out = outs[0]
    for j in range(1, per_group):
        out = jnp.where(lane >= j * head_dim, outs[j], out)
    o_ref[0] = out.astype(o_ref.dtype)


def attend(query_heads, cache_heads, span_heads, lengths):
    local_reqs, span, groups, lanes = query_heads.shape
    cached = cache_heads.shape[1]
    head_dim = cache_heads.shape[-1] // 2
    tk = 256 if cached % 256 == 0 else cached
    q2 = query_heads.reshape(local_reqs, span, groups * lanes)
    c2 = cache_heads.reshape(local_reqs, cached, groups * lanes)
    s2 = span_heads.reshape(local_reqs, span, groups * lanes)
    flops = 2 * local_reqs * groups * (lanes // head_dim) * span * (cached + span) * lanes * 3
    out = pl.pallas_call(
        functools.partial(attend_kernel, tk=tk, head_dim=head_dim),
        out_shape=jax.ShapeDtypeStruct(q2.shape, jnp.bfloat16),
        grid_spec=pltpu.PrefetchScalarGridSpec(
            num_scalar_prefetch=1,
            grid=(local_reqs, groups),
            in_specs=[
                pl.BlockSpec((1, span, lanes), lambda b, g, n: (b, 0, g)),
                pl.BlockSpec((1, cached, lanes), lambda b, g, n: (b, 0, g)),
                pl.BlockSpec((1, span, lanes), lambda b, g, n: (b, 0, g)),
            ],
            out_specs=pl.BlockSpec((1, span, lanes), lambda b, g, n: (b, 0, g)),
        ),
        cost_estimate=pl.CostEstimate(
            flops=flops,
            transcendentals=local_reqs * groups * 2 * span * (cached + span),
            bytes_accessed=2 * (2 * q2.size + c2.size + s2.size),
        ),
    )(lengths.astype(jnp.int32), q2, c2, s2)
    return out.reshape(local_reqs, span, groups, lanes)


def place_pages(page_rows, slot_numbers, slots_dev):
    owner_index = slot_numbers // slots_dev
    arrangement = jnp.argsort(owner_index, stable=True)
    return (page_rows[arrangement], (slot_numbers % slots_dev)[arrangement])


def body(
    hidden,
    queries,
    span_kv,
    cache,
    req_order,
    cached_len,
    out_weight,
    norm_gain,
    expert_ids,
    expert_weights,
    w_experts,
    block_map,
):
    local_reqs, local_tokens, width_model = hidden.shape
    row_count = local_reqs * local_tokens
    req_count = lax.axis_size(REQ)
    kv_count = lax.axis_size("kv")
    kv_heads = span_kv.shape[2]
    head_pair = span_kv.shape[3]
    group_width = queries.shape[2] // kv_heads
    group_count = kv_heads // kv_count
    slots_dev = local_reqs * block_map.shape[1]
    lengths = lookup_lengths(req_order, cached_len, local_reqs)
    queries_grouped = queries.reshape(local_reqs, local_tokens, kv_heads, group_width)
    cache_heads, span_heads, query_heads = (
        lax.all_to_all(cache, "kv", split_axis=2, concat_axis=1, tiled=True),
        lax.all_to_all(span_kv, "kv", split_axis=2, concat_axis=1, tiled=True),
        lax.all_to_all(queries_grouped, "kv", split_axis=2, concat_axis=1, tiled=True),
    )
    pair_weights = lax.all_gather(w_experts, "zhi", axis=0, tiled=False)
    pair_weights, cache_heads, block_map = lax.optimization_barrier(
        (pair_weights, cache_heads, block_map)
    )
    full_weights = lax.all_gather(pair_weights, "kv", axis=1, tiled=False)
    page_total = block_map.shape[1]
    visible = jnp.arange(cache_heads.shape[1])[None, :] < lengths[:, None]
    visible_cache = jnp.where(visible[:, :, None, None], cache_heads, jnp.zeros((), jnp.bfloat16))
    page_rows = (
        visible_cache.reshape(local_reqs, page_total, BLOCK, group_count, head_pair)
        .transpose(0, 1, 3, 2, 4)
        .reshape(local_reqs * page_total, group_count, BLOCK, head_pair)
    )
    sorted_pages, local_slot = place_pages(page_rows, block_map.reshape(-1), slots_dev)
    per_owner = sorted_pages.shape[0] // req_count
    outgoing = sorted_pages.reshape(req_count, per_owner, group_count, BLOCK, head_pair)
    arrived, where_to = (
        lax.all_to_all(outgoing, REQ, split_axis=0, concat_axis=0, tiled=True),
        lax.all_to_all(
            local_slot.reshape(req_count, per_owner), REQ, split_axis=0, concat_axis=0, tiled=True
        ),
    )
    attn_heads = attend(query_heads, cache_heads, span_heads, lengths)
    attn_heads, arrived, where_to = lax.optimization_barrier((attn_heads, arrived, where_to))
    attn = lax.all_to_all(attn_heads, "kv", split_axis=1, concat_axis=2, tiled=True).reshape(
        row_count, kv_heads * group_width
    )
    placement = (
        where_to.reshape(1, -1) == jnp.arange(slots_dev, dtype=jnp.int32)[:, None]
    ).astype(jnp.bfloat16)
    decode_pool = jnp.dot(
        placement,
        arrived.reshape(slots_dev, group_count * BLOCK * head_pair),
        preferred_element_type=jnp.float32,
    ).astype(jnp.bfloat16).reshape(slots_dev, group_count, BLOCK, head_pair)
    residual = hidden.reshape(row_count, width_model).astype(jnp.float32) + jnp.dot(
        attn, out_weight, preferred_element_type=jnp.float32
    )
    inverse_rms = lax.rsqrt(jnp.mean(residual * residual, axis=-1, keepdims=True) + 1e-05)
    normed = (residual * inverse_rms * norm_gain).astype(jnp.bfloat16)
    top_count = expert_ids.shape[1]
    exp_dev = w_experts.shape[0]
    experts = exp_dev * req_count
    capacity = min(row_count, 2 * row_count * top_count // experts)
    halves = lax.axis_size("zhi")
    side = lax.axis_size("rlow")
    match = expert_ids[:, :, None] == jnp.arange(experts, dtype=jnp.int32)[None, None, :]
    picks = jnp.sum(match.astype(jnp.int32), axis=1)
    pick_weight = jnp.sum(jnp.where(match, expert_weights[:, :, None], 0.0), axis=1)
    rank = jnp.cumsum(picks, axis=0) - 1

    def side_major(table):
        return (
            table.reshape(halves, side, exp_dev, row_count)
            .transpose(1, 0, 2, 3)
            .reshape(experts, row_count)
        )

    slot_of = side_major(jnp.where(picks > 0, rank, -1).T)
    weight_of = side_major(pick_weight.T)
    selector = slot_of[:, None, :] == jnp.arange(capacity, dtype=jnp.int32)[None, :, None]
    buffer = jnp.einsum(
        "ect,td->ecd", selector.astype(jnp.bfloat16), normed, preferred_element_type=jnp.float32
    ).astype(jnp.bfloat16)
    per_dev = halves * exp_dev
    slot_block = lax.all_to_all(
        buffer.reshape(side, per_dev * capacity, width_model), "rlow", split_axis=0, concat_axis=0, tiled=True
    )
    grouped = slot_block.reshape(side, halves, exp_dev, capacity, width_model)
    weights = full_weights.reshape(halves, kv_count, *w_experts.shape)
    gate_act = jnp.einsum(
        "szjcd,zkjdf->szjckf", grouped, weights[:, :, :, 0], preferred_element_type=jnp.float32
    )
    up_act = jnp.einsum(
        "szjcd,zkjdf->szjckf", grouped, weights[:, :, :, 1], preferred_element_type=jnp.float32
    )
    activated = (jax.nn.silu(gate_act) * up_act).astype(jnp.bfloat16)
    expert_out = jnp.einsum(
        "szjckf,zkjdf->szjcd", activated, weights[:, :, :, 2], preferred_element_type=jnp.float32
    ).astype(jnp.bfloat16)
    returned = lax.all_to_all(
        expert_out.reshape(side, per_dev * capacity, width_model), "rlow", split_axis=0, concat_axis=0, tiled=True
    )
    combine = jnp.where(selector, weight_of[:, None, :], 0.0)
    combine_hi = combine.astype(jnp.bfloat16)
    combine_lo = (combine - combine_hi.astype(jnp.float32)).astype(jnp.bfloat16)
    returned = returned.reshape(experts, capacity, width_model)
    expert_sum = jnp.einsum(
        "ect,ecd->td", combine_hi, returned, preferred_element_type=jnp.float32
    ) + jnp.einsum("ect,ecd->td", combine_lo, returned, preferred_element_type=jnp.float32)
    layer_out = (
        (residual + expert_sum).astype(jnp.bfloat16).reshape(local_reqs, local_tokens, width_model)
    )
    return (layer_out, decode_pool)


def solution(mesh):
    devices = mesh.devices
    req_total, kv_total = devices.shape
    split_mesh = jax.sharding.Mesh(
        devices.reshape(2, req_total // 2, kv_total), ("zhi", "rlow", "kv")
    )
    return jax.shard_map(
        body,
        mesh=split_mesh,
        in_specs=(
            P(REQ, "kv", None),
            P(REQ, "kv", None),
            P(REQ, "kv", None, None),
            P(REQ, "kv", None, None),
            P(),
            P(),
            P(),
            P(),
            P((*REQ, "kv"), None),
            P((*REQ, "kv"), None),
            P(REQ, None, None, "kv"),
            P(REQ, None),
        ),
        out_specs=(P(REQ, "kv", None), P(REQ, "kv", None, None)),
        check_vma=False,
    )
```

```python
import functools
import math

import jax
import jax.numpy as jnp
from jax import lax
from jax.experimental import pallas as pl
from jax.experimental.pallas import tpu as pltpu
from jax.sharding import PartitionSpec as P

BLOCK = 16


REQ = ("zhi", "rlow")


def lookup_lengths(req_order, cached_len, count):
    start = lax.axis_index(REQ) * count
    mine = lax.dynamic_slice_in_dim(req_order, start, count)
    match = mine[:, None] == jnp.arange(cached_len.shape[0], dtype=jnp.int32)[None, :]
    return jnp.sum(jnp.where(match, cached_len[None, :], 0), axis=1)


def attend_kernel(len_ref, q_ref, c_ref, s_ref, o_ref, *, tk, head_dim):
    b = pl.program_id(0)
    length = len_ref[b]
    span = q_ref.shape[1]
    lanes = q_ref.shape[2]
    per_group = lanes // head_dim
    scale = 1.0 / math.sqrt(head_dim)
    lane = lax.broadcasted_iota(jnp.int32, (span, lanes), 1)
    q_all = q_ref[0].astype(jnp.float32) * scale
    blocks = c_ref.shape[1] // tk
    full = length // tk
    tail = jnp.minimum(full, blocks - 1)
    row = lax.broadcasted_iota(jnp.int32, (span, span), 0)
    col = lax.broadcasted_iota(jnp.int32, (span, span), 1)
    causal = col <= row
    key_lane = lax.broadcasted_iota(jnp.int32, (tk, lanes), 1) < head_dim
    span_lane = lax.broadcasted_iota(jnp.int32, (span, lanes), 1) < head_dim
    span_keys = s_ref[0]
    span_vals = jnp.where(span_lane, jnp.ones_like(span_keys), span_keys)
    dims = (((1,), (1,)), ((), ()))
    tail_pos = tail * tk + lax.broadcasted_iota(jnp.int32, (span, tk), 1)
    tail_ok = (tail_pos >= full * tk) & (tail_pos < length)
    outs = []
    for j in range(per_group):
        shifted = q_all if j == 0 else pltpu.roll(q_all, lanes - j * head_dim, 1)
        qj = jnp.where(lane < head_dim, shifted, 0.0).astype(jnp.bfloat16)

        def block(kb):
            start = pl.multiple_of(kb * tk, tk)
            keys = c_ref[0, pl.ds(start, tk), :]
            s = lax.dot_general(qj, keys, dims, preferred_element_type=jnp.float32)
            return keys, s

        def update(m, acc, ok, s, vals):
            if ok is None:
                m_new = jnp.maximum(m, jnp.max(s, axis=1, keepdims=True))
                p = jnp.exp(s - m_new)
            else:
                m_new = jnp.maximum(m, jnp.max(jnp.where(ok, s, -1e30), axis=1, keepdims=True))
                p = jnp.where(ok, jnp.exp(s - m_new), 0.0)
            acc = acc * jnp.exp(m - m_new) + jnp.dot(
                p.astype(jnp.bfloat16), vals, preferred_element_type=jnp.float32
            )
            return m_new, acc

        def values(keys):
            return jnp.where(key_lane, jnp.ones_like(keys), keys)

        s_span = lax.dot_general(qj, span_keys, dims, preferred_element_type=jnp.float32)
        m = jnp.full((span, 1), -1e30, jnp.float32)
        acc = jnp.zeros((span, lanes), jnp.float32)
        m, acc = update(m, acc, causal, s_span, span_vals)

        def full_body(kb, carry):
            keys, s = block(kb)
            return update(*carry, None, s, values(keys))

        m, acc = lax.fori_loop(0, full, full_body, (m, acc))
        keys_tail, s_tail = block(tail)
        m, acc = update(m, acc, tail_ok, s_tail, values(keys_tail))
        total = acc[:, 0:1]
        res = acc / total
        shift = (j * head_dim - head_dim) % lanes
        outs.append(res if shift == 0 else pltpu.roll(res, shift, 1))
    out = outs[0]
    for j in range(1, per_group):
        out = jnp.where(lane >= j * head_dim, outs[j], out)
    o_ref[0] = out.astype(o_ref.dtype)


def attend(query_heads, cache_heads, span_heads, lengths):
    local_reqs, span, groups, lanes = query_heads.shape
    cached = cache_heads.shape[1]
    head_dim = cache_heads.shape[-1] // 2
    tk = 256 if cached % 256 == 0 else cached
    q2 = query_heads.reshape(local_reqs, span, groups * lanes)
    c2 = cache_heads.reshape(local_reqs, cached, groups * lanes)
    s2 = span_heads.reshape(local_reqs, span, groups * lanes)
    flops = 2 * local_reqs * groups * (lanes // head_dim) * span * (cached + span) * lanes * 3
    out = pl.pallas_call(
        functools.partial(attend_kernel, tk=tk, head_dim=head_dim),
        out_shape=jax.ShapeDtypeStruct(q2.shape, jnp.bfloat16),
        grid_spec=pltpu.PrefetchScalarGridSpec(
            num_scalar_prefetch=1,
            grid=(local_reqs, groups),
            in_specs=[
                pl.BlockSpec((1, span, lanes), lambda b, g, n: (b, 0, g)),
                pl.BlockSpec((1, cached, lanes), lambda b, g, n: (b, 0, g)),
                pl.BlockSpec((1, span, lanes), lambda b, g, n: (b, 0, g)),
            ],
            out_specs=pl.BlockSpec((1, span, lanes), lambda b, g, n: (b, 0, g)),
        ),
        cost_estimate=pl.CostEstimate(
            flops=flops,
            transcendentals=local_reqs * groups * 2 * span * (cached + span),
            bytes_accessed=2 * (2 * q2.size + c2.size + s2.size),
        ),
    )(lengths.astype(jnp.int32), q2, c2, s2)
    return out.reshape(local_reqs, span, groups, lanes)


def place_pages(page_rows, slot_numbers, slots_dev):
    owner_index = slot_numbers // slots_dev
    arrangement = jnp.argsort(owner_index, stable=True)
    return (page_rows[arrangement], (slot_numbers % slots_dev)[arrangement])


def body(
    hidden,
    queries,
    span_kv,
    cache,
    req_order,
    cached_len,
    out_weight,
    norm_gain,
    expert_ids,
    expert_weights,
    w_experts,
    block_map,
):
    local_reqs, local_tokens, width_model = hidden.shape
    row_count = local_reqs * local_tokens
    req_count = lax.axis_size(REQ)
    kv_count = lax.axis_size("kv")
    kv_heads = span_kv.shape[2]
    head_pair = span_kv.shape[3]
    group_width = queries.shape[2] // kv_heads
    group_count = kv_heads // kv_count
    slots_dev = local_reqs * block_map.shape[1]
    lengths = lookup_lengths(req_order, cached_len, local_reqs)
    queries_grouped = queries.reshape(local_reqs, local_tokens, kv_heads, group_width)
    cache_heads, span_heads, query_heads = (
        lax.all_to_all(cache, "kv", split_axis=2, concat_axis=1, tiled=True),
        lax.all_to_all(span_kv, "kv", split_axis=2, concat_axis=1, tiled=True),
        lax.all_to_all(queries_grouped, "kv", split_axis=2, concat_axis=1, tiled=True),
    )
    pair_weights = lax.all_gather(w_experts, "zhi", axis=0, tiled=False)
    pair_weights, cache_heads, block_map = lax.optimization_barrier(
        (pair_weights, cache_heads, block_map)
    )
    full_weights = lax.all_gather(pair_weights, "kv", axis=1, tiled=False)
    page_total = block_map.shape[1]
    visible = jnp.arange(cache_heads.shape[1])[None, :] < lengths[:, None]
    visible_cache = jnp.where(visible[:, :, None, None], cache_heads, jnp.zeros((), jnp.bfloat16))
    page_rows = (
        visible_cache.reshape(local_reqs, page_total, BLOCK, group_count, head_pair)
        .transpose(0, 1, 3, 2, 4)
        .reshape(local_reqs * page_total, group_count, BLOCK, head_pair)
    )
    sorted_pages, local_slot = place_pages(page_rows, block_map.reshape(-1), slots_dev)
    per_owner = sorted_pages.shape[0] // req_count
    outgoing = sorted_pages.reshape(req_count, per_owner, group_count, BLOCK, head_pair)
    arrived, where_to = (
        lax.all_to_all(outgoing, REQ, split_axis=0, concat_axis=0, tiled=True),
        lax.all_to_all(
            local_slot.reshape(req_count, per_owner), REQ, split_axis=0, concat_axis=0, tiled=True
        ),
    )
    attn_heads = attend(query_heads, cache_heads, span_heads, lengths)
    attn_heads, full_weights, arrived, where_to = lax.optimization_barrier(
        (attn_heads, full_weights, arrived, where_to)
    )
    attn = lax.all_to_all(attn_heads, "kv", split_axis=1, concat_axis=2, tiled=True).reshape(
        row_count, kv_heads * group_width
    )
    placement = (
        where_to.reshape(1, -1) == jnp.arange(slots_dev, dtype=jnp.int32)[:, None]
    ).astype(jnp.bfloat16)
    decode_pool = jnp.dot(
        placement,
        arrived.reshape(slots_dev, group_count * BLOCK * head_pair),
        preferred_element_type=jnp.float32,
    ).astype(jnp.bfloat16).reshape(slots_dev, group_count, BLOCK, head_pair)
    residual = hidden.reshape(row_count, width_model).astype(jnp.float32) + jnp.dot(
        attn, out_weight, preferred_element_type=jnp.float32
    )
    inverse_rms = lax.rsqrt(jnp.mean(residual * residual, axis=-1, keepdims=True) + 1e-05)
    normed = (residual * inverse_rms * norm_gain).astype(jnp.bfloat16)
    top_count = expert_ids.shape[1]
    exp_dev = w_experts.shape[0]
    experts = exp_dev * req_count
    capacity = min(row_count, 2 * row_count * top_count // experts)
    halves = lax.axis_size("zhi")
    side = lax.axis_size("rlow")
    match = expert_ids[:, :, None] == jnp.arange(experts, dtype=jnp.int32)[None, None, :]
    picks = jnp.sum(match.astype(jnp.int32), axis=1)
    pick_weight = jnp.sum(jnp.where(match, expert_weights[:, :, None], 0.0), axis=1)
    rank = jnp.cumsum(picks, axis=0) - 1

    def side_major(table):
        return (
            table.reshape(halves, side, exp_dev, row_count)
            .transpose(1, 0, 2, 3)
            .reshape(experts, row_count)
        )

    slot_of = side_major(jnp.where(picks > 0, rank, -1).T)
    weight_of = side_major(pick_weight.T)
    selector = slot_of[:, None, :] == jnp.arange(capacity, dtype=jnp.int32)[None, :, None]
    per_dev = halves * exp_dev
    weights = full_weights.reshape(halves, kv_count, *w_experts.shape)
    combine = jnp.where(selector, weight_of[:, None, :], 0.0)
    combine_hi = combine.astype(jnp.bfloat16)
    combine_lo = (combine - combine_hi.astype(jnp.float32)).astype(jnp.bfloat16)
    chunks = 2 if capacity % 16 == 0 else 1
    size = capacity // chunks
    expert_sum = jnp.zeros((row_count, width_model), jnp.float32)
    for chunk in range(chunks):
        rows = slice(chunk * size, (chunk + 1) * size)
        buffer = jnp.einsum(
            "ect,td->ecd", selector[:, rows].astype(jnp.bfloat16), normed,
            preferred_element_type=jnp.float32,
        ).astype(jnp.bfloat16)
        slot_block = lax.all_to_all(
            buffer.reshape(side, per_dev * size, width_model), "rlow", split_axis=0, concat_axis=0, tiled=True
        )
        grouped = slot_block.reshape(side, halves, exp_dev, size, width_model)
        gate_act = jnp.einsum(
            "szjcd,zkjdf->szjckf", grouped, weights[:, :, :, 0], preferred_element_type=jnp.float32
        )
        up_act = jnp.einsum(
            "szjcd,zkjdf->szjckf", grouped, weights[:, :, :, 1], preferred_element_type=jnp.float32
        )
        activated = (jax.nn.silu(gate_act) * up_act).astype(jnp.bfloat16)
        expert_out = jnp.einsum(
            "szjckf,zkjdf->szjcd", activated, weights[:, :, :, 2], preferred_element_type=jnp.float32
        ).astype(jnp.bfloat16)
        returned = lax.all_to_all(
            expert_out.reshape(side, per_dev * size, width_model), "rlow", split_axis=0, concat_axis=0, tiled=True
        ).reshape(experts, size, width_model)
        expert_sum = expert_sum + jnp.einsum(
            "ect,ecd->td", combine_hi[:, rows], returned, preferred_element_type=jnp.float32
        ) + jnp.einsum("ect,ecd->td", combine_lo[:, rows], returned, preferred_element_type=jnp.float32)
    layer_out = (
        (residual + expert_sum).astype(jnp.bfloat16).reshape(local_reqs, local_tokens, width_model)
    )
    return (layer_out, decode_pool)


def solution(mesh):
    devices = mesh.devices
    req_total, kv_total = devices.shape
    split_mesh = jax.sharding.Mesh(
        devices.reshape(2, req_total // 2, kv_total), ("zhi", "rlow", "kv")
    )
    return jax.shard_map(
        body,
        mesh=split_mesh,
        in_specs=(
            P(REQ, "kv", None),
            P(REQ, "kv", None),
            P(REQ, "kv", None, None),
            P(REQ, "kv", None, None),
            P(),
            P(),
            P(),
            P(),
            P((*REQ, "kv"), None),
            P((*REQ, "kv"), None),
            P(REQ, None, None, "kv"),
            P(REQ, None),
        ),
        out_specs=(P(REQ, "kv", None), P(REQ, "kv", None, None)),
        check_vma=False,
    )
```

```python
import functools
import math

import jax
import jax.numpy as jnp
from jax import lax
from jax.experimental import pallas as pl
from jax.experimental.pallas import tpu as pltpu
from jax.sharding import PartitionSpec as P

BLOCK = 16


REQ = ("zhi", "rlow")


def lookup_lengths(req_order, cached_len, count):
    start = lax.axis_index(REQ) * count
    mine = lax.dynamic_slice_in_dim(req_order, start, count)
    match = mine[:, None] == jnp.arange(cached_len.shape[0], dtype=jnp.int32)[None, :]
    return jnp.sum(jnp.where(match, cached_len[None, :], 0), axis=1)


def attend_kernel(len_ref, q_ref, c_ref, s_ref, o_ref, *, tk, head_dim):
    b = pl.program_id(0)
    length = len_ref[b]
    span = q_ref.shape[1]
    lanes = q_ref.shape[2]
    per_group = lanes // head_dim
    scale = 1.0 / math.sqrt(head_dim)
    lane = lax.broadcasted_iota(jnp.int32, (span, lanes), 1)
    q_all = q_ref[0].astype(jnp.float32) * scale
    blocks = c_ref.shape[1] // tk
    full = length // tk
    tail = jnp.minimum(full, blocks - 1)
    row = lax.broadcasted_iota(jnp.int32, (span, span), 0)
    col = lax.broadcasted_iota(jnp.int32, (span, span), 1)
    causal = col <= row
    key_lane = lax.broadcasted_iota(jnp.int32, (tk, lanes), 1) < head_dim
    span_lane = lax.broadcasted_iota(jnp.int32, (span, lanes), 1) < head_dim
    span_keys = s_ref[0]
    span_vals = jnp.where(span_lane, jnp.ones_like(span_keys), span_keys)
    dims = (((1,), (1,)), ((), ()))
    tail_pos = tail * tk + lax.broadcasted_iota(jnp.int32, (span, tk), 1)
    tail_ok = (tail_pos >= full * tk) & (tail_pos < length)
    outs = []
    for j in range(per_group):
        shifted = q_all if j == 0 else pltpu.roll(q_all, lanes - j * head_dim, 1)
        qj = jnp.where(lane < head_dim, shifted, 0.0).astype(jnp.bfloat16)

        def block(kb):
            start = pl.multiple_of(kb * tk, tk)
            keys = c_ref[0, pl.ds(start, tk), :]
            s = lax.dot_general(qj, keys, dims, preferred_element_type=jnp.float32)
            return keys, s

        def update(m, acc, ok, s, vals):
            if ok is None:
                m_new = jnp.maximum(m, jnp.max(s, axis=1, keepdims=True))
                p = jnp.exp(s - m_new)
            else:
                m_new = jnp.maximum(m, jnp.max(jnp.where(ok, s, -1e30), axis=1, keepdims=True))
                p = jnp.where(ok, jnp.exp(s - m_new), 0.0)
            acc = acc * jnp.exp(m - m_new) + jnp.dot(
                p.astype(jnp.bfloat16), vals, preferred_element_type=jnp.float32
            )
            return m_new, acc

        def values(keys):
            return jnp.where(key_lane, jnp.ones_like(keys), keys)

        s_span = lax.dot_general(qj, span_keys, dims, preferred_element_type=jnp.float32)
        m = jnp.full((span, 1), -1e30, jnp.float32)
        acc = jnp.zeros((span, lanes), jnp.float32)
        m, acc = update(m, acc, causal, s_span, span_vals)

        def full_body(kb, carry):
            keys, s = block(kb)
            return update(*carry, None, s, values(keys))

        m, acc = lax.fori_loop(0, full, full_body, (m, acc))
        keys_tail, s_tail = block(tail)
        m, acc = update(m, acc, tail_ok, s_tail, values(keys_tail))
        total = acc[:, 0:1]
        res = acc / total
        shift = (j * head_dim - head_dim) % lanes
        outs.append(res if shift == 0 else pltpu.roll(res, shift, 1))
    out = outs[0]
    for j in range(1, per_group):
        out = jnp.where(lane >= j * head_dim, outs[j], out)
    o_ref[0] = out.astype(o_ref.dtype)


def attend(query_heads, cache_heads, span_heads, lengths):
    local_reqs, span, groups, lanes = query_heads.shape
    cached = cache_heads.shape[1]
    head_dim = cache_heads.shape[-1] // 2
    tk = 256 if cached % 256 == 0 else cached
    q2 = query_heads.reshape(local_reqs, span, groups * lanes)
    c2 = cache_heads.reshape(local_reqs, cached, groups * lanes)
    s2 = span_heads.reshape(local_reqs, span, groups * lanes)
    flops = 2 * local_reqs * groups * (lanes // head_dim) * span * (cached + span) * lanes * 3
    out = pl.pallas_call(
        functools.partial(attend_kernel, tk=tk, head_dim=head_dim),
        out_shape=jax.ShapeDtypeStruct(q2.shape, jnp.bfloat16),
        grid_spec=pltpu.PrefetchScalarGridSpec(
            num_scalar_prefetch=1,
            grid=(local_reqs, groups),
            in_specs=[
                pl.BlockSpec((1, span, lanes), lambda b, g, n: (b, 0, g)),
                pl.BlockSpec((1, cached, lanes), lambda b, g, n: (b, 0, g)),
                pl.BlockSpec((1, span, lanes), lambda b, g, n: (b, 0, g)),
            ],
            out_specs=pl.BlockSpec((1, span, lanes), lambda b, g, n: (b, 0, g)),
        ),
        cost_estimate=pl.CostEstimate(
            flops=flops,
            transcendentals=local_reqs * groups * 2 * span * (cached + span),
            bytes_accessed=2 * (2 * q2.size + c2.size + s2.size),
        ),
    )(lengths.astype(jnp.int32), q2, c2, s2)
    return out.reshape(local_reqs, span, groups, lanes)


def place_pages(page_rows, slot_numbers, slots_dev):
    owner_index = slot_numbers // slots_dev
    arrangement = jnp.argsort(owner_index, stable=True)
    return (page_rows[arrangement], (slot_numbers % slots_dev)[arrangement])


def body(
    hidden,
    queries,
    span_kv,
    cache,
    req_order,
    cached_len,
    out_weight,
    norm_gain,
    expert_ids,
    expert_weights,
    w_experts,
    block_map,
):
    local_reqs, local_tokens, width_model = hidden.shape
    row_count = local_reqs * local_tokens
    req_count = lax.axis_size(REQ)
    kv_count = lax.axis_size("kv")
    kv_heads = span_kv.shape[2]
    head_pair = span_kv.shape[3]
    group_width = queries.shape[2] // kv_heads
    group_count = kv_heads // kv_count
    slots_dev = local_reqs * block_map.shape[1]
    lengths = lookup_lengths(req_order, cached_len, local_reqs)
    queries_grouped = queries.reshape(local_reqs, local_tokens, kv_heads, group_width)
    cache_heads, span_heads, query_heads = (
        lax.all_to_all(cache, "kv", split_axis=2, concat_axis=1, tiled=True),
        lax.all_to_all(span_kv, "kv", split_axis=2, concat_axis=1, tiled=True),
        lax.all_to_all(queries_grouped, "kv", split_axis=2, concat_axis=1, tiled=True),
    )
    pair_weights = lax.all_gather(w_experts, "zhi", axis=0, tiled=False)
    pair_weights, cache_heads, block_map = lax.optimization_barrier(
        (pair_weights, cache_heads, block_map)
    )
    full_weights = lax.all_gather(pair_weights, "kv", axis=1, tiled=False)
    page_total = block_map.shape[1]
    visible = jnp.arange(cache_heads.shape[1])[None, :] < lengths[:, None]
    visible_cache = jnp.where(visible[:, :, None, None], cache_heads, jnp.zeros((), jnp.bfloat16))
    page_rows = (
        visible_cache.reshape(local_reqs, page_total, BLOCK, group_count, head_pair)
        .transpose(0, 1, 3, 2, 4)
        .reshape(local_reqs * page_total, group_count, BLOCK, head_pair)
    )
    sorted_pages, local_slot = place_pages(page_rows, block_map.reshape(-1), slots_dev)
    per_owner = sorted_pages.shape[0] // req_count
    outgoing = sorted_pages.reshape(req_count, per_owner, group_count, BLOCK, head_pair)
    arrived, where_to = (
        lax.all_to_all(outgoing, REQ, split_axis=0, concat_axis=0, tiled=True),
        lax.all_to_all(
            local_slot.reshape(req_count, per_owner), REQ, split_axis=0, concat_axis=0, tiled=True
        ),
    )
    attn_heads = attend(query_heads, cache_heads, span_heads, lengths)
    attn_heads, full_weights, arrived, where_to = lax.optimization_barrier(
        (attn_heads, full_weights, arrived, where_to)
    )
    attn = lax.all_to_all(attn_heads, "kv", split_axis=1, concat_axis=2, tiled=True).reshape(
        row_count, kv_heads * group_width
    )
    placement = (
        where_to.reshape(1, -1) == jnp.arange(slots_dev, dtype=jnp.int32)[:, None]
    ).astype(jnp.bfloat16)
    decode_pool = jnp.dot(
        placement,
        arrived.reshape(slots_dev, group_count * BLOCK * head_pair),
        preferred_element_type=jnp.float32,
    ).astype(jnp.bfloat16).reshape(slots_dev, group_count, BLOCK, head_pair)
    residual = hidden.reshape(row_count, width_model).astype(jnp.float32) + jnp.dot(
        attn, out_weight, preferred_element_type=jnp.float32
    )
    inverse_rms = lax.rsqrt(jnp.mean(residual * residual, axis=-1, keepdims=True) + 1e-05)
    normed = (residual * inverse_rms * norm_gain).astype(jnp.bfloat16)
    top_count = expert_ids.shape[1]
    exp_dev = w_experts.shape[0]
    experts = exp_dev * req_count
    capacity = min(row_count, 2 * row_count * top_count // experts)
    halves = lax.axis_size("zhi")
    side = lax.axis_size("rlow")
    match = expert_ids[:, :, None] == jnp.arange(experts, dtype=jnp.int32)[None, None, :]
    picks = jnp.sum(match.astype(jnp.int32), axis=1)
    pick_weight = jnp.sum(jnp.where(match, expert_weights[:, :, None], 0.0), axis=1)
    rank = jnp.cumsum(picks, axis=0) - 1

    def side_major(table):
        return (
            table.reshape(halves, side, exp_dev, row_count)
            .transpose(1, 0, 2, 3)
            .reshape(experts, row_count)
        )

    slot_of = side_major(jnp.where(picks > 0, rank, -1).T)
    weight_of = side_major(pick_weight.T)
    selector = slot_of[:, None, :] == jnp.arange(capacity, dtype=jnp.int32)[None, :, None]
    per_dev = halves * exp_dev
    weights = full_weights.reshape(halves, kv_count, *w_experts.shape)
    combine = jnp.where(selector, weight_of[:, None, :], 0.0)
    combine_hi = combine.astype(jnp.bfloat16)
    combine_lo = (combine - combine_hi.astype(jnp.float32)).astype(jnp.bfloat16)
    chunks = 4 if capacity % 32 == 0 else 1
    size = capacity // chunks
    expert_sum = jnp.zeros((row_count, width_model), jnp.float32)
    for chunk in range(chunks):
        rows = slice(chunk * size, (chunk + 1) * size)
        buffer = jnp.einsum(
            "ect,td->ecd", selector[:, rows].astype(jnp.bfloat16), normed,
            preferred_element_type=jnp.float32,
        ).astype(jnp.bfloat16)
        slot_block = lax.all_to_all(
            buffer.reshape(side, per_dev * size, width_model), "rlow", split_axis=0, concat_axis=0, tiled=True
        )
        grouped = slot_block.reshape(side, halves, exp_dev, size, width_model)
        gate_act = jnp.einsum(
            "szjcd,zkjdf->szjckf", grouped, weights[:, :, :, 0], preferred_element_type=jnp.float32
        )
        up_act = jnp.einsum(
            "szjcd,zkjdf->szjckf", grouped, weights[:, :, :, 1], preferred_element_type=jnp.float32
        )
        activated = (jax.nn.silu(gate_act) * up_act).astype(jnp.bfloat16)
        expert_out = jnp.einsum(
            "szjckf,zkjdf->szjcd", activated, weights[:, :, :, 2], preferred_element_type=jnp.float32
        ).astype(jnp.bfloat16)
        returned = lax.all_to_all(
            expert_out.reshape(side, per_dev * size, width_model), "rlow", split_axis=0, concat_axis=0, tiled=True
        ).reshape(experts, size, width_model)
        expert_sum = expert_sum + jnp.einsum(
            "ect,ecd->td", combine_hi[:, rows], returned, preferred_element_type=jnp.float32
        ) + jnp.einsum("ect,ecd->td", combine_lo[:, rows], returned, preferred_element_type=jnp.float32)
    layer_out = (
        (residual + expert_sum).astype(jnp.bfloat16).reshape(local_reqs, local_tokens, width_model)
    )
    return (layer_out, decode_pool)


def solution(mesh):
    devices = mesh.devices
    req_total, kv_total = devices.shape
    split_mesh = jax.sharding.Mesh(
        devices.reshape(2, req_total // 2, kv_total), ("zhi", "rlow", "kv")
    )
    return jax.shard_map(
        body,
        mesh=split_mesh,
        in_specs=(
            P(REQ, "kv", None),
            P(REQ, "kv", None),
            P(REQ, "kv", None, None),
            P(REQ, "kv", None, None),
            P(),
            P(),
            P(),
            P(),
            P((*REQ, "kv"), None),
            P((*REQ, "kv"), None),
            P(REQ, None, None, "kv"),
            P(REQ, None),
        ),
        out_specs=(P(REQ, "kv", None), P(REQ, "kv", None, None)),
        check_vma=False,
    )
```

```python
import functools
import math

import jax
import jax.numpy as jnp
from jax import lax
from jax.experimental import pallas as pl
from jax.experimental.pallas import tpu as pltpu
from jax.sharding import PartitionSpec as P

BLOCK = 16


REQ = ("zhi", "rlow")


def lookup_lengths(req_order, cached_len, count):
    start = lax.axis_index(REQ) * count
    mine = lax.dynamic_slice_in_dim(req_order, start, count)
    match = mine[:, None] == jnp.arange(cached_len.shape[0], dtype=jnp.int32)[None, :]
    return jnp.sum(jnp.where(match, cached_len[None, :], 0), axis=1)


def attend_kernel(len_ref, q_ref, c_ref, s_ref, o_ref, *, tk, head_dim):
    b = pl.program_id(0)
    length = len_ref[b]
    span = q_ref.shape[1]
    lanes = q_ref.shape[2]
    per_group = lanes // head_dim
    scale = 1.0 / math.sqrt(head_dim)
    lane = lax.broadcasted_iota(jnp.int32, (span, lanes), 1)
    q_all = q_ref[0].astype(jnp.float32) * scale
    blocks = c_ref.shape[1] // tk
    full = length // tk
    tail = jnp.minimum(full, blocks - 1)
    row = lax.broadcasted_iota(jnp.int32, (span, span), 0)
    col = lax.broadcasted_iota(jnp.int32, (span, span), 1)
    causal = col <= row
    key_lane = lax.broadcasted_iota(jnp.int32, (tk, lanes), 1) < head_dim
    span_lane = lax.broadcasted_iota(jnp.int32, (span, lanes), 1) < head_dim
    span_keys = s_ref[0]
    span_vals = jnp.where(span_lane, jnp.ones_like(span_keys), span_keys)
    dims = (((1,), (1,)), ((), ()))
    tail_pos = tail * tk + lax.broadcasted_iota(jnp.int32, (span, tk), 1)
    tail_ok = (tail_pos >= full * tk) & (tail_pos < length)
    outs = []
    for j in range(per_group):
        shifted = q_all if j == 0 else pltpu.roll(q_all, lanes - j * head_dim, 1)
        qj = jnp.where(lane < head_dim, shifted, 0.0).astype(jnp.bfloat16)

        def block(kb):
            start = pl.multiple_of(kb * tk, tk)
            keys = c_ref[0, pl.ds(start, tk), :]
            s = lax.dot_general(qj, keys, dims, preferred_element_type=jnp.float32)
            return keys, s

        def update(m, acc, ok, s, vals):
            if ok is None:
                m_new = jnp.maximum(m, jnp.max(s, axis=1, keepdims=True))
                p = jnp.exp(s - m_new)
            else:
                m_new = jnp.maximum(m, jnp.max(jnp.where(ok, s, -1e30), axis=1, keepdims=True))
                p = jnp.where(ok, jnp.exp(s - m_new), 0.0)
            acc = acc * jnp.exp(m - m_new) + jnp.dot(
                p.astype(jnp.bfloat16), vals, preferred_element_type=jnp.float32
            )
            return m_new, acc

        def values(keys):
            return jnp.where(key_lane, jnp.ones_like(keys), keys)

        s_span = lax.dot_general(qj, span_keys, dims, preferred_element_type=jnp.float32)
        m = jnp.full((span, 1), -1e30, jnp.float32)
        acc = jnp.zeros((span, lanes), jnp.float32)
        m, acc = update(m, acc, causal, s_span, span_vals)

        def full_body(kb, carry):
            keys, s = block(kb)
            return update(*carry, None, s, values(keys))

        m, acc = lax.fori_loop(0, full, full_body, (m, acc))
        keys_tail, s_tail = block(tail)
        m, acc = update(m, acc, tail_ok, s_tail, values(keys_tail))
        total = acc[:, 0:1]
        res = acc / total
        shift = (j * head_dim - head_dim) % lanes
        outs.append(res if shift == 0 else pltpu.roll(res, shift, 1))
    out = outs[0]
    for j in range(1, per_group):
        out = jnp.where(lane >= j * head_dim, outs[j], out)
    o_ref[0] = out.astype(o_ref.dtype)


def attend(query_heads, cache_heads, span_heads, lengths):
    local_reqs, span, groups, lanes = query_heads.shape
    cached = cache_heads.shape[1]
    head_dim = cache_heads.shape[-1] // 2
    tk = 256 if cached % 256 == 0 else cached
    q2 = query_heads.reshape(local_reqs, span, groups * lanes)
    c2 = cache_heads.reshape(local_reqs, cached, groups * lanes)
    s2 = span_heads.reshape(local_reqs, span, groups * lanes)
    flops = 2 * local_reqs * groups * (lanes // head_dim) * span * (cached + span) * lanes * 3
    out = pl.pallas_call(
        functools.partial(attend_kernel, tk=tk, head_dim=head_dim),
        out_shape=jax.ShapeDtypeStruct(q2.shape, jnp.bfloat16),
        grid_spec=pltpu.PrefetchScalarGridSpec(
            num_scalar_prefetch=1,
            grid=(local_reqs, groups),
            in_specs=[
                pl.BlockSpec((1, span, lanes), lambda b, g, n: (b, 0, g)),
                pl.BlockSpec((1, cached, lanes), lambda b, g, n: (b, 0, g)),
                pl.BlockSpec((1, span, lanes), lambda b, g, n: (b, 0, g)),
            ],
            out_specs=pl.BlockSpec((1, span, lanes), lambda b, g, n: (b, 0, g)),
        ),
        cost_estimate=pl.CostEstimate(
            flops=flops,
            transcendentals=local_reqs * groups * 2 * span * (cached + span),
            bytes_accessed=2 * (2 * q2.size + c2.size + s2.size),
        ),
    )(lengths.astype(jnp.int32), q2, c2, s2)
    return out.reshape(local_reqs, span, groups, lanes)


def place_pages(page_rows, slot_numbers, slots_dev):
    owner_index = slot_numbers // slots_dev
    arrangement = jnp.argsort(owner_index, stable=True)
    return (page_rows[arrangement], (slot_numbers % slots_dev)[arrangement])


def body(
    hidden,
    queries,
    span_kv,
    cache,
    req_order,
    cached_len,
    out_weight,
    norm_gain,
    expert_ids,
    expert_weights,
    w_experts,
    block_map,
):
    local_reqs, local_tokens, width_model = hidden.shape
    row_count = local_reqs * local_tokens
    req_count = lax.axis_size(REQ)
    kv_count = lax.axis_size("kv")
    kv_heads = span_kv.shape[2]
    head_pair = span_kv.shape[3]
    group_width = queries.shape[2] // kv_heads
    group_count = kv_heads // kv_count
    slots_dev = local_reqs * block_map.shape[1]
    lengths = lookup_lengths(req_order, cached_len, local_reqs)
    queries_grouped = queries.reshape(local_reqs, local_tokens, kv_heads, group_width)
    cache_heads, span_heads, query_heads = (
        lax.all_to_all(cache, "kv", split_axis=2, concat_axis=1, tiled=True),
        lax.all_to_all(span_kv, "kv", split_axis=2, concat_axis=1, tiled=True),
        lax.all_to_all(queries_grouped, "kv", split_axis=2, concat_axis=1, tiled=True),
    )
    pair_weights = lax.all_gather(w_experts, "zhi", axis=0, tiled=False)
    pair_weights, cache_heads, block_map = lax.optimization_barrier(
        (pair_weights, cache_heads, block_map)
    )
    full_weights = lax.all_gather(pair_weights, "kv", axis=1, tiled=False)
    page_total = block_map.shape[1]
    visible = jnp.arange(cache_heads.shape[1])[None, :] < lengths[:, None]
    visible_cache = jnp.where(visible[:, :, None, None], cache_heads, jnp.zeros((), jnp.bfloat16))
    page_rows = (
        visible_cache.reshape(local_reqs, page_total, BLOCK, group_count, head_pair)
        .transpose(0, 1, 3, 2, 4)
        .reshape(local_reqs * page_total, group_count, BLOCK, head_pair)
    )
    sorted_pages, local_slot = place_pages(page_rows, block_map.reshape(-1), slots_dev)
    per_owner = sorted_pages.shape[0] // req_count
    outgoing = sorted_pages.reshape(req_count, per_owner, group_count, BLOCK, head_pair)
    arrived, where_to = (
        lax.all_to_all(outgoing, REQ, split_axis=0, concat_axis=0, tiled=True),
        lax.all_to_all(
            local_slot.reshape(req_count, per_owner), REQ, split_axis=0, concat_axis=0, tiled=True
        ),
    )
    attn_heads = attend(query_heads, cache_heads, span_heads, lengths)
    attn_heads, arrived, where_to = lax.optimization_barrier((attn_heads, arrived, where_to))
    attn = lax.all_to_all(attn_heads, "kv", split_axis=1, concat_axis=2, tiled=True).reshape(
        row_count, kv_heads * group_width
    )
    placement = (
        where_to.reshape(1, -1) == jnp.arange(slots_dev, dtype=jnp.int32)[:, None]
    ).astype(jnp.bfloat16)
    decode_pool = jnp.dot(
        placement,
        arrived.reshape(slots_dev, group_count * BLOCK * head_pair),
        preferred_element_type=jnp.float32,
    ).astype(jnp.bfloat16).reshape(slots_dev, group_count, BLOCK, head_pair)
    residual = hidden.reshape(row_count, width_model).astype(jnp.float32) + jnp.dot(
        attn, out_weight, preferred_element_type=jnp.float32
    )
    inverse_rms = lax.rsqrt(jnp.mean(residual * residual, axis=-1, keepdims=True) + 1e-05)
    normed = (residual * inverse_rms * norm_gain).astype(jnp.bfloat16)
    top_count = expert_ids.shape[1]
    exp_dev = w_experts.shape[0]
    experts = exp_dev * req_count
    capacity = min(row_count, 2 * row_count * top_count // experts)
    halves = lax.axis_size("zhi")
    side = lax.axis_size("rlow")
    match = expert_ids[:, :, None] == jnp.arange(experts, dtype=jnp.int32)[None, None, :]
    picks = jnp.sum(match.astype(jnp.int32), axis=1)
    pick_weight = jnp.sum(jnp.where(match, expert_weights[:, :, None], 0.0), axis=1)
    rank = jnp.cumsum(picks, axis=0) - 1

    def side_major(table):
        return (
            table.reshape(halves, side, exp_dev, row_count)
            .transpose(1, 0, 2, 3)
            .reshape(experts, row_count)
        )

    slot_of = side_major(jnp.where(picks > 0, rank, -1).T)
    weight_of = side_major(pick_weight.T)
    selector = slot_of[:, None, :] == jnp.arange(capacity, dtype=jnp.int32)[None, :, None]
    per_dev = halves * exp_dev
    weights = full_weights.reshape(halves, kv_count, *w_experts.shape)
    combine = jnp.where(selector, weight_of[:, None, :], 0.0)
    combine_hi = combine.astype(jnp.bfloat16)
    combine_lo = (combine - combine_hi.astype(jnp.float32)).astype(jnp.bfloat16)
    chunks = 2 if capacity % 16 == 0 else 1
    size = capacity // chunks
    expert_sum = jnp.zeros((row_count, width_model), jnp.float32)
    for chunk in range(chunks):
        rows = slice(chunk * size, (chunk + 1) * size)
        buffer = jnp.einsum(
            "ect,td->ecd", selector[:, rows].astype(jnp.bfloat16), normed,
            preferred_element_type=jnp.float32,
        ).astype(jnp.bfloat16)
        slot_block = lax.all_to_all(
            buffer.reshape(side, per_dev * size, width_model), "rlow", split_axis=0, concat_axis=0, tiled=True
        )
        grouped = slot_block.reshape(side, halves, exp_dev, size, width_model)
        gate_act = jnp.einsum(
            "szjcd,zkjdf->szjckf", grouped, weights[:, :, :, 0], preferred_element_type=jnp.float32
        )
        up_act = jnp.einsum(
            "szjcd,zkjdf->szjckf", grouped, weights[:, :, :, 1], preferred_element_type=jnp.float32
        )
        activated = (jax.nn.silu(gate_act) * up_act).astype(jnp.bfloat16)
        expert_out = jnp.einsum(
            "szjckf,zkjdf->szjcd", activated, weights[:, :, :, 2], preferred_element_type=jnp.float32
        ).astype(jnp.bfloat16)
        returned = lax.all_to_all(
            expert_out.reshape(side, per_dev * size, width_model), "rlow", split_axis=0, concat_axis=0, tiled=True
        ).reshape(experts, size, width_model)
        expert_sum = expert_sum + jnp.einsum(
            "ect,ecd->td", combine_hi[:, rows], returned, preferred_element_type=jnp.float32
        ) + jnp.einsum("ect,ecd->td", combine_lo[:, rows], returned, preferred_element_type=jnp.float32)
    layer_out = (
        (residual + expert_sum).astype(jnp.bfloat16).reshape(local_reqs, local_tokens, width_model)
    )
    return (layer_out, decode_pool)


def solution(mesh):
    devices = mesh.devices
    req_total, kv_total = devices.shape
    split_mesh = jax.sharding.Mesh(
        devices.reshape(2, req_total // 2, kv_total), ("zhi", "rlow", "kv")
    )
    return jax.shard_map(
        body,
        mesh=split_mesh,
        in_specs=(
            P(REQ, "kv", None),
            P(REQ, "kv", None),
            P(REQ, "kv", None, None),
            P(REQ, "kv", None, None),
            P(),
            P(),
            P(),
            P(),
            P((*REQ, "kv"), None),
            P((*REQ, "kv"), None),
            P(REQ, None, None, "kv"),
            P(REQ, None),
        ),
        out_specs=(P(REQ, "kv", None), P(REQ, "kv", None, None)),
        check_vma=False,
    )
```

```python
import functools
import math

import jax
import jax.numpy as jnp
from jax import lax
from jax.experimental import pallas as pl
from jax.experimental.pallas import tpu as pltpu
from jax.sharding import PartitionSpec as P

BLOCK = 16


REQ = ("zhi", "rlow")


def lookup_lengths(req_order, cached_len, count):
    start = lax.axis_index(REQ) * count
    mine = lax.dynamic_slice_in_dim(req_order, start, count)
    match = mine[:, None] == jnp.arange(cached_len.shape[0], dtype=jnp.int32)[None, :]
    return jnp.sum(jnp.where(match, cached_len[None, :], 0), axis=1)


def attend_kernel(len_ref, q_ref, c_ref, s_ref, o_ref, *, tk, head_dim):
    b = pl.program_id(0)
    length = len_ref[b]
    span = q_ref.shape[1]
    lanes = q_ref.shape[2]
    per_group = lanes // head_dim
    scale = 1.0 / math.sqrt(head_dim)
    lane = lax.broadcasted_iota(jnp.int32, (span, lanes), 1)
    q_all = q_ref[0].astype(jnp.float32) * scale
    blocks = c_ref.shape[1] // tk
    full = length // tk
    tail = jnp.minimum(full, blocks - 1)
    row = lax.broadcasted_iota(jnp.int32, (span, span), 0)
    col = lax.broadcasted_iota(jnp.int32, (span, span), 1)
    causal = col <= row
    key_lane = lax.broadcasted_iota(jnp.int32, (tk, lanes), 1) < head_dim
    span_lane = lax.broadcasted_iota(jnp.int32, (span, lanes), 1) < head_dim
    span_keys = s_ref[0]
    span_vals = jnp.where(span_lane, jnp.ones_like(span_keys), span_keys)
    dims = (((1,), (1,)), ((), ()))
    tail_pos = tail * tk + lax.broadcasted_iota(jnp.int32, (span, tk), 1)
    tail_ok = (tail_pos >= full * tk) & (tail_pos < length)
    outs = []
    for j in range(per_group):
        shifted = q_all if j == 0 else pltpu.roll(q_all, lanes - j * head_dim, 1)
        qj = jnp.where(lane < head_dim, shifted, 0.0).astype(jnp.bfloat16)

        def block(kb):
            start = pl.multiple_of(kb * tk, tk)
            keys = c_ref[0, pl.ds(start, tk), :]
            s = lax.dot_general(qj, keys, dims, preferred_element_type=jnp.float32)
            return keys, s

        def update(m, acc, ok, s, vals):
            if ok is None:
                m_new = jnp.maximum(m, jnp.max(s, axis=1, keepdims=True))
                p = jnp.exp(s - m_new)
            else:
                m_new = jnp.maximum(m, jnp.max(jnp.where(ok, s, -1e30), axis=1, keepdims=True))
                p = jnp.where(ok, jnp.exp(s - m_new), 0.0)
            acc = acc * jnp.exp(m - m_new) + jnp.dot(
                p.astype(jnp.bfloat16), vals, preferred_element_type=jnp.float32
            )
            return m_new, acc

        def values(keys):
            return jnp.where(key_lane, jnp.ones_like(keys), keys)

        s_span = lax.dot_general(qj, span_keys, dims, preferred_element_type=jnp.float32)
        m = jnp.full((span, 1), -1e30, jnp.float32)
        acc = jnp.zeros((span, lanes), jnp.float32)
        m, acc = update(m, acc, causal, s_span, span_vals)

        def full_body(kb, carry):
            keys, s = block(kb)
            return update(*carry, None, s, values(keys))

        m, acc = lax.fori_loop(0, full, full_body, (m, acc))
        keys_tail, s_tail = block(tail)
        m, acc = update(m, acc, tail_ok, s_tail, values(keys_tail))
        total = acc[:, 0:1]
        res = acc / total
        shift = (j * head_dim - head_dim) % lanes
        outs.append(res if shift == 0 else pltpu.roll(res, shift, 1))
    out = outs[0]
    for j in range(1, per_group):
        out = jnp.where(lane >= j * head_dim, outs[j], out)
    o_ref[0] = out.astype(o_ref.dtype)


def attend(query_heads, cache_heads, span_heads, lengths):
    local_reqs, span, groups, lanes = query_heads.shape
    cached = cache_heads.shape[1]
    head_dim = cache_heads.shape[-1] // 2
    tk = 256 if cached % 256 == 0 else cached
    q2 = query_heads.reshape(local_reqs, span, groups * lanes)
    c2 = cache_heads.reshape(local_reqs, cached, groups * lanes)
    s2 = span_heads.reshape(local_reqs, span, groups * lanes)
    flops = 2 * local_reqs * groups * (lanes // head_dim) * span * (cached + span) * lanes * 3
    out = pl.pallas_call(
        functools.partial(attend_kernel, tk=tk, head_dim=head_dim),
        out_shape=jax.ShapeDtypeStruct(q2.shape, jnp.bfloat16),
        grid_spec=pltpu.PrefetchScalarGridSpec(
            num_scalar_prefetch=1,
            grid=(local_reqs, groups),
            in_specs=[
                pl.BlockSpec((1, span, lanes), lambda b, g, n: (b, 0, g)),
                pl.BlockSpec((1, cached, lanes), lambda b, g, n: (b, 0, g)),
                pl.BlockSpec((1, span, lanes), lambda b, g, n: (b, 0, g)),
            ],
            out_specs=pl.BlockSpec((1, span, lanes), lambda b, g, n: (b, 0, g)),
        ),
        cost_estimate=pl.CostEstimate(
            flops=flops,
            transcendentals=local_reqs * groups * 2 * span * (cached + span),
            bytes_accessed=2 * (2 * q2.size + c2.size + s2.size),
        ),
    )(lengths.astype(jnp.int32), q2, c2, s2)
    return out.reshape(local_reqs, span, groups, lanes)


def place_pages(page_rows, slot_numbers, slots_dev):
    owner_index = slot_numbers // slots_dev
    arrangement = jnp.argsort(owner_index, stable=True)
    return (page_rows[arrangement], (slot_numbers % slots_dev)[arrangement])


def body(
    hidden,
    queries,
    span_kv,
    cache,
    req_order,
    cached_len,
    out_weight,
    norm_gain,
    expert_ids,
    expert_weights,
    w_experts,
    block_map,
):
    local_reqs, local_tokens, width_model = hidden.shape
    row_count = local_reqs * local_tokens
    req_count = lax.axis_size(REQ)
    kv_count = lax.axis_size("kv")
    kv_heads = span_kv.shape[2]
    head_pair = span_kv.shape[3]
    group_width = queries.shape[2] // kv_heads
    group_count = kv_heads // kv_count
    slots_dev = local_reqs * block_map.shape[1]
    lengths = lookup_lengths(req_order, cached_len, local_reqs)
    queries_grouped = queries.reshape(local_reqs, local_tokens, kv_heads, group_width)
    cache_heads, span_heads, query_heads = (
        lax.all_to_all(cache, "kv", split_axis=2, concat_axis=1, tiled=True),
        lax.all_to_all(span_kv, "kv", split_axis=2, concat_axis=1, tiled=True),
        lax.all_to_all(queries_grouped, "kv", split_axis=2, concat_axis=1, tiled=True),
    )
    pair_weights = lax.all_gather(w_experts, "zhi", axis=0, tiled=False)
    pair_weights, cache_heads, block_map = lax.optimization_barrier(
        (pair_weights, cache_heads, block_map)
    )
    full_weights = lax.all_gather(pair_weights, "kv", axis=1, tiled=False)
    page_total = block_map.shape[1]
    visible = jnp.arange(cache_heads.shape[1])[None, :] < lengths[:, None]
    visible_cache = jnp.where(visible[:, :, None, None], cache_heads, jnp.zeros((), jnp.bfloat16))
    page_rows = (
        visible_cache.reshape(local_reqs, page_total, BLOCK, group_count, head_pair)
        .transpose(0, 1, 3, 2, 4)
        .reshape(local_reqs * page_total, group_count, BLOCK, head_pair)
    )
    sorted_pages, local_slot = place_pages(page_rows, block_map.reshape(-1), slots_dev)
    per_owner = sorted_pages.shape[0] // req_count
    outgoing = sorted_pages.reshape(req_count, per_owner, group_count, BLOCK, head_pair)
    arrived, where_to = (
        lax.all_to_all(outgoing, REQ, split_axis=0, concat_axis=0, tiled=True),
        lax.all_to_all(
            local_slot.reshape(req_count, per_owner), REQ, split_axis=0, concat_axis=0, tiled=True
        ),
    )
    attn_heads = attend(query_heads, cache_heads, span_heads, lengths)
    attn_heads, full_weights, arrived, where_to = lax.optimization_barrier(
        (attn_heads, full_weights, arrived, where_to)
    )
    attn = lax.all_to_all(attn_heads, "kv", split_axis=1, concat_axis=2, tiled=True).reshape(
        row_count, kv_heads * group_width
    )
    placement = (
        where_to.reshape(1, -1) == jnp.arange(slots_dev, dtype=jnp.int32)[:, None]
    ).astype(jnp.bfloat16)
    decode_pool = jnp.dot(
        placement,
        arrived.reshape(slots_dev, group_count * BLOCK * head_pair),
        preferred_element_type=jnp.float32,
    ).astype(jnp.bfloat16).reshape(slots_dev, group_count, BLOCK, head_pair)
    residual = hidden.reshape(row_count, width_model).astype(jnp.float32) + jnp.dot(
        attn, out_weight, preferred_element_type=jnp.float32
    )
    inverse_rms = lax.rsqrt(jnp.mean(residual * residual, axis=-1, keepdims=True) + 1e-05)
    normed = (residual * inverse_rms * norm_gain).astype(jnp.bfloat16)
    top_count = expert_ids.shape[1]
    exp_dev = w_experts.shape[0]
    experts = exp_dev * req_count
    capacity = min(row_count, 2 * row_count * top_count // experts)
    halves = lax.axis_size("zhi")
    side = lax.axis_size("rlow")
    match = expert_ids[:, :, None] == jnp.arange(experts, dtype=jnp.int32)[None, None, :]
    picks = jnp.sum(match.astype(jnp.int32), axis=1)
    pick_weight = jnp.sum(jnp.where(match, expert_weights[:, :, None], 0.0), axis=1)
    rank = jnp.cumsum(picks, axis=0) - 1

    def side_major(table):
        return (
            table.reshape(halves, side, exp_dev, row_count)
            .transpose(1, 0, 2, 3)
            .reshape(experts, row_count)
        )

    slot_of = side_major(jnp.where(picks > 0, rank, -1).T)
    weight_of = side_major(pick_weight.T)
    selector = slot_of[:, None, :] == jnp.arange(capacity, dtype=jnp.int32)[None, :, None]
    per_dev = halves * exp_dev
    weights = full_weights.reshape(halves, kv_count, *w_experts.shape)
    combine = jnp.where(selector, weight_of[:, None, :], 0.0)
    combine_hi = combine.astype(jnp.bfloat16)
    combine_lo = (combine - combine_hi.astype(jnp.float32)).astype(jnp.bfloat16)
    edge = (capacity * 5 // 16) // 8 * 8
    bounds = [0, edge, capacity - edge, capacity] if edge > 0 else [0, capacity]
    expert_sum = jnp.zeros((row_count, width_model), jnp.float32)
    for lo, hi in zip(bounds[:-1], bounds[1:]):
        rows = slice(lo, hi)
        size = hi - lo
        buffer = jnp.einsum(
            "ect,td->ecd", selector[:, rows].astype(jnp.bfloat16), normed,
            preferred_element_type=jnp.float32,
        ).astype(jnp.bfloat16)
        slot_block = lax.all_to_all(
            buffer.reshape(side, per_dev * size, width_model), "rlow", split_axis=0, concat_axis=0, tiled=True
        )
        grouped = slot_block.reshape(side, halves, exp_dev, size, width_model)
        gate_act = jnp.einsum(
            "szjcd,zkjdf->szjckf", grouped, weights[:, :, :, 0], preferred_element_type=jnp.float32
        )
        up_act = jnp.einsum(
            "szjcd,zkjdf->szjckf", grouped, weights[:, :, :, 1], preferred_element_type=jnp.float32
        )
        activated = (jax.nn.silu(gate_act) * up_act).astype(jnp.bfloat16)
        expert_out = jnp.einsum(
            "szjckf,zkjdf->szjcd", activated, weights[:, :, :, 2], preferred_element_type=jnp.float32
        ).astype(jnp.bfloat16)
        returned = lax.all_to_all(
            expert_out.reshape(side, per_dev * size, width_model), "rlow", split_axis=0, concat_axis=0, tiled=True
        ).reshape(experts, size, width_model)
        expert_sum = expert_sum + jnp.einsum(
            "ect,ecd->td", combine_hi[:, rows], returned, preferred_element_type=jnp.float32
        ) + jnp.einsum("ect,ecd->td", combine_lo[:, rows], returned, preferred_element_type=jnp.float32)
    layer_out = (
        (residual + expert_sum).astype(jnp.bfloat16).reshape(local_reqs, local_tokens, width_model)
    )
    return (layer_out, decode_pool)


def solution(mesh):
    devices = mesh.devices
    req_total, kv_total = devices.shape
    split_mesh = jax.sharding.Mesh(
        devices.reshape(2, req_total // 2, kv_total), ("zhi", "rlow", "kv")
    )
    return jax.shard_map(
        body,
        mesh=split_mesh,
        in_specs=(
            P(REQ, "kv", None),
            P(REQ, "kv", None),
            P(REQ, "kv", None, None),
            P(REQ, "kv", None, None),
            P(),
            P(),
            P(),
            P(),
            P((*REQ, "kv"), None),
            P((*REQ, "kv"), None),
            P(REQ, None, None, "kv"),
            P(REQ, None),
        ),
        out_specs=(P(REQ, "kv", None), P(REQ, "kv", None, None)),
        check_vma=False,
    )
```

```python
import functools
import math

import jax
import jax.numpy as jnp
from jax import lax
from jax.experimental import pallas as pl
from jax.experimental.pallas import tpu as pltpu
from jax.sharding import PartitionSpec as P

BLOCK = 16


REQ = ("zhi", "rlow")


def lookup_lengths(req_order, cached_len, count):
    start = lax.axis_index(REQ) * count
    mine = lax.dynamic_slice_in_dim(req_order, start, count)
    match = mine[:, None] == jnp.arange(cached_len.shape[0], dtype=jnp.int32)[None, :]
    return jnp.sum(jnp.where(match, cached_len[None, :], 0), axis=1)


def attend_kernel(len_ref, q_ref, c_ref, s_ref, o_ref, *, tk, head_dim):
    b = pl.program_id(0)
    length = len_ref[b]
    span = q_ref.shape[1]
    lanes = q_ref.shape[2]
    per_group = lanes // head_dim
    scale = 1.0 / math.sqrt(head_dim)
    lane = lax.broadcasted_iota(jnp.int32, (span, lanes), 1)
    q_all = q_ref[0].astype(jnp.float32) * scale
    blocks = c_ref.shape[1] // tk
    full = length // tk
    tail = jnp.minimum(full, blocks - 1)
    row = lax.broadcasted_iota(jnp.int32, (span, span), 0)
    col = lax.broadcasted_iota(jnp.int32, (span, span), 1)
    causal = col <= row
    key_lane = lax.broadcasted_iota(jnp.int32, (tk, lanes), 1) < head_dim
    span_lane = lax.broadcasted_iota(jnp.int32, (span, lanes), 1) < head_dim
    span_keys = s_ref[0]
    span_vals = jnp.where(span_lane, jnp.ones_like(span_keys), span_keys)
    dims = (((1,), (1,)), ((), ()))
    tail_pos = tail * tk + lax.broadcasted_iota(jnp.int32, (span, tk), 1)
    tail_ok = (tail_pos >= full * tk) & (tail_pos < length)
    outs = []
    for j in range(per_group):
        shifted = q_all if j == 0 else pltpu.roll(q_all, lanes - j * head_dim, 1)
        qj = jnp.where(lane < head_dim, shifted, 0.0).astype(jnp.bfloat16)

        def block(kb):
            start = pl.multiple_of(kb * tk, tk)
            keys = c_ref[0, pl.ds(start, tk), :]
            s = lax.dot_general(qj, keys, dims, preferred_element_type=jnp.float32)
            return keys, s

        def update(m, acc, ok, s, vals):
            if ok is None:
                m_new = jnp.maximum(m, jnp.max(s, axis=1, keepdims=True))
                p = jnp.exp(s - m_new)
            else:
                m_new = jnp.maximum(m, jnp.max(jnp.where(ok, s, -1e30), axis=1, keepdims=True))
                p = jnp.where(ok, jnp.exp(s - m_new), 0.0)
            acc = acc * jnp.exp(m - m_new) + jnp.dot(
                p.astype(jnp.bfloat16), vals, preferred_element_type=jnp.float32
            )
            return m_new, acc

        def values(keys):
            return jnp.where(key_lane, jnp.ones_like(keys), keys)

        s_span = lax.dot_general(qj, span_keys, dims, preferred_element_type=jnp.float32)
        m = jnp.full((span, 1), -1e30, jnp.float32)
        acc = jnp.zeros((span, lanes), jnp.float32)
        m, acc = update(m, acc, causal, s_span, span_vals)

        def full_body(kb, carry):
            keys, s = block(kb)
            return update(*carry, None, s, values(keys))

        m, acc = lax.fori_loop(0, full, full_body, (m, acc))
        keys_tail, s_tail = block(tail)
        m, acc = update(m, acc, tail_ok, s_tail, values(keys_tail))
        total = acc[:, 0:1]
        res = acc / total
        shift = (j * head_dim - head_dim) % lanes
        outs.append(res if shift == 0 else pltpu.roll(res, shift, 1))
    out = outs[0]
    for j in range(1, per_group):
        out = jnp.where(lane >= j * head_dim, outs[j], out)
    o_ref[0] = out.astype(o_ref.dtype)


def attend(query_heads, cache_heads, span_heads, lengths):
    local_reqs, span, groups, lanes = query_heads.shape
    cached = cache_heads.shape[1]
    head_dim = cache_heads.shape[-1] // 2
    tk = 256 if cached % 256 == 0 else cached
    q2 = query_heads.reshape(local_reqs, span, groups * lanes)
    c2 = cache_heads.reshape(local_reqs, cached, groups * lanes)
    s2 = span_heads.reshape(local_reqs, span, groups * lanes)
    flops = 2 * local_reqs * groups * (lanes // head_dim) * span * (cached + span) * lanes * 3
    out = pl.pallas_call(
        functools.partial(attend_kernel, tk=tk, head_dim=head_dim),
        out_shape=jax.ShapeDtypeStruct(q2.shape, jnp.bfloat16),
        grid_spec=pltpu.PrefetchScalarGridSpec(
            num_scalar_prefetch=1,
            grid=(local_reqs, groups),
            in_specs=[
                pl.BlockSpec((1, span, lanes), lambda b, g, n: (b, 0, g)),
                pl.BlockSpec((1, cached, lanes), lambda b, g, n: (b, 0, g)),
                pl.BlockSpec((1, span, lanes), lambda b, g, n: (b, 0, g)),
            ],
            out_specs=pl.BlockSpec((1, span, lanes), lambda b, g, n: (b, 0, g)),
        ),
        cost_estimate=pl.CostEstimate(
            flops=flops,
            transcendentals=local_reqs * groups * 2 * span * (cached + span),
            bytes_accessed=2 * (2 * q2.size + c2.size + s2.size),
        ),
    )(lengths.astype(jnp.int32), q2, c2, s2)
    return out.reshape(local_reqs, span, groups, lanes)


def place_pages(page_rows, slot_numbers, slots_dev):
    owner_index = slot_numbers // slots_dev
    arrangement = jnp.argsort(owner_index, stable=True)
    return (page_rows[arrangement], (slot_numbers % slots_dev)[arrangement])


def body(
    hidden,
    queries,
    span_kv,
    cache,
    req_order,
    cached_len,
    out_weight,
    norm_gain,
    expert_ids,
    expert_weights,
    w_experts,
    block_map,
):
    local_reqs, local_tokens, width_model = hidden.shape
    row_count = local_reqs * local_tokens
    req_count = lax.axis_size(REQ)
    kv_count = lax.axis_size("kv")
    kv_heads = span_kv.shape[2]
    head_pair = span_kv.shape[3]
    group_width = queries.shape[2] // kv_heads
    group_count = kv_heads // kv_count
    slots_dev = local_reqs * block_map.shape[1]
    lengths = lookup_lengths(req_order, cached_len, local_reqs)
    queries_grouped = queries.reshape(local_reqs, local_tokens, kv_heads, group_width)
    cache_heads, span_heads, query_heads = (
        lax.all_to_all(cache, "kv", split_axis=2, concat_axis=1, tiled=True),
        lax.all_to_all(span_kv, "kv", split_axis=2, concat_axis=1, tiled=True),
        lax.all_to_all(queries_grouped, "kv", split_axis=2, concat_axis=1, tiled=True),
    )
    pair_weights = lax.all_gather(w_experts, "zhi", axis=0, tiled=False)
    pair_weights, cache_heads, block_map = lax.optimization_barrier(
        (pair_weights, cache_heads, block_map)
    )
    full_weights = lax.all_gather(pair_weights, "kv", axis=1, tiled=False)
    page_total = block_map.shape[1]
    visible = jnp.arange(cache_heads.shape[1])[None, :] < lengths[:, None]
    visible_cache = jnp.where(visible[:, :, None, None], cache_heads, jnp.zeros((), jnp.bfloat16))
    page_rows = (
        visible_cache.reshape(local_reqs, page_total, BLOCK, group_count, head_pair)
        .transpose(0, 1, 3, 2, 4)
        .reshape(local_reqs * page_total, group_count, BLOCK, head_pair)
    )
    sorted_pages, local_slot = place_pages(page_rows, block_map.reshape(-1), slots_dev)
    per_owner = sorted_pages.shape[0] // req_count
    outgoing = sorted_pages.reshape(req_count, per_owner, group_count, BLOCK, head_pair)
    arrived = lax.all_to_all(outgoing, REQ, split_axis=0, concat_axis=0, tiled=True)
    every_map = lax.all_gather(block_map, REQ, axis=0, tiled=True).reshape(req_count, -1)
    mine = every_map // slots_dev == lax.axis_index(REQ)
    order = jnp.cumsum(mine.astype(jnp.int32), axis=1) - 1
    hit = mine[:, :, None] & (order[:, :, None] == jnp.arange(per_owner, dtype=jnp.int32)[None, None, :])
    where_to = jnp.sum(jnp.where(hit, (every_map % slots_dev)[:, :, None], 0), axis=1)
    attn_heads = attend(query_heads, cache_heads, span_heads, lengths)
    attn_heads, full_weights, arrived, where_to = lax.optimization_barrier(
        (attn_heads, full_weights, arrived, where_to)
    )
    attn = lax.all_to_all(attn_heads, "kv", split_axis=1, concat_axis=2, tiled=True).reshape(
        row_count, kv_heads * group_width
    )
    placement = (
        where_to.reshape(1, -1) == jnp.arange(slots_dev, dtype=jnp.int32)[:, None]
    ).astype(jnp.bfloat16)
    decode_pool = jnp.dot(
        placement,
        arrived.reshape(slots_dev, group_count * BLOCK * head_pair),
        preferred_element_type=jnp.float32,
    ).astype(jnp.bfloat16).reshape(slots_dev, group_count, BLOCK, head_pair)
    residual = hidden.reshape(row_count, width_model).astype(jnp.float32) + jnp.dot(
        attn, out_weight, preferred_element_type=jnp.float32
    )
    inverse_rms = lax.rsqrt(jnp.mean(residual * residual, axis=-1, keepdims=True) + 1e-05)
    normed = (residual * inverse_rms * norm_gain).astype(jnp.bfloat16)
    top_count = expert_ids.shape[1]
    exp_dev = w_experts.shape[0]
    experts = exp_dev * req_count
    capacity = min(row_count, 2 * row_count * top_count // experts)
    halves = lax.axis_size("zhi")
    side = lax.axis_size("rlow")
    match = expert_ids[:, :, None] == jnp.arange(experts, dtype=jnp.int32)[None, None, :]
    picks = jnp.sum(match.astype(jnp.int32), axis=1)
    pick_weight = jnp.sum(jnp.where(match, expert_weights[:, :, None], 0.0), axis=1)
    rank = jnp.cumsum(picks, axis=0) - 1

    def side_major(table):
        return (
            table.reshape(halves, side, exp_dev, row_count)
            .transpose(1, 0, 2, 3)
            .reshape(experts, row_count)
        )

    slot_of = side_major(jnp.where(picks > 0, rank, -1).T)
    weight_of = side_major(pick_weight.T)
    selector = slot_of[:, None, :] == jnp.arange(capacity, dtype=jnp.int32)[None, :, None]
    per_dev = halves * exp_dev
    weights = full_weights.reshape(halves, kv_count, *w_experts.shape)
    combine = jnp.where(selector, weight_of[:, None, :], 0.0)
    combine_hi = combine.astype(jnp.bfloat16)
    combine_lo = (combine - combine_hi.astype(jnp.float32)).astype(jnp.bfloat16)
    chunks = 2 if capacity % 16 == 0 else 1
    size = capacity // chunks
    expert_sum = jnp.zeros((row_count, width_model), jnp.float32)
    for chunk in range(chunks):
        rows = slice(chunk * size, (chunk + 1) * size)
        buffer = jnp.einsum(
            "ect,td->ecd", selector[:, rows].astype(jnp.bfloat16), normed,
            preferred_element_type=jnp.float32,
        ).astype(jnp.bfloat16)
        slot_block = lax.all_to_all(
            buffer.reshape(side, per_dev * size, width_model), "rlow", split_axis=0, concat_axis=0, tiled=True
        )
        grouped = slot_block.reshape(side, halves, exp_dev, size, width_model)
        gate_act = jnp.einsum(
            "szjcd,zkjdf->szjckf", grouped, weights[:, :, :, 0], preferred_element_type=jnp.float32
        )
        up_act = jnp.einsum(
            "szjcd,zkjdf->szjckf", grouped, weights[:, :, :, 1], preferred_element_type=jnp.float32
        )
        activated = (jax.nn.silu(gate_act) * up_act).astype(jnp.bfloat16)
        expert_out = jnp.einsum(
            "szjckf,zkjdf->szjcd", activated, weights[:, :, :, 2], preferred_element_type=jnp.float32
        ).astype(jnp.bfloat16)
        returned = lax.all_to_all(
            expert_out.reshape(side, per_dev * size, width_model), "rlow", split_axis=0, concat_axis=0, tiled=True
        ).reshape(experts, size, width_model)
        expert_sum = expert_sum + jnp.einsum(
            "ect,ecd->td", combine_hi[:, rows], returned, preferred_element_type=jnp.float32
        ) + jnp.einsum("ect,ecd->td", combine_lo[:, rows], returned, preferred_element_type=jnp.float32)
    layer_out = (
        (residual + expert_sum).astype(jnp.bfloat16).reshape(local_reqs, local_tokens, width_model)
    )
    return (layer_out, decode_pool)


def solution(mesh):
    devices = mesh.devices
    req_total, kv_total = devices.shape
    split_mesh = jax.sharding.Mesh(
        devices.reshape(2, req_total // 2, kv_total), ("zhi", "rlow", "kv")
    )
    return jax.shard_map(
        body,
        mesh=split_mesh,
        in_specs=(
            P(REQ, "kv", None),
            P(REQ, "kv", None),
            P(REQ, "kv", None, None),
            P(REQ, "kv", None, None),
            P(),
            P(),
            P(),
            P(),
            P((*REQ, "kv"), None),
            P((*REQ, "kv"), None),
            P(REQ, None, None, "kv"),
            P(REQ, None),
        ),
        out_specs=(P(REQ, "kv", None), P(REQ, "kv", None, None)),
        check_vma=False,
    )
```
